128 devices in a mesh: dom: 8 (over y, core), fsdp: 16 (over z, x).
Axes of the slice: x: 4, y: 4, z: 4, core: 2. Of those that a mesh axis runs over, the one named last changes fastest.
Arguments:
- features: bfloat16 [512, 1024, 128], P(('dom', 'fsdp')), may hold values from -24 to 24
- history_first: bfloat16 [1024, 1024, 128], P('dom', 'fsdp'), may hold values from -6 to 6
- history_second: bfloat16 [1024, 1024, 128], P('dom', 'fsdp'), may hold values from -3 to 3
- pull_list: int32 [8, 128, 4], P('dom'), may hold values from 0 to 127
- pull_count: int32 [8, 128], P('dom'), may hold values from 1 to 4, as said below
- tile_src: int32 [512, 6], P(('dom', 'fsdp')), may hold values from 0 to 35
- tile_count: int32 [512], P(('dom', 'fsdp')), may hold values from 1 to 6
- tile_values: bfloat16 [512, 6, 128, 128], P(('dom', 'fsdp')), may hold values from -0.21875 to 0.21875
- w_first: bfloat16 [1024, 1024], P('fsdp'), may hold values from -0.1875 to 0.1875
- w_second: bfloat16 [1024, 1024], P('fsdp'), may hold values from -0.1875 to 0.1875
- bias_first: bfloat16 [1024], P('fsdp'), may hold values from -3 to 3
- out_grad: bfloat16 [512, 1024, 128], P(('dom', 'fsdp')), may hold values from -0.0625 to 0.0625
Outputs:
- hidden_new: bfloat16 [512, 1024, 128], P(('dom', 'fsdp'))
- grad_w1: float32 [1024, 1024], P('fsdp')
- grad_w2: float32 [1024, 1024], P('fsdp')
- grad_b1: float32 [1024], P('fsdp')
The draws below stay inside these ranges and needn't reach their ends.
Inputs may be any that keep to these rules, and one draw needn't show every extreme that they name: pull_list[o, q, c] numbers a block within partition o. Slot c of list (o, q) is live when c < pull_count[o, q]; every device q has 4 live slots from at least one partition. tile_src below 4 names one of the device's own batch blocks; 4 + s names its pulled slot s.
All inputs are finite; a program needn't handle non-finite values.
Results may differ from the reference program's by a relative error of at most 0.0075.
Values may be sent and summed in bfloat16 or wider, within the bound.
No kernel may reach another device: no remote copies, remote signals or barrier semaphores. Data moves between devices by JAX's collectives and lax.ppermute only.
A program may use at most 192 MiB of HBM per device.

```python
import jax
import jax.numpy as jnp
from jax import lax

F = 1024
H = 1024
BLK = 128
TILES = 6
CAP = 4
B_DEV = 4
OWN = 128
PARTITIONS = 8
SOURCES = 36
BATCH_BLK = 512
TABLE_BLK = 1024
N_DOM = 8
DEVICES = 128


def draw_pull_count(key, part):
    base_key, full_key = jax.random.split(jax.random.fold_in(key, 7))
    base = jax.random.randint(base_key, (N_DOM, DEVICES), 1, CAP + 1)
    picked = jax.random.randint(full_key, (DEVICES,), 0, N_DOM)
    filled = jnp.arange(N_DOM)[:, None] == picked[None, :]
    return jnp.where(filled, CAP, base).astype(jnp.int32)


def with_ends(array, key, low, top_value):
    spot = [jax.random.randint(jax.random.fold_in(key, axis), (), 0, length) for axis, length in enumerate(array.shape)]
    main_axis = array.shape.index(max(array.shape))
    beside = spot[:main_axis] + [(spot[main_axis] + 1) % array.shape[main_axis]] + spot[main_axis + 1:]
    return array.at[tuple(spot)].set(low).at[tuple(beside)].set(top_value)


def strengthened(values, own_key, source, target, parts, factor):
    owner, partner = [(jnp.arange(values.shape[dim]) // (values.shape[dim] // parts)).reshape([-1 if axis == dim else 1 for axis in range(values.ndim)]) for dim in (source, target)]
    chosen = jax.random.permutation(own_key, parts)[partner]
    strong = (owner == chosen) | (owner == (partner + parts // 2) % parts)
    return jnp.where(strong, factor * values, values)


def steps_of(key, dims, cuts, least, largest):
    gain = 1.0
    for dim, shards_of in cuts:
        steps = jax.random.uniform(jax.random.fold_in(jax.random.fold_in(key, 6), dim), (shards_of,), jnp.float32, least / len(cuts), largest / len(cuts))
        gain = gain * jnp.repeat(jnp.exp(steps), dims[dim] // shards_of).reshape((-1,) + (1,) * (len(dims) - 1 - dim))
    return gain


def scatter_about(stream_key, dims, spread, limit, cuts=(), kind=jnp.bfloat16):
    values = spread * jax.random.normal(stream_key, dims, jnp.float32)
    if cuts:
        values = values * steps_of(stream_key, dims, cuts, -0.22, 0.18)
    return jnp.clip(values, -limit, limit).astype(kind)


def gaussian_with(key, extent, width, limit, shards, heavy, held_as=jnp.bfloat16):
    entries = width * jax.random.normal(key, extent, jnp.float32)
    if shards:
        entries = entries * steps_of(key, extent, shards, -0.22, 0.18)
    return jnp.clip(strengthened(entries, jax.random.fold_in(key, 3), *heavy), -limit, limit).astype(held_as)


def setup_inputs(seed: int = 0) -> dict:
    keys = jax.random.split(jax.random.key(seed), 13)
    features = gaussian_with(keys[0], (BATCH_BLK, F, BLK), 1.0, 24.0, ((0, 128),), (0, 1, 128, 5.5))
    history_first = scatter_about(keys[1], (TABLE_BLK, F, BLK), 1.0, 6.0, ((0, 8), (1, 16)))
    history_second = scatter_about(keys[2], (TABLE_BLK, H, BLK), 0.5, 3.0, ((0, 8), (1, 16)))
    pull_list = with_ends(jax.random.randint(keys[3], (PARTITIONS, DEVICES, CAP), 0, OWN), jax.random.fold_in(keys[3], 1), 0, OWN - 1).astype(jnp.int32)
    pull_count = draw_pull_count(jax.random.fold_in(keys[12], 71), 0)
    tile_src = with_ends(jax.random.randint(keys[5], (BATCH_BLK, TILES), 0, SOURCES), jax.random.fold_in(keys[5], 1), 0, SOURCES - 1).astype(jnp.int32)
    tile_count = with_ends(jax.random.randint(keys[6], (BATCH_BLK,), 1, TILES + 1), jax.random.fold_in(keys[6], 1), 1, TILES).astype(jnp.int32)
    tile_values = scatter_about(keys[7], (BATCH_BLK, TILES, BLK, BLK), (BLK * TILES) ** -0.5, 0.21875, ((0, 128),))
    w_first = scatter_about(keys[8], (F, H), F ** -0.5, 0.1875, ((0, 16),))
    w_second = scatter_about(keys[9], (H, H), H ** -0.5, 0.1875, ((0, 16),))
    bias_first = scatter_about(keys[10], (H,), 0.5, 3.0, ((0, 16),))
    out_grad = scatter_about(keys[11], (BATCH_BLK, H, BLK), ((BATCH_BLK * BLK) ** -0.5), 0.0625, ((0, 128),))
    return dict(features=features, history_first=history_first, history_second=history_second, pull_list=pull_list, pull_count=pull_count, tile_src=tile_src, tile_count=tile_count, tile_values=tile_values, w_first=w_first, w_second=w_second, bias_first=bias_first, out_grad=out_grad)


def gelu_tanh(inputs):
    return jax.nn.gelu(inputs, approximate=True)

def aggregate(sources, source_ids, tile_live, tile_vals):
    running = jnp.zeros((source_ids.shape[0], sources.shape[1], sources.shape[2]), jnp.float32)
    for tile_slot in range(TILES):
        blocks = jnp.take(sources, source_ids[:, tile_slot], axis=0).astype(jnp.float32)
        product = jnp.einsum('vfj,vji->vfi', blocks, tile_vals[:, tile_slot].astype(jnp.float32))
        running = running + jnp.where(tile_live[:, tile_slot][:, None, None], product, 0.0)
    return running

def spread_back(back_second, source_ids, tile_live, tile_vals):
    targets = jnp.arange(B_DEV, dtype=jnp.int32)[None, :]
    running = jnp.zeros(back_second.shape, jnp.float32)
    for tile_slot in range(TILES):
        product = jnp.einsum('vai,vji->vaj', back_second.astype(jnp.float32), tile_vals[:, tile_slot].astype(jnp.float32))
        matches = jnp.where((source_ids[:, tile_slot][:, None] == targets) & tile_live[:, tile_slot][:, None], 1.0, 0.0).astype(jnp.float32)
        running = running + jnp.einsum('vu,vaj->uaj', matches, product, precision=lax.Precision.HIGHEST)
    return running

def reference(features, history_first, history_second, pull_list, pull_count, tile_src, tile_count, tile_values, w_first, w_second, bias_first, out_grad):
    owners = jnp.arange(PARTITIONS, dtype=jnp.int32)
    first_weight = w_first.astype(jnp.float32)
    second_weight = w_second.astype(jnp.float32)
    bias_full = bias_first.astype(jnp.float32)

    def per_device(sums_so_far, device):
        first_sum, second_sum, bias_sum = sums_so_far
        first_block = (device * B_DEV).astype(jnp.int32)
        own_feats = lax.dynamic_slice_in_dim(features, first_block, B_DEV, 0)
        source_ids = lax.dynamic_slice_in_dim(tile_src, first_block, B_DEV, 0)
        live_tiles = lax.dynamic_slice_in_dim(tile_count, first_block, B_DEV, 0)
        tile_vals = lax.dynamic_slice_in_dim(tile_values, first_block, B_DEV, 0)
        cotangent = lax.dynamic_slice_in_dim(out_grad, first_block, B_DEV, 0)
        chosen = lax.dynamic_index_in_dim(pull_list, device, 1, keepdims=False)
        live_count = lax.dynamic_index_in_dim(pull_count, device, 1, keepdims=False)
        block_rows = (chosen + OWN * owners[:, None]).T.reshape(-1).astype(jnp.int32)
        is_live = (jnp.arange(CAP, dtype=jnp.int32)[None, :] < live_count[:, None]).T.reshape(-1)
        pulled_first = jnp.where(is_live[:, None, None], jnp.take(history_first, block_rows, axis=0), jnp.zeros((), history_first.dtype))
        pulled_second = jnp.where(is_live[:, None, None], jnp.take(history_second, block_rows, axis=0), jnp.zeros((), history_second.dtype))
        tile_live = jnp.arange(TILES, dtype=jnp.int32)[None, :] < live_tiles[:, None]
        agg_first = aggregate(jnp.concatenate([own_feats, pulled_first], 0), source_ids, tile_live, tile_vals).astype(jnp.bfloat16)
        pre_act = jnp.einsum('fh,vfn->vhn', first_weight, agg_first.astype(jnp.float32)) + bias_full[None, :, None]
        hidden_out = gelu_tanh(pre_act).astype(jnp.bfloat16)
        agg_second = aggregate(jnp.concatenate([hidden_out, pulled_second], 0), source_ids, tile_live, tile_vals).astype(jnp.bfloat16)
        second_term = jnp.einsum('van,vbn->ab', agg_second.astype(jnp.float32), cotangent.astype(jnp.float32))
        back_second = jnp.einsum('ab,vbn->van', second_weight, cotangent.astype(jnp.float32)).astype(jnp.bfloat16)
        back_hidden = spread_back(back_second, source_ids, tile_live, tile_vals)
        _, pullback = jax.vjp(gelu_tanh, pre_act)
        back_pre = pullback(back_hidden)[0].astype(jnp.bfloat16)
        first_term = jnp.einsum('vfn,vhn->fh', agg_first.astype(jnp.float32), back_pre.astype(jnp.float32))
        bias_term = lax.optimization_barrier(jnp.sum(back_pre.astype(jnp.float32), axis=(0, 2)))
        return ((first_sum + first_term, second_sum + second_term, bias_sum + bias_term), hidden_out)
    zero_sums = (jnp.zeros((F, H), jnp.float32), jnp.zeros((H, H), jnp.float32), jnp.zeros((H,), jnp.float32))
    totals, hidden_all = lax.scan(per_device, zero_sums, jnp.arange(DEVICES, dtype=jnp.int32))
    return (hidden_all.reshape(BATCH_BLK, H, BLK), totals[0], totals[1], totals[2])
```

```python
import functools

import jax
import jax.numpy as jnp
from jax import lax
from jax.experimental import pallas as pl
from jax.experimental.pallas import tpu as pltpu
from jax.sharding import PartitionSpec as P


def gelu_tanh(inputs):
    return jax.nn.gelu(inputs, approximate=True)


def _agg_kernel(own_count, last_tile, src_ref, cnt_ref, live_ref, own_ref, pulled_ref, tile_ref, out_ref, acc_ref):
    v = pl.program_id(0)
    t = pl.program_id(1)

    @pl.when(t == 0)
    def _():
        acc_ref[...] = jnp.zeros_like(acc_ref)

    src = src_ref[v, t]
    tile_live = t < cnt_ref[v]
    own_ok = tile_live & (src < own_count)
    pull_ok = tile_live & (src >= own_count) & (live_ref[jnp.maximum(src - own_count, 0)] > 0)

    @pl.when(own_ok)
    def _():
        acc_ref[...] += jnp.dot(own_ref[0], tile_ref[0, 0], preferred_element_type=jnp.float32)

    @pl.when(pull_ok)
    def _():
        block = pulled_ref[0, 0]
        block = block.reshape(block.shape[0] * block.shape[1], block.shape[2])
        acc_ref[...] += jnp.dot(block, tile_ref[0, 0], preferred_element_type=jnp.float32)

    @pl.when(t == last_tile)
    def _():
        out_ref[0] = acc_ref[...].astype(out_ref.dtype)


def aggregate(own, pulled, tile_src, tile_count, slot_live, tile_values):
    nb, feat, blk = own.shape
    cap, dom = pulled.shape[0], pulled.shape[1]
    tiles = tile_src.shape[1]

    def eff(v, t, src_ref, cnt_ref):
        return jnp.minimum(t, cnt_ref[v] - 1)

    def own_map(v, t, src_ref, cnt_ref, live_ref):
        s = src_ref[v, eff(v, t, src_ref, cnt_ref)]
        return (jnp.clip(s, 0, nb - 1), 0, 0)

    def pulled_map(v, t, src_ref, cnt_ref, live_ref):
        s = jnp.clip(src_ref[v, eff(v, t, src_ref, cnt_ref)] - nb, 0, cap * dom - 1)
        return (s // dom, s % dom, 0, 0, 0)

    def tile_map(v, t, src_ref, cnt_ref, live_ref):
        return (v, eff(v, t, src_ref, cnt_ref), 0, 0)

    def out_map(v, t, src_ref, cnt_ref, live_ref):
        return (v, 0, 0)

    grid_spec = pltpu.PrefetchScalarGridSpec(
        num_scalar_prefetch=3,
        grid=(nb, tiles),
        in_specs=[
            pl.BlockSpec((1, feat, blk), own_map),
            pl.BlockSpec((1, 1) + pulled.shape[2:], pulled_map),
            pl.BlockSpec((1, 1, blk, blk), tile_map),
        ],
        out_specs=pl.BlockSpec((1, feat, blk), out_map),
        scratch_shapes=[pltpu.VMEM((feat, blk), jnp.float32)],
    )
    flops = 2 * nb * tiles * feat * blk * blk
    return pl.pallas_call(
        functools.partial(_agg_kernel, nb, tiles - 1),
        grid_spec=grid_spec,
        out_shape=jax.ShapeDtypeStruct(own.shape, jnp.bfloat16),
        compiler_params=pltpu.CompilerParams(dimension_semantics=("arbitrary", "arbitrary")),
        cost_estimate=pl.CostEstimate(
            flops=flops, transcendentals=0, bytes_accessed=nb * tiles * (2 * feat * blk * 2 + blk * blk * 2) + own.size * 2
        ),
    )(tile_src, tile_count, slot_live, own, pulled, tile_values)


def _spread_kernel(own_count, src_ref, cnt_ref, back_ref, tile_ref, out_ref):
    v = pl.program_id(0)
    t = pl.program_id(1)

    @pl.when((v == 0) & (t == 0))
    def _():
        out_ref[...] = jnp.zeros_like(out_ref)

    src = src_ref[v, t]

    @pl.when((t < cnt_ref[v]) & (src < own_count))
    def _():
        term = lax.dot_general(
            back_ref[0], tile_ref[0, 0], (((1,), (1,)), ((), ())), preferred_element_type=jnp.float32
        )
        out_ref[src] = out_ref[src] + term


def spread_back(back_second, tile_src, tile_count, tile_values):
    nb, width, blk = back_second.shape
    tiles = tile_src.shape[1]

    def eff(v, t, cnt_ref):
        return jnp.minimum(t, cnt_ref[v] - 1)

    grid_spec = pltpu.PrefetchScalarGridSpec(
        num_scalar_prefetch=2,
        grid=(nb, tiles),
        in_specs=[
            pl.BlockSpec((1, width, blk), lambda v, t, s, c: (v, 0, 0)),
            pl.BlockSpec((1, 1, blk, blk), lambda v, t, s, c: (v, eff(v, t, c), 0, 0)),
        ],
        out_specs=pl.BlockSpec((nb, width, blk), lambda v, t, s, c: (0, 0, 0)),
    )
    return pl.pallas_call(
        functools.partial(_spread_kernel, nb),
        grid_spec=grid_spec,
        out_shape=jax.ShapeDtypeStruct(back_second.shape, jnp.float32),
        compiler_params=pltpu.CompilerParams(dimension_semantics=("arbitrary", "arbitrary")),
        cost_estimate=pl.CostEstimate(
            flops=2 * nb * tiles * width * blk * blk,
            transcendentals=0,
            bytes_accessed=back_second.size * 2 + nb * tiles * blk * blk * 2 + back_second.size * 4,
        ),
    )(tile_src, tile_count, back_second, tile_values)


def on_device(
    features,
    history_first,
    history_second,
    pull_list,
    pull_count,
    tile_src,
    tile_count,
    tile_values,
    w_first,
    w_second,
    bias_first,
    out_grad,
):
    dom_size = lax.axis_size("dom")
    fsdp_size = lax.axis_size("fsdp")
    me = lax.axis_index("dom") * fsdp_size + lax.axis_index("fsdp")
    rows, hidden = w_first.shape
    bias_cols = jnp.broadcast_to(bias_first[:, None], (rows, 128))
    packed = lax.all_gather(jnp.concatenate([w_first, bias_cols], axis=1), "fsdp", axis=0, tiled=True)
    first_full = packed[:, :hidden]
    bias_full = packed[:, hidden].astype(jnp.float32)
    second_full = lax.all_gather(w_second, "fsdp", axis=0, tiled=True)

    chosen = pull_list[0]
    requesters, slot_cap = chosen.shape
    counts_all = lax.all_gather(pull_count, "dom", axis=0, tiled=True)
    my_counts = lax.dynamic_index_in_dim(counts_all, me, axis=1, keepdims=False)
    slot_live = (lax.broadcasted_iota(jnp.int32, (slot_cap, dom_size), 0) < my_counts[None, :]).astype(jnp.int32)
    slot_live = slot_live.reshape(-1)

    block_len = features.shape[2]
    first_cols = history_first.shape[1]
    second_cols = history_second.shape[1]
    sent_first = jnp.take(history_first, chosen.reshape(-1), axis=0, mode="clip").reshape(requesters, slot_cap, 1, first_cols, block_len)
    sent_second = jnp.take(history_second, chosen.reshape(-1), axis=0, mode="clip").reshape(requesters, slot_cap, 1, second_cols, block_len)
    arrived_first = lax.all_to_all(sent_first, ("dom", "fsdp"), split_axis=0, concat_axis=2, tiled=True)
    arrived_second = lax.all_to_all(sent_second, ("dom", "fsdp"), split_axis=0, concat_axis=2, tiled=True)
    pulled_first = arrived_first.reshape(slot_cap, dom_size, fsdp_size, first_cols, block_len)
    pulled_second = arrived_second.reshape(slot_cap, dom_size, fsdp_size, second_cols, block_len)

    back_second = jnp.einsum(
        "ab,vbn->van", second_full, out_grad, preferred_element_type=jnp.float32
    ).astype(jnp.bfloat16)
    back_hidden = spread_back(back_second, tile_src, tile_count, tile_values)

    agg_first = aggregate(features, pulled_first, tile_src, tile_count, slot_live, tile_values)
    pre_act = (
        jnp.einsum("fh,vfn->vhn", first_full, agg_first, preferred_element_type=jnp.float32)
        + bias_full[None, :, None]
    )
    hidden_new = gelu_tanh(pre_act).astype(jnp.bfloat16)
    _, pullback = jax.vjp(gelu_tanh, pre_act)
    back_pre = pullback(back_hidden)[0].astype(jnp.bfloat16)
    first_term = jnp.einsum("vfn,vhn->fh", agg_first, back_pre, preferred_element_type=jnp.float32)
    bias_term = jnp.sum(back_pre.astype(jnp.float32), axis=(0, 2))

    agg_second = aggregate(hidden_new, pulled_second, tile_src, tile_count, slot_live, tile_values)
    second_term = jnp.einsum(
        "van,vbn->ab", agg_second, out_grad, preferred_element_type=jnp.float32
    )
    first_shard, second_shard, bias_shard = (
        lax.psum_scatter(first_term, "fsdp", scatter_dimension=0, tiled=True),
        lax.psum_scatter(second_term, "fsdp", scatter_dimension=0, tiled=True),
        lax.psum_scatter(bias_term, "fsdp", scatter_dimension=0, tiled=True),
    )
    first_total, second_total, bias_total = lax.psum((first_shard, second_shard, bias_shard), "dom")
    return (hidden_new, first_total, second_total, bias_total)


def solution(mesh):
    return jax.shard_map(
        on_device,
        mesh=mesh,
        in_specs=(
            P(("dom", "fsdp"), None, None),
            P("dom", "fsdp", None),
            P("dom", "fsdp", None),
            P("dom", None, None),
            P("dom", None),
            P(("dom", "fsdp"), None),
            P(("dom", "fsdp")),
            P(("dom", "fsdp"), None, None, None),
            P("fsdp", None),
            P("fsdp", None),
            P("fsdp"),
            P(("dom", "fsdp"), None, None),
        ),
        out_specs=(P(("dom", "fsdp"), None, None), P("fsdp", None), P("fsdp", None), P("fsdp")),
        check_vma=False,
    )
```

```python
import functools

import jax
import jax.numpy as jnp
from jax import lax
from jax.experimental import pallas as pl
from jax.experimental.pallas import tpu as pltpu
from jax.sharding import PartitionSpec as P


def gelu_tanh(inputs):
    return jax.nn.gelu(inputs, approximate=True)


def _agg_kernel(own_count, last_tile, src_ref, cnt_ref, live_ref, own_ref, pulled_ref, tile_ref, out_ref, acc_ref):
    v = pl.program_id(0)
    t = pl.program_id(1)

    @pl.when(t == 0)
    def _():
        acc_ref[...] = jnp.zeros_like(acc_ref)

    src = src_ref[v, t]
    tile_live = t < cnt_ref[v]
    own_ok = tile_live & (src < own_count)
    pull_ok = tile_live & (src >= own_count) & (live_ref[jnp.maximum(src - own_count, 0)] > 0)

    @pl.when(own_ok)
    def _():
        acc_ref[...] += jnp.dot(own_ref[0], tile_ref[0, 0], preferred_element_type=jnp.float32)

    @pl.when(pull_ok)
    def _():
        block = pulled_ref[0, :, 0]
        block = block.reshape(block.shape[0] * block.shape[1], block.shape[2])
        acc_ref[...] += jnp.dot(block, tile_ref[0, 0], preferred_element_type=jnp.float32)

    @pl.when(t == last_tile)
    def _():
        out_ref[0] = acc_ref[...].astype(out_ref.dtype)


def aggregate(own, pulled, tile_src, tile_count, slot_live, tile_values):
    nb, feat, blk = own.shape
    dom, fsdp, cap = pulled.shape[0], pulled.shape[1], pulled.shape[2]
    tiles = tile_src.shape[1]

    def eff(v, t, src_ref, cnt_ref):
        return jnp.minimum(t, cnt_ref[v] - 1)

    def own_map(v, t, src_ref, cnt_ref, live_ref):
        s = src_ref[v, eff(v, t, src_ref, cnt_ref)]
        return (jnp.clip(s, 0, nb - 1), 0, 0)

    def pulled_map(v, t, src_ref, cnt_ref, live_ref):
        s = jnp.clip(src_ref[v, eff(v, t, src_ref, cnt_ref)] - nb, 0, cap * dom - 1)
        return (s % dom, 0, s // dom, 0, 0)

    def tile_map(v, t, src_ref, cnt_ref, live_ref):
        return (v, eff(v, t, src_ref, cnt_ref), 0, 0)

    def out_map(v, t, src_ref, cnt_ref, live_ref):
        return (v, 0, 0)

    grid_spec = pltpu.PrefetchScalarGridSpec(
        num_scalar_prefetch=3,
        grid=(nb, tiles),
        in_specs=[
            pl.BlockSpec((1, feat, blk), own_map),
            pl.BlockSpec((1, fsdp, 1) + pulled.shape[3:], pulled_map),
            pl.BlockSpec((1, 1, blk, blk), tile_map),
        ],
        out_specs=pl.BlockSpec((1, feat, blk), out_map),
        scratch_shapes=[pltpu.VMEM((feat, blk), jnp.float32)],
    )
    flops = 2 * nb * tiles * feat * blk * blk
    return pl.pallas_call(
        functools.partial(_agg_kernel, nb, tiles - 1),
        grid_spec=grid_spec,
        out_shape=jax.ShapeDtypeStruct(own.shape, jnp.bfloat16),
        compiler_params=pltpu.CompilerParams(dimension_semantics=("arbitrary", "arbitrary")),
        cost_estimate=pl.CostEstimate(
            flops=flops, transcendentals=0, bytes_accessed=nb * tiles * (2 * feat * blk * 2 + blk * blk * 2) + own.size * 2
        ),
    )(tile_src, tile_count, slot_live, own, pulled, tile_values)


def _spread_kernel(own_count, src_ref, cnt_ref, back_ref, tile_ref, out_ref):
    v = pl.program_id(0)
    t = pl.program_id(1)

    @pl.when((v == 0) & (t == 0))
    def _():
        out_ref[...] = jnp.zeros_like(out_ref)

    src = src_ref[v, t]

    @pl.when((t < cnt_ref[v]) & (src < own_count))
    def _():
        term = lax.dot_general(
            back_ref[0], tile_ref[0, 0], (((1,), (1,)), ((), ())), preferred_element_type=jnp.float32
        )
        out_ref[src] = out_ref[src] + term


def spread_back(back_second, tile_src, tile_count, tile_values):
    nb, width, blk = back_second.shape
    tiles = tile_src.shape[1]

    def eff(v, t, cnt_ref):
        return jnp.minimum(t, cnt_ref[v] - 1)

    grid_spec = pltpu.PrefetchScalarGridSpec(
        num_scalar_prefetch=2,
        grid=(nb, tiles),
        in_specs=[
            pl.BlockSpec((1, width, blk), lambda v, t, s, c: (v, 0, 0)),
            pl.BlockSpec((1, 1, blk, blk), lambda v, t, s, c: (v, eff(v, t, c), 0, 0)),
        ],
        out_specs=pl.BlockSpec((nb, width, blk), lambda v, t, s, c: (0, 0, 0)),
    )
    return pl.pallas_call(
        functools.partial(_spread_kernel, nb),
        grid_spec=grid_spec,
        out_shape=jax.ShapeDtypeStruct(back_second.shape, jnp.float32),
        compiler_params=pltpu.CompilerParams(dimension_semantics=("arbitrary", "arbitrary")),
        cost_estimate=pl.CostEstimate(
            flops=2 * nb * tiles * width * blk * blk,
            transcendentals=0,
            bytes_accessed=back_second.size * 2 + nb * tiles * blk * blk * 2 + back_second.size * 4,
        ),
    )(tile_src, tile_count, back_second, tile_values)


def on_device(
    features,
    history_first,
    history_second,
    pull_list,
    pull_count,
    tile_src,
    tile_count,
    tile_values,
    w_first,
    w_second,
    bias_first,
    out_grad,
):
    dom_size = lax.axis_size("dom")
    fsdp_size = lax.axis_size("fsdp")
    me = lax.axis_index("dom") * fsdp_size + lax.axis_index("fsdp")
    rows, hidden = w_first.shape
    bias_cols = jnp.broadcast_to(bias_first[:, None], (rows, 128))
    packed = lax.all_gather(jnp.concatenate([w_first, bias_cols], axis=1), "fsdp", axis=0, tiled=True)
    first_full = packed[:, :hidden]
    bias_full = packed[:, hidden].astype(jnp.float32)
    second_full = lax.all_gather(w_second, "fsdp", axis=0, tiled=True)

    chosen = pull_list[0]
    requesters, slot_cap = chosen.shape
    counts_all = lax.all_gather(pull_count, "dom", axis=0, tiled=True)
    counts_all, chosen = lax.optimization_barrier((counts_all, chosen))
    my_counts = lax.dynamic_index_in_dim(counts_all, me, axis=1, keepdims=False)
    slot_live = (lax.broadcasted_iota(jnp.int32, (slot_cap, dom_size), 0) < my_counts[None, :]).astype(jnp.int32)
    slot_live = slot_live.reshape(-1)

    block_len = features.shape[2]
    first_cols = history_first.shape[1]
    second_cols = history_second.shape[1]
    sent_first = jnp.take(history_first, chosen.reshape(-1), axis=0, mode="clip").reshape(requesters, slot_cap, first_cols, block_len)
    sent_second = jnp.take(history_second, chosen.reshape(-1), axis=0, mode="clip").reshape(requesters, slot_cap, second_cols, block_len)
    arrived_first = lax.all_to_all(sent_first, ("dom", "fsdp"), split_axis=0, concat_axis=0, tiled=True)
    arrived_second = lax.all_to_all(sent_second, ("dom", "fsdp"), split_axis=0, concat_axis=0, tiled=True)
    pulled_first = arrived_first.reshape(dom_size, fsdp_size, slot_cap, first_cols, block_len)
    pulled_second = arrived_second.reshape(dom_size, fsdp_size, slot_cap, second_cols, block_len)

    core = lax.axis_index("dom") % 2
    pair = [(d, d ^ 1) for d in range(dom_size)]
    partner_grad = lax.ppermute(out_grad, "dom", pair)

    back_second = jnp.einsum(
        "ab,vbn->van", second_full, out_grad, preferred_element_type=jnp.float32
    ).astype(jnp.bfloat16)
    back_hidden = spread_back(back_second, tile_src, tile_count, tile_values)

    def halves(x):
        split = x.reshape(x.shape[0], fsdp_size, 2, x.shape[1] // (2 * fsdp_size), x.shape[2])
        mine = lax.dynamic_index_in_dim(split, core, axis=2, keepdims=False)
        theirs = lax.dynamic_index_in_dim(split, 1 - core, axis=2, keepdims=False)
        return mine, theirs

    agg_first = aggregate(features, pulled_first, tile_src, tile_count, slot_live, tile_values)
    pre_act = (
        jnp.einsum("fh,vfn->vhn", first_full, agg_first, preferred_element_type=jnp.float32)
        + bias_full[None, :, None]
    )
    hidden_new = gelu_tanh(pre_act).astype(jnp.bfloat16)
    _, pullback = jax.vjp(gelu_tanh, pre_act)
    back_pre = pullback(back_hidden)[0].astype(jnp.bfloat16)
    bias_term = jnp.sum(back_pre.astype(jnp.float32), axis=(0, 2))
    first_mine, first_theirs = halves(agg_first)
    first_got, back_got = lax.ppermute((first_theirs, back_pre), "dom", pair)
    first_term = jnp.einsum(
        "vprn,vhn->prh", first_mine, back_pre, preferred_element_type=jnp.float32
    ) + jnp.einsum("vprn,vhn->prh", first_got, back_got, preferred_element_type=jnp.float32)

    agg_second = aggregate(hidden_new, pulled_second, tile_src, tile_count, slot_live, tile_values)
    second_mine, second_theirs = halves(agg_second)
    second_got = lax.ppermute(second_theirs, "dom", pair)
    second_term = jnp.einsum(
        "vprn,vbn->prb", second_mine, out_grad, preferred_element_type=jnp.float32
    ) + jnp.einsum("vprn,vbn->prb", second_got, partner_grad, preferred_element_type=jnp.float32)

    half_rows = first_term.shape[1]
    lanes = 128
    bias_cols = jnp.zeros((fsdp_size, 2 * half_rows, lanes), jnp.float32)
    bias_cols = bias_cols.at[:, 0, : hidden // fsdp_size].set(bias_term.reshape(fsdp_size, hidden // fsdp_size))
    packed_terms = jnp.concatenate([jnp.concatenate([first_term, second_term], axis=1), bias_cols], axis=2)
    packed_terms = packed_terms.reshape(fsdp_size * 2 * half_rows, hidden + lanes)
    shard = lax.psum_scatter(packed_terms, "fsdp", scatter_dimension=0, tiled=True)
    zero_half = jnp.zeros((half_rows, hidden), jnp.float32)

    def placed(part):
        return jnp.where(core == 0, jnp.concatenate([part, zero_half], 0), jnp.concatenate([zero_half, part], 0))

    bias_block = jnp.zeros((8, hidden), jnp.float32).at[0, :lanes].set(shard[0, hidden:])
    full = jnp.concatenate(
        [placed(shard[:half_rows, :hidden]), placed(shard[half_rows:, :hidden]), bias_block], axis=0
    )
    total = lax.psum(full, "dom")
    first_total = total[: 2 * half_rows]
    second_total = total[2 * half_rows : 4 * half_rows]
    bias_total = total[4 * half_rows, : hidden // fsdp_size]
    return (hidden_new, first_total, second_total, bias_total)


def solution(mesh):
    return jax.shard_map(
        on_device,
        mesh=mesh,
        in_specs=(
            P(("dom", "fsdp"), None, None),
            P("dom", "fsdp", None),
            P("dom", "fsdp", None),
            P("dom", None, None),
            P("dom", None),
            P(("dom", "fsdp"), None),
            P(("dom", "fsdp")),
            P(("dom", "fsdp"), None, None, None),
            P("fsdp", None),
            P("fsdp", None),
            P("fsdp"),
            P(("dom", "fsdp"), None, None),
        ),
        out_specs=(P(("dom", "fsdp"), None, None), P("fsdp", None), P("fsdp", None), P("fsdp")),
        check_vma=False,
    )
```

```python
import functools

import jax
import jax.numpy as jnp
from jax import lax
from jax.experimental import pallas as pl
from jax.experimental.pallas import tpu as pltpu
from jax.sharding import PartitionSpec as P


def gelu_tanh(inputs):
    return jax.nn.gelu(inputs, approximate=True)


def _agg_kernel(own_count, last_tile, src_ref, cnt_ref, live_ref, own_ref, pulled_ref, tile_ref, out_ref, acc_ref):
    v = pl.program_id(0)
    t = pl.program_id(1)

    @pl.when(t == 0)
    def _():
        acc_ref[...] = jnp.zeros_like(acc_ref)

    src = src_ref[v, t]
    tile_live = t < cnt_ref[v]
    own_ok = tile_live & (src < own_count)
    pull_ok = tile_live & (src >= own_count) & (live_ref[jnp.maximum(src - own_count, 0)] > 0)

    @pl.when(own_ok)
    def _():
        acc_ref[...] += jnp.dot(own_ref[0], tile_ref[0, 0], preferred_element_type=jnp.float32)

    @pl.when(pull_ok)
    def _():
        block = pulled_ref[0, :, 0]
        block = block.reshape(block.shape[0] * block.shape[1], block.shape[2])
        acc_ref[...] += jnp.dot(block, tile_ref[0, 0], preferred_element_type=jnp.float32)

    @pl.when(t == last_tile)
    def _():
        out_ref[0] = acc_ref[...].astype(out_ref.dtype)


def aggregate(own, pulled, tile_src, tile_count, slot_live, tile_values):
    nb, feat, blk = own.shape
    dom, fsdp, cap = pulled.shape[0], pulled.shape[1], pulled.shape[2]
    tiles = tile_src.shape[1]

    def eff(v, t, src_ref, cnt_ref):
        return jnp.minimum(t, cnt_ref[v] - 1)

    def own_map(v, t, src_ref, cnt_ref, live_ref):
        s = src_ref[v, eff(v, t, src_ref, cnt_ref)]
        return (jnp.clip(s, 0, nb - 1), 0, 0)

    def pulled_map(v, t, src_ref, cnt_ref, live_ref):
        s = jnp.clip(src_ref[v, eff(v, t, src_ref, cnt_ref)] - nb, 0, cap * dom - 1)
        return (s % dom, 0, s // dom, 0, 0)

    def tile_map(v, t, src_ref, cnt_ref, live_ref):
        return (v, eff(v, t, src_ref, cnt_ref), 0, 0)

    def out_map(v, t, src_ref, cnt_ref, live_ref):
        return (v, 0, 0)

    grid_spec = pltpu.PrefetchScalarGridSpec(
        num_scalar_prefetch=3,
        grid=(nb, tiles),
        in_specs=[
            pl.BlockSpec((1, feat, blk), own_map),
            pl.BlockSpec((1, fsdp, 1) + pulled.shape[3:], pulled_map),
            pl.BlockSpec((1, 1, blk, blk), tile_map),
        ],
        out_specs=pl.BlockSpec((1, feat, blk), out_map),
        scratch_shapes=[pltpu.VMEM((feat, blk), jnp.float32)],
    )
    flops = 2 * nb * tiles * feat * blk * blk
    return pl.pallas_call(
        functools.partial(_agg_kernel, nb, tiles - 1),
        grid_spec=grid_spec,
        out_shape=jax.ShapeDtypeStruct(own.shape, jnp.bfloat16),
        compiler_params=pltpu.CompilerParams(dimension_semantics=("arbitrary", "arbitrary")),
        cost_estimate=pl.CostEstimate(
            flops=flops, transcendentals=0, bytes_accessed=nb * tiles * (2 * feat * blk * 2 + blk * blk * 2) + own.size * 2
        ),
    )(tile_src, tile_count, slot_live, own, pulled, tile_values)


def _spread_kernel(own_count, src_ref, cnt_ref, back_ref, tile_ref, out_ref):
    v = pl.program_id(0)
    t = pl.program_id(1)

    @pl.when((v == 0) & (t == 0))
    def _():
        out_ref[...] = jnp.zeros_like(out_ref)

    src = src_ref[v, t]

    @pl.when((t < cnt_ref[v]) & (src < own_count))
    def _():
        term = lax.dot_general(
            back_ref[0], tile_ref[0, 0], (((1,), (1,)), ((), ())), preferred_element_type=jnp.float32
        )
        out_ref[src] = out_ref[src] + term


def spread_back(back_second, tile_src, tile_count, tile_values):
    nb, width, blk = back_second.shape
    tiles = tile_src.shape[1]

    def eff(v, t, cnt_ref):
        return jnp.minimum(t, cnt_ref[v] - 1)

    grid_spec = pltpu.PrefetchScalarGridSpec(
        num_scalar_prefetch=2,
        grid=(nb, tiles),
        in_specs=[
            pl.BlockSpec((1, width, blk), lambda v, t, s, c: (v, 0, 0)),
            pl.BlockSpec((1, 1, blk, blk), lambda v, t, s, c: (v, eff(v, t, c), 0, 0)),
        ],
        out_specs=pl.BlockSpec((nb, width, blk), lambda v, t, s, c: (0, 0, 0)),
    )
    return pl.pallas_call(
        functools.partial(_spread_kernel, nb),
        grid_spec=grid_spec,
        out_shape=jax.ShapeDtypeStruct(back_second.shape, jnp.float32),
        compiler_params=pltpu.CompilerParams(dimension_semantics=("arbitrary", "arbitrary")),
        cost_estimate=pl.CostEstimate(
            flops=2 * nb * tiles * width * blk * blk,
            transcendentals=0,
            bytes_accessed=back_second.size * 2 + nb * tiles * blk * blk * 2 + back_second.size * 4,
        ),
    )(tile_src, tile_count, back_second, tile_values)


def on_device(
    features,
    history_first,
    history_second,
    pull_list,
    pull_count,
    tile_src,
    tile_count,
    tile_values,
    w_first,
    w_second,
    bias_first,
    out_grad,
):
    dom_size = lax.axis_size("dom")
    fsdp_size = lax.axis_size("fsdp")
    me = lax.axis_index("dom") * fsdp_size + lax.axis_index("fsdp")
    rows, hidden = w_first.shape
    bias_cols = jnp.broadcast_to(bias_first[:, None], (rows, 128))
    packed = lax.all_gather(jnp.concatenate([w_first, bias_cols], axis=1), "fsdp", axis=0, tiled=True)
    second_full = lax.all_gather(w_second, "fsdp", axis=0, tiled=True)

    chosen = pull_list[0]
    requesters, slot_cap = chosen.shape
    counts_all = lax.all_gather(pull_count, "dom", axis=0, tiled=True)
    counts_all, chosen = lax.optimization_barrier((counts_all, chosen))
    my_counts = lax.dynamic_index_in_dim(counts_all, me, axis=1, keepdims=False)
    slot_live = (lax.broadcasted_iota(jnp.int32, (slot_cap, dom_size), 0) < my_counts[None, :]).astype(jnp.int32)
    slot_live = slot_live.reshape(-1)

    block_len = features.shape[2]
    first_cols = history_first.shape[1]
    second_cols = history_second.shape[1]
    sent_first = jnp.take(history_first, chosen.reshape(-1), axis=0, mode="clip").reshape(requesters, slot_cap, first_cols, block_len)
    sent_second = jnp.take(history_second, chosen.reshape(-1), axis=0, mode="clip").reshape(requesters, slot_cap, second_cols, block_len)
    packed, second_full, sent_first, sent_second = lax.optimization_barrier((packed, second_full, sent_first, sent_second))
    first_full = packed[:, :hidden]
    bias_full = packed[:, hidden].astype(jnp.float32)
    arrived_first = lax.all_to_all(sent_first, ("dom", "fsdp"), split_axis=0, concat_axis=0, tiled=True)
    arrived_second = lax.all_to_all(sent_second, ("dom", "fsdp"), split_axis=0, concat_axis=0, tiled=True)
    pulled_first = arrived_first.reshape(dom_size, fsdp_size, slot_cap, first_cols, block_len)
    pulled_second = arrived_second.reshape(dom_size, fsdp_size, slot_cap, second_cols, block_len)

    core = lax.axis_index("dom") % 2
    pair = [(d, d ^ 1) for d in range(dom_size)]
    partner_grad = lax.ppermute(out_grad, "dom", pair)

    back_second = jnp.einsum(
        "ab,vbn->van", second_full, out_grad, preferred_element_type=jnp.float32
    ).astype(jnp.bfloat16)
    back_hidden = spread_back(back_second, tile_src, tile_count, tile_values)

    def halves(x):
        split = x.reshape(x.shape[0], fsdp_size, 2, x.shape[1] // (2 * fsdp_size), x.shape[2])
        mine = lax.dynamic_index_in_dim(split, core, axis=2, keepdims=False)
        theirs = lax.dynamic_index_in_dim(split, 1 - core, axis=2, keepdims=False)
        return mine, theirs

    agg_first = aggregate(features, pulled_first, tile_src, tile_count, slot_live, tile_values)
    pre_act = (
        jnp.einsum("fh,vfn->vhn", first_full, agg_first, preferred_element_type=jnp.float32)
        + bias_full[None, :, None]
    )
    hidden_new = gelu_tanh(pre_act).astype(jnp.bfloat16)
    _, pullback = jax.vjp(gelu_tanh, pre_act)
    back_pre = pullback(back_hidden)[0].astype(jnp.bfloat16)
    bias_term = jnp.sum(back_pre.astype(jnp.float32), axis=(0, 2))
    first_mine, first_theirs = halves(agg_first)
    first_got, back_got = lax.ppermute((first_theirs, back_pre), "dom", pair)
    first_term = jnp.einsum(
        "vprn,vhn->prh", first_mine, back_pre, preferred_element_type=jnp.float32
    ) + jnp.einsum("vprn,vhn->prh", first_got, back_got, preferred_element_type=jnp.float32)

    agg_second = aggregate(hidden_new, pulled_second, tile_src, tile_count, slot_live, tile_values)
    second_mine, second_theirs = halves(agg_second)
    second_got = lax.ppermute(second_theirs, "dom", pair)
    second_term = jnp.einsum(
        "vprn,vbn->prb", second_mine, out_grad, preferred_element_type=jnp.float32
    ) + jnp.einsum("vprn,vbn->prb", second_got, partner_grad, preferred_element_type=jnp.float32)

    half_rows = first_term.shape[1]
    lanes = 128
    bias_cols = jnp.zeros((fsdp_size, 2 * half_rows, lanes), jnp.float32)
    bias_cols = bias_cols.at[:, 0, : hidden // fsdp_size].set(bias_term.reshape(fsdp_size, hidden // fsdp_size))
    packed_terms = jnp.concatenate([jnp.concatenate([first_term, second_term], axis=1), bias_cols], axis=2)
    packed_terms = packed_terms.reshape(fsdp_size * 2 * half_rows, hidden + lanes)
    shard = lax.psum_scatter(packed_terms, "fsdp", scatter_dimension=0, tiled=True)
    zero_half = jnp.zeros((half_rows, hidden), jnp.float32)

    def placed(part):
        return jnp.where(core == 0, jnp.concatenate([part, zero_half], 0), jnp.concatenate([zero_half, part], 0))

    bias_block = jnp.zeros((8, hidden), jnp.float32).at[0, :lanes].set(shard[0, hidden:])
    full = jnp.concatenate(
        [placed(shard[:half_rows, :hidden]), placed(shard[half_rows:, :hidden]), bias_block], axis=0
    )
    total = lax.psum(full, "dom")
    first_total = total[: 2 * half_rows]
    second_total = total[2 * half_rows : 4 * half_rows]
    bias_total = total[4 * half_rows, : hidden // fsdp_size]
    return (hidden_new, first_total, second_total, bias_total)


def solution(mesh):
    return jax.shard_map(
        on_device,
        mesh=mesh,
        in_specs=(
            P(("dom", "fsdp"), None, None),
            P("dom", "fsdp", None),
            P("dom", "fsdp", None),
            P("dom", None, None),
            P("dom", None),
            P(("dom", "fsdp"), None),
            P(("dom", "fsdp")),
            P(("dom", "fsdp"), None, None, None),
            P("fsdp", None),
            P("fsdp", None),
            P("fsdp"),
            P(("dom", "fsdp"), None, None),
        ),
        out_specs=(P(("dom", "fsdp"), None, None), P("fsdp", None), P("fsdp", None), P("fsdp")),
        check_vma=False,
    )
```

```python
import functools

import jax
import jax.numpy as jnp
from jax import lax
from jax.experimental import pallas as pl
from jax.experimental.pallas import tpu as pltpu
from jax.sharding import PartitionSpec as P


def gelu_tanh(inputs):
    return jax.nn.gelu(inputs, approximate=True)


def _agg_kernel(own_count, last_tile, src_ref, cnt_ref, live_ref, own_ref, pulled_ref, tile_ref, out_ref, acc_ref):
    v = pl.program_id(0)
    t = pl.program_id(1)

    @pl.when(t == 0)
    def _():
        acc_ref[...] = jnp.zeros_like(acc_ref)

    src = src_ref[v, t]
    tile_live = t < cnt_ref[v]
    own_ok = tile_live & (src < own_count)
    pull_ok = tile_live & (src >= own_count) & (live_ref[jnp.maximum(src - own_count, 0)] > 0)

    @pl.when(own_ok)
    def _():
        acc_ref[...] += jnp.dot(own_ref[0], tile_ref[0, 0], preferred_element_type=jnp.float32)

    @pl.when(pull_ok)
    def _():
        block = pulled_ref[0, :, 0]
        block = block.reshape(block.shape[0] * block.shape[1], block.shape[2])
        acc_ref[...] += jnp.dot(block, tile_ref[0, 0], preferred_element_type=jnp.float32)

    @pl.when(t == last_tile)
    def _():
        out_ref[0] = acc_ref[...].astype(out_ref.dtype)


def aggregate(own, pulled, tile_src, tile_count, slot_live, tile_values):
    nb, feat, blk = own.shape
    dom, fsdp, cap = pulled.shape[0], pulled.shape[1], pulled.shape[2]
    tiles = tile_src.shape[1]

    def eff(v, t, src_ref, cnt_ref):
        return jnp.minimum(t, cnt_ref[v] - 1)

    def own_map(v, t, src_ref, cnt_ref, live_ref):
        s = src_ref[v, eff(v, t, src_ref, cnt_ref)]
        return (jnp.clip(s, 0, nb - 1), 0, 0)

    def pulled_map(v, t, src_ref, cnt_ref, live_ref):
        s = jnp.clip(src_ref[v, eff(v, t, src_ref, cnt_ref)] - nb, 0, cap * dom - 1)
        return (s % dom, 0, s // dom, 0, 0)

    def tile_map(v, t, src_ref, cnt_ref, live_ref):
        return (v, eff(v, t, src_ref, cnt_ref), 0, 0)

    def out_map(v, t, src_ref, cnt_ref, live_ref):
        return (v, 0, 0)

    grid_spec = pltpu.PrefetchScalarGridSpec(
        num_scalar_prefetch=3,
        grid=(nb, tiles),
        in_specs=[
            pl.BlockSpec((1, feat, blk), own_map),
            pl.BlockSpec((1, fsdp, 1) + pulled.shape[3:], pulled_map),
            pl.BlockSpec((1, 1, blk, blk), tile_map),
        ],
        out_specs=pl.BlockSpec((1, feat, blk), out_map),
        scratch_shapes=[pltpu.VMEM((feat, blk), jnp.float32)],
    )
    flops = 2 * nb * tiles * feat * blk * blk
    return pl.pallas_call(
        functools.partial(_agg_kernel, nb, tiles - 1),
        grid_spec=grid_spec,
        out_shape=jax.ShapeDtypeStruct(own.shape, jnp.bfloat16),
        compiler_params=pltpu.CompilerParams(dimension_semantics=("arbitrary", "arbitrary")),
        cost_estimate=pl.CostEstimate(
            flops=flops, transcendentals=0, bytes_accessed=nb * tiles * (2 * feat * blk * 2 + blk * blk * 2) + own.size * 2
        ),
    )(tile_src, tile_count, slot_live, own, pulled, tile_values)


def _spread_kernel(own_count, src_ref, cnt_ref, back_ref, tile_ref, out_ref):
    v = pl.program_id(0)
    t = pl.program_id(1)

    @pl.when((v == 0) & (t == 0))
    def _():
        out_ref[...] = jnp.zeros_like(out_ref)

    src = src_ref[v, t]

    @pl.when((t < cnt_ref[v]) & (src < own_count))
    def _():
        term = lax.dot_general(
            back_ref[0], tile_ref[0, 0], (((1,), (1,)), ((), ())), preferred_element_type=jnp.float32
        )
        out_ref[src] = out_ref[src] + term


def spread_back(back_second, tile_src, tile_count, tile_values):
    nb, width, blk = back_second.shape
    tiles = tile_src.shape[1]

    def eff(v, t, cnt_ref):
        return jnp.minimum(t, cnt_ref[v] - 1)

    grid_spec = pltpu.PrefetchScalarGridSpec(
        num_scalar_prefetch=2,
        grid=(nb, tiles),
        in_specs=[
            pl.BlockSpec((1, width, blk), lambda v, t, s, c: (v, 0, 0)),
            pl.BlockSpec((1, 1, blk, blk), lambda v, t, s, c: (v, eff(v, t, c), 0, 0)),
        ],
        out_specs=pl.BlockSpec((nb, width, blk), lambda v, t, s, c: (0, 0, 0)),
    )
    return pl.pallas_call(
        functools.partial(_spread_kernel, nb),
        grid_spec=grid_spec,
        out_shape=jax.ShapeDtypeStruct(back_second.shape, jnp.float32),
        compiler_params=pltpu.CompilerParams(dimension_semantics=("arbitrary", "arbitrary")),
        cost_estimate=pl.CostEstimate(
            flops=2 * nb * tiles * width * blk * blk,
            transcendentals=0,
            bytes_accessed=back_second.size * 2 + nb * tiles * blk * blk * 2 + back_second.size * 4,
        ),
    )(tile_src, tile_count, back_second, tile_values)


def gather_rows(x, axis):
    n = lax.axis_size(axis)
    spread = lax.all_to_all(jnp.broadcast_to(x[None], (n,) + x.shape), axis, split_axis=0, concat_axis=0, tiled=True)
    return spread.reshape((n * x.shape[0],) + x.shape[1:])


def on_device(
    features,
    history_first,
    history_second,
    pull_list,
    pull_count,
    tile_src,
    tile_count,
    tile_values,
    w_first,
    w_second,
    bias_first,
    out_grad,
):
    dom_size = lax.axis_size("dom")
    fsdp_size = lax.axis_size("fsdp")
    me = lax.axis_index("dom") * fsdp_size + lax.axis_index("fsdp")
    rows, hidden = w_first.shape
    bias_cols = jnp.broadcast_to(bias_first[:, None], (rows, 128))
    packed = gather_rows(jnp.concatenate([w_first, bias_cols], axis=1), "fsdp")
    first_full = packed[:, :hidden]
    bias_full = packed[:, hidden].astype(jnp.float32)
    second_full = gather_rows(w_second, "fsdp")

    chosen = pull_list[0]
    requesters, slot_cap = chosen.shape
    counts_all = lax.all_gather(pull_count, "dom", axis=0, tiled=True)
    counts_all, chosen = lax.optimization_barrier((counts_all, chosen))
    my_counts = lax.dynamic_index_in_dim(counts_all, me, axis=1, keepdims=False)
    slot_live = (lax.broadcasted_iota(jnp.int32, (slot_cap, dom_size), 0) < my_counts[None, :]).astype(jnp.int32)
    slot_live = slot_live.reshape(-1)

    block_len = features.shape[2]
    first_cols = history_first.shape[1]
    second_cols = history_second.shape[1]
    sent_first = jnp.take(history_first, chosen.reshape(-1), axis=0, mode="clip").reshape(requesters, slot_cap, first_cols, block_len)
    sent_second = jnp.take(history_second, chosen.reshape(-1), axis=0, mode="clip").reshape(requesters, slot_cap, second_cols, block_len)
    arrived_first = lax.all_to_all(sent_first, ("dom", "fsdp"), split_axis=0, concat_axis=0, tiled=True)
    arrived_second = lax.all_to_all(sent_second, ("dom", "fsdp"), split_axis=0, concat_axis=0, tiled=True)
    pulled_first = arrived_first.reshape(dom_size, fsdp_size, slot_cap, first_cols, block_len)
    pulled_second = arrived_second.reshape(dom_size, fsdp_size, slot_cap, second_cols, block_len)

    core = lax.axis_index("dom") % 2
    pair = [(d, d ^ 1) for d in range(dom_size)]
    partner_grad = lax.ppermute(out_grad, "dom", pair)

    back_second = jnp.einsum(
        "ab,vbn->van", second_full, out_grad, preferred_element_type=jnp.float32
    ).astype(jnp.bfloat16)
    back_hidden = spread_back(back_second, tile_src, tile_count, tile_values)

    def halves(x):
        split = x.reshape(x.shape[0], fsdp_size, 2, x.shape[1] // (2 * fsdp_size), x.shape[2])
        mine = lax.dynamic_index_in_dim(split, core, axis=2, keepdims=False)
        theirs = lax.dynamic_index_in_dim(split, 1 - core, axis=2, keepdims=False)
        return mine, theirs

    agg_first = aggregate(features, pulled_first, tile_src, tile_count, slot_live, tile_values)
    pre_act = (
        jnp.einsum("fh,vfn->vhn", first_full, agg_first, preferred_element_type=jnp.float32)
        + bias_full[None, :, None]
    )
    hidden_new = gelu_tanh(pre_act).astype(jnp.bfloat16)
    _, pullback = jax.vjp(gelu_tanh, pre_act)
    back_pre = pullback(back_hidden)[0].astype(jnp.bfloat16)
    bias_term = jnp.sum(back_pre.astype(jnp.float32), axis=(0, 2))
    first_mine, first_theirs = halves(agg_first)
    first_got, back_got = lax.ppermute((first_theirs, back_pre), "dom", pair)
    first_term = jnp.einsum(
        "vprn,vhn->prh", first_mine, back_pre, preferred_element_type=jnp.float32
    ) + jnp.einsum("vprn,vhn->prh", first_got, back_got, preferred_element_type=jnp.float32)

    agg_second = aggregate(hidden_new, pulled_second, tile_src, tile_count, slot_live, tile_values)
    second_mine, second_theirs = halves(agg_second)
    second_got = lax.ppermute(second_theirs, "dom", pair)
    second_term = jnp.einsum(
        "vprn,vbn->prb", second_mine, out_grad, preferred_element_type=jnp.float32
    ) + jnp.einsum("vprn,vbn->prb", second_got, partner_grad, preferred_element_type=jnp.float32)

    half_rows = first_term.shape[1]
    lanes = 128
    bias_cols = jnp.zeros((fsdp_size, 2 * half_rows, lanes), jnp.float32)
    bias_cols = bias_cols.at[:, 0, : hidden // fsdp_size].set(bias_term.reshape(fsdp_size, hidden // fsdp_size))
    packed_terms = jnp.concatenate([jnp.concatenate([first_term, second_term], axis=1), bias_cols], axis=2)
    packed_terms = packed_terms.reshape(fsdp_size * 2 * half_rows, hidden + lanes)
    arrived_terms = lax.all_to_all(
        packed_terms.reshape(fsdp_size, 2 * half_rows, hidden + lanes), "fsdp", split_axis=0, concat_axis=0, tiled=True
    )
    shard = jnp.sum(arrived_terms, axis=0)
    everyone = lax.all_to_all(
        jnp.broadcast_to(shard[None], (dom_size,) + shard.shape), "dom", split_axis=0, concat_axis=0, tiled=True
    )
    by_core = jnp.sum(everyone.reshape(dom_size // 2, 2, 2 * half_rows, hidden + lanes), axis=0)
    first_total = by_core[:, :half_rows, :hidden].reshape(2 * half_rows, hidden)
    second_total = by_core[:, half_rows:, :hidden].reshape(2 * half_rows, hidden)
    bias_total = jnp.sum(by_core[:, 0, hidden : hidden + hidden // fsdp_size], axis=0)
    return (hidden_new, first_total, second_total, bias_total)


def solution(mesh):
    return jax.shard_map(
        on_device,
        mesh=mesh,
        in_specs=(
            P(("dom", "fsdp"), None, None),
            P("dom", "fsdp", None),
            P("dom", "fsdp", None),
            P("dom", None, None),
            P("dom", None),
            P(("dom", "fsdp"), None),
            P(("dom", "fsdp")),
            P(("dom", "fsdp"), None, None, None),
            P("fsdp", None),
            P("fsdp", None),
            P("fsdp"),
            P(("dom", "fsdp"), None, None),
        ),
        out_specs=(P(("dom", "fsdp"), None, None), P("fsdp", None), P("fsdp", None), P("fsdp")),
        check_vma=False,
    )
```

```python
import functools

import jax
import jax.numpy as jnp
from jax import lax
from jax.experimental import pallas as pl
from jax.experimental.pallas import tpu as pltpu
from jax.sharding import PartitionSpec as P


def gelu_tanh(inputs):
    return jax.nn.gelu(inputs, approximate=True)


def _agg_kernel(own_count, last_tile, src_ref, cnt_ref, live_ref, own_ref, pulled_ref, tile_ref, out_ref, acc_ref):
    v = pl.program_id(0)
    t = pl.program_id(1)

    @pl.when(t == 0)
    def _():
        acc_ref[...] = jnp.zeros_like(acc_ref)

    src = src_ref[v, t]
    tile_live = t < cnt_ref[v]
    own_ok = tile_live & (src < own_count)
    pull_ok = tile_live & (src >= own_count) & (live_ref[jnp.maximum(src - own_count, 0)] > 0)

    @pl.when(own_ok)
    def _():
        acc_ref[...] += jnp.dot(own_ref[0], tile_ref[0, 0], preferred_element_type=jnp.float32)

    @pl.when(pull_ok)
    def _():
        block = pulled_ref[0, :, 0]
        block = block.reshape(block.shape[0] * block.shape[1], block.shape[2])
        acc_ref[...] += jnp.dot(block, tile_ref[0, 0], preferred_element_type=jnp.float32)

    @pl.when(t == last_tile)
    def _():
        out_ref[0] = acc_ref[...].astype(out_ref.dtype)


def aggregate(own, pulled, tile_src, tile_count, slot_live, tile_values):
    nb, feat, blk = own.shape
    dom, fsdp, cap = pulled.shape[0], pulled.shape[1], pulled.shape[2]
    tiles = tile_src.shape[1]

    def eff(v, t, src_ref, cnt_ref):
        return jnp.minimum(t, cnt_ref[v] - 1)

    def own_map(v, t, src_ref, cnt_ref, live_ref):
        s = src_ref[v, eff(v, t, src_ref, cnt_ref)]
        return (jnp.clip(s, 0, nb - 1), 0, 0)

    def pulled_map(v, t, src_ref, cnt_ref, live_ref):
        s = jnp.clip(src_ref[v, eff(v, t, src_ref, cnt_ref)] - nb, 0, cap * dom - 1)
        return (s % dom, 0, s // dom, 0, 0)

    def tile_map(v, t, src_ref, cnt_ref, live_ref):
        return (v, eff(v, t, src_ref, cnt_ref), 0, 0)

    def out_map(v, t, src_ref, cnt_ref, live_ref):
        return (v, 0, 0)

    grid_spec = pltpu.PrefetchScalarGridSpec(
        num_scalar_prefetch=3,
        grid=(nb, tiles),
        in_specs=[
            pl.BlockSpec((1, feat, blk), own_map),
            pl.BlockSpec((1, fsdp, 1) + pulled.shape[3:], pulled_map),
            pl.BlockSpec((1, 1, blk, blk), tile_map),
        ],
        out_specs=pl.BlockSpec((1, feat, blk), out_map),
        scratch_shapes=[pltpu.VMEM((feat, blk), jnp.float32)],
    )
    flops = 2 * nb * tiles * feat * blk * blk
    return pl.pallas_call(
        functools.partial(_agg_kernel, nb, tiles - 1),
        grid_spec=grid_spec,
        out_shape=jax.ShapeDtypeStruct(own.shape, jnp.bfloat16),
        compiler_params=pltpu.CompilerParams(dimension_semantics=("arbitrary", "arbitrary")),
        cost_estimate=pl.CostEstimate(
            flops=flops, transcendentals=0, bytes_accessed=nb * tiles * (2 * feat * blk * 2 + blk * blk * 2) + own.size * 2
        ),
    )(tile_src, tile_count, slot_live, own, pulled, tile_values)


def _spread_kernel(own_count, src_ref, cnt_ref, back_ref, tile_ref, out_ref):
    v = pl.program_id(0)
    t = pl.program_id(1)

    @pl.when((v == 0) & (t == 0))
    def _():
        out_ref[...] = jnp.zeros_like(out_ref)

    src = src_ref[v, t]

    @pl.when((t < cnt_ref[v]) & (src < own_count))
    def _():
        term = lax.dot_general(
            back_ref[0], tile_ref[0, 0], (((1,), (1,)), ((), ())), preferred_element_type=jnp.float32
        )
        out_ref[src] = out_ref[src] + term


def spread_back(back_second, tile_src, tile_count, tile_values):
    nb, width, blk = back_second.shape
    tiles = tile_src.shape[1]

    def eff(v, t, cnt_ref):
        return jnp.minimum(t, cnt_ref[v] - 1)

    grid_spec = pltpu.PrefetchScalarGridSpec(
        num_scalar_prefetch=2,
        grid=(nb, tiles),
        in_specs=[
            pl.BlockSpec((1, width, blk), lambda v, t, s, c: (v, 0, 0)),
            pl.BlockSpec((1, 1, blk, blk), lambda v, t, s, c: (v, eff(v, t, c), 0, 0)),
        ],
        out_specs=pl.BlockSpec((nb, width, blk), lambda v, t, s, c: (0, 0, 0)),
    )
    return pl.pallas_call(
        functools.partial(_spread_kernel, nb),
        grid_spec=grid_spec,
        out_shape=jax.ShapeDtypeStruct(back_second.shape, jnp.float32),
        compiler_params=pltpu.CompilerParams(dimension_semantics=("arbitrary", "arbitrary")),
        cost_estimate=pl.CostEstimate(
            flops=2 * nb * tiles * width * blk * blk,
            transcendentals=0,
            bytes_accessed=back_second.size * 2 + nb * tiles * blk * blk * 2 + back_second.size * 4,
        ),
    )(tile_src, tile_count, back_second, tile_values)


def gather_rows(x, axis):
    n = lax.axis_size(axis)
    spread = lax.all_to_all(jnp.broadcast_to(x[None], (n,) + x.shape), axis, split_axis=0, concat_axis=0, tiled=True)
    return spread.reshape((n * x.shape[0],) + x.shape[1:])


def on_device(
    features,
    history_first,
    history_second,
    pull_list,
    pull_count,
    tile_src,
    tile_count,
    tile_values,
    w_first,
    w_second,
    bias_first,
    out_grad,
):
    dom_size = lax.axis_size("dom")
    fsdp_size = lax.axis_size("fsdp")
    me = lax.axis_index("dom") * fsdp_size + lax.axis_index("fsdp")
    rows, hidden = w_first.shape
    bias_cols = jnp.broadcast_to(bias_first[:, None], (rows, 128))
    packed = gather_rows(jnp.concatenate([w_first, bias_cols], axis=1), "fsdp")
    first_full = packed[:, :hidden]
    bias_full = packed[:, hidden].astype(jnp.float32)
    second_full = gather_rows(w_second, "fsdp")

    chosen = pull_list[0]
    requesters, slot_cap = chosen.shape
    counts_all = lax.all_gather(pull_count, "dom", axis=0, tiled=True)
    counts_all, chosen = lax.optimization_barrier((counts_all, chosen))
    my_counts = lax.dynamic_index_in_dim(counts_all, me, axis=1, keepdims=False)
    slot_live = (lax.broadcasted_iota(jnp.int32, (slot_cap, dom_size), 0) < my_counts[None, :]).astype(jnp.int32)
    slot_live = slot_live.reshape(-1)

    block_len = features.shape[2]
    first_cols = history_first.shape[1]
    second_cols = history_second.shape[1]
    sent_first = jnp.take(history_first, chosen.reshape(-1), axis=0, mode="clip").reshape(requesters, slot_cap, first_cols, block_len)
    sent_second = jnp.take(history_second, chosen.reshape(-1), axis=0, mode="clip").reshape(requesters, slot_cap, second_cols, block_len)
    arrived_first = lax.all_to_all(sent_first, ("dom", "fsdp"), split_axis=0, concat_axis=0, tiled=True)
    arrived_second = lax.all_to_all(sent_second, ("dom", "fsdp"), split_axis=0, concat_axis=0, tiled=True)
    pulled_first = arrived_first.reshape(dom_size, fsdp_size, slot_cap, first_cols, block_len)
    pulled_second = arrived_second.reshape(dom_size, fsdp_size, slot_cap, second_cols, block_len)

    core = lax.axis_index("dom") % 2
    pair = [(d, d ^ 1) for d in range(dom_size)]
    partner_grad = lax.ppermute(out_grad, "dom", pair)

    back_second = jnp.einsum(
        "ab,vbn->van", second_full, out_grad, preferred_element_type=jnp.float32
    ).astype(jnp.bfloat16)
    back_hidden = spread_back(back_second, tile_src, tile_count, tile_values)

    def halves(x):
        split = x.reshape(x.shape[0], fsdp_size, 2, x.shape[1] // (2 * fsdp_size), x.shape[2])
        mine = lax.dynamic_index_in_dim(split, core, axis=2, keepdims=False)
        theirs = lax.dynamic_index_in_dim(split, 1 - core, axis=2, keepdims=False)
        return mine, theirs

    agg_first = aggregate(features, pulled_first, tile_src, tile_count, slot_live, tile_values)
    pre_act = (
        jnp.einsum("fh,vfn->vhn", first_full, agg_first, preferred_element_type=jnp.float32)
        + bias_full[None, :, None]
    )
    hidden_new = gelu_tanh(pre_act).astype(jnp.bfloat16)
    _, pullback = jax.vjp(gelu_tanh, pre_act)
    back_pre = pullback(back_hidden)[0].astype(jnp.bfloat16)
    bias_term = jnp.sum(back_pre.astype(jnp.float32), axis=(0, 2))
    first_mine, first_theirs = halves(agg_first)
    first_got, back_got = lax.ppermute((first_theirs, back_pre), "dom", pair)
    first_term = jnp.einsum(
        "vprn,vhn->prh", first_mine, back_pre, preferred_element_type=jnp.float32
    ) + jnp.einsum("vprn,vhn->prh", first_got, back_got, preferred_element_type=jnp.float32)

    half_rows = first_term.shape[1]
    lanes = 128
    bias_cols = jnp.zeros((fsdp_size, half_rows, lanes), jnp.float32)
    bias_cols = bias_cols.at[:, 0, : hidden // fsdp_size].set(bias_term.reshape(fsdp_size, hidden // fsdp_size))
    first_packed = jnp.concatenate([first_term, bias_cols], axis=2)
    first_shard = jnp.sum(lax.all_to_all(first_packed, "fsdp", split_axis=0, concat_axis=0, tiled=True), axis=0)

    agg_second = aggregate(hidden_new, pulled_second, tile_src, tile_count, slot_live, tile_values)
    second_mine, second_theirs = halves(agg_second)
    second_got = lax.ppermute(second_theirs, "dom", pair)
    second_term = jnp.einsum(
        "vprn,vbn->prb", second_mine, out_grad, preferred_element_type=jnp.float32
    ) + jnp.einsum("vprn,vbn->prb", second_got, partner_grad, preferred_element_type=jnp.float32)
    second_shard = jnp.sum(lax.all_to_all(second_term, "fsdp", split_axis=0, concat_axis=0, tiled=True), axis=0)

    shard = jnp.concatenate([first_shard, jnp.pad(second_shard, ((0, 0), (0, lanes)))], axis=0)
    for flip in (2, 4):
        shard = shard + lax.ppermute(shard, "dom", [(d, d ^ flip) for d in range(dom_size)])
    other = lax.ppermute(shard, "dom", pair)
    low = jnp.where(core == 0, shard, other)
    high = jnp.where(core == 0, other, shard)
    first_total = jnp.concatenate([low[:half_rows, :hidden], high[:half_rows, :hidden]], axis=0)
    second_total = jnp.concatenate([low[half_rows:, :hidden], high[half_rows:, :hidden]], axis=0)
    bias_total = (shard + other)[0, hidden : hidden + hidden // fsdp_size]
    return (hidden_new, first_total, second_total, bias_total)


def solution(mesh):
    return jax.shard_map(
        on_device,
        mesh=mesh,
        in_specs=(
            P(("dom", "fsdp"), None, None),
            P("dom", "fsdp", None),
            P("dom", "fsdp", None),
            P("dom", None, None),
            P("dom", None),
            P(("dom", "fsdp"), None),
            P(("dom", "fsdp")),
            P(("dom", "fsdp"), None, None, None),
            P("fsdp", None),
            P("fsdp", None),
            P("fsdp"),
            P(("dom", "fsdp"), None, None),
        ),
        out_specs=(P(("dom", "fsdp"), None, None), P("fsdp", None), P("fsdp", None), P("fsdp")),
        check_vma=False,
    )
```

```python
import functools

import jax
import jax.numpy as jnp
from jax import lax
from jax.experimental import pallas as pl
from jax.experimental.pallas import tpu as pltpu
from jax.sharding import PartitionSpec as P


def gelu_tanh(inputs):
    return jax.nn.gelu(inputs, approximate=True)


def _agg_kernel(own_count, last_tile, src_ref, cnt_ref, live_ref, own_ref, pulled_ref, tile_ref, out_ref, acc_ref):
    v = pl.program_id(0)
    t = pl.program_id(1)

    @pl.when(t == 0)
    def _():
        acc_ref[...] = jnp.zeros_like(acc_ref)

    src = src_ref[v, t]
    tile_live = t < cnt_ref[v]
    own_ok = tile_live & (src < own_count)
    pull_ok = tile_live & (src >= own_count) & (live_ref[jnp.maximum(src - own_count, 0)] > 0)

    @pl.when(own_ok)
    def _():
        acc_ref[...] += jnp.dot(own_ref[0], tile_ref[0, 0], preferred_element_type=jnp.float32)

    @pl.when(pull_ok)
    def _():
        block = pulled_ref[0, :, 0]
        block = block.reshape(block.shape[0] * block.shape[1], block.shape[2])
        acc_ref[...] += jnp.dot(block, tile_ref[0, 0], preferred_element_type=jnp.float32)

    @pl.when(t == last_tile)
    def _():
        out_ref[0] = acc_ref[...].astype(out_ref.dtype)


def aggregate(own, pulled, tile_src, tile_count, slot_live, tile_values):
    nb, feat, blk = own.shape
    dom, fsdp, cap = pulled.shape[0], pulled.shape[1], pulled.shape[2]
    tiles = tile_src.shape[1]

    def eff(v, t, src_ref, cnt_ref):
        return jnp.minimum(t, cnt_ref[v] - 1)

    def own_map(v, t, src_ref, cnt_ref, live_ref):
        s = src_ref[v, eff(v, t, src_ref, cnt_ref)]
        return (jnp.clip(s, 0, nb - 1), 0, 0)

    def pulled_map(v, t, src_ref, cnt_ref, live_ref):
        s = jnp.clip(src_ref[v, eff(v, t, src_ref, cnt_ref)] - nb, 0, cap * dom - 1)
        return (s % dom, 0, s // dom, 0, 0)

    def tile_map(v, t, src_ref, cnt_ref, live_ref):
        return (v, eff(v, t, src_ref, cnt_ref), 0, 0)

    def out_map(v, t, src_ref, cnt_ref, live_ref):
        return (v, 0, 0)

    grid_spec = pltpu.PrefetchScalarGridSpec(
        num_scalar_prefetch=3,
        grid=(nb, tiles),
        in_specs=[
            pl.BlockSpec((1, feat, blk), own_map),
            pl.BlockSpec((1, fsdp, 1) + pulled.shape[3:], pulled_map),
            pl.BlockSpec((1, 1, blk, blk), tile_map),
        ],
        out_specs=pl.BlockSpec((1, feat, blk), out_map),
        scratch_shapes=[pltpu.VMEM((feat, blk), jnp.float32)],
    )
    flops = 2 * nb * tiles * feat * blk * blk
    return pl.pallas_call(
        functools.partial(_agg_kernel, nb, tiles - 1),
        grid_spec=grid_spec,
        out_shape=jax.ShapeDtypeStruct(own.shape, jnp.bfloat16),
        compiler_params=pltpu.CompilerParams(dimension_semantics=("arbitrary", "arbitrary")),
        cost_estimate=pl.CostEstimate(
            flops=flops, transcendentals=0, bytes_accessed=nb * tiles * (2 * feat * blk * 2 + blk * blk * 2) + own.size * 2
        ),
    )(tile_src, tile_count, slot_live, own, pulled, tile_values)


def _spread_kernel(own_count, src_ref, cnt_ref, back_ref, tile_ref, out_ref):
    v = pl.program_id(0)
    t = pl.program_id(1)

    @pl.when((v == 0) & (t == 0))
    def _():
        out_ref[...] = jnp.zeros_like(out_ref)

    src = src_ref[v, t]

    @pl.when((t < cnt_ref[v]) & (src < own_count))
    def _():
        term = lax.dot_general(
            back_ref[0], tile_ref[0, 0], (((1,), (1,)), ((), ())), preferred_element_type=jnp.float32
        )
        out_ref[src] = out_ref[src] + term


def spread_back(back_second, tile_src, tile_count, tile_values):
    nb, width, blk = back_second.shape
    tiles = tile_src.shape[1]

    def eff(v, t, cnt_ref):
        return jnp.minimum(t, cnt_ref[v] - 1)

    grid_spec = pltpu.PrefetchScalarGridSpec(
        num_scalar_prefetch=2,
        grid=(nb, tiles),
        in_specs=[
            pl.BlockSpec((1, width, blk), lambda v, t, s, c: (v, 0, 0)),
            pl.BlockSpec((1, 1, blk, blk), lambda v, t, s, c: (v, eff(v, t, c), 0, 0)),
        ],
        out_specs=pl.BlockSpec((nb, width, blk), lambda v, t, s, c: (0, 0, 0)),
    )
    return pl.pallas_call(
        functools.partial(_spread_kernel, nb),
        grid_spec=grid_spec,
        out_shape=jax.ShapeDtypeStruct(back_second.shape, jnp.float32),
        compiler_params=pltpu.CompilerParams(dimension_semantics=("arbitrary", "arbitrary")),
        cost_estimate=pl.CostEstimate(
            flops=2 * nb * tiles * width * blk * blk,
            transcendentals=0,
            bytes_accessed=back_second.size * 2 + nb * tiles * blk * blk * 2 + back_second.size * 4,
        ),
    )(tile_src, tile_count, back_second, tile_values)


def gather_rows(x, axis):
    n = lax.axis_size(axis)
    spread = lax.all_to_all(jnp.broadcast_to(x[None], (n,) + x.shape), axis, split_axis=0, concat_axis=0, tiled=True)
    return spread.reshape((n * x.shape[0],) + x.shape[1:])


def on_device(
    features,
    history_first,
    history_second,
    pull_list,
    pull_count,
    tile_src,
    tile_count,
    tile_values,
    w_first,
    w_second,
    bias_first,
    out_grad,
):
    dom_size = lax.axis_size("dom")
    fsdp_size = lax.axis_size("fsdp")
    me = lax.axis_index("dom") * fsdp_size + lax.axis_index("fsdp")
    rows, hidden = w_first.shape
    bias_cols = jnp.broadcast_to(bias_first[:, None], (rows, 128))
    packed = gather_rows(jnp.concatenate([w_first, bias_cols], axis=1), "fsdp")
    first_full = packed[:, :hidden]
    bias_full = packed[:, hidden].astype(jnp.float32)
    second_full = gather_rows(w_second, "fsdp")

    chosen = pull_list[0]
    requesters, slot_cap = chosen.shape
    counts_all = lax.all_gather(pull_count, "dom", axis=0, tiled=True)
    counts_all, chosen = lax.optimization_barrier((counts_all, chosen))
    my_counts = lax.dynamic_index_in_dim(counts_all, me, axis=1, keepdims=False)
    slot_live = (lax.broadcasted_iota(jnp.int32, (slot_cap, dom_size), 0) < my_counts[None, :]).astype(jnp.int32)
    slot_live = slot_live.reshape(-1)

    block_len = features.shape[2]
    first_cols = history_first.shape[1]
    second_cols = history_second.shape[1]
    sent_first = jnp.take(history_first, chosen.reshape(-1), axis=0, mode="clip").reshape(requesters, slot_cap, first_cols, block_len)
    sent_second = jnp.take(history_second, chosen.reshape(-1), axis=0, mode="clip").reshape(requesters, slot_cap, second_cols, block_len)
    arrived_first = lax.all_to_all(sent_first, ("dom", "fsdp"), split_axis=0, concat_axis=0, tiled=True)
    arrived_second = lax.all_to_all(sent_second, ("dom", "fsdp"), split_axis=0, concat_axis=0, tiled=True)
    pulled_first = arrived_first.reshape(dom_size, fsdp_size, slot_cap, first_cols, block_len)
    pulled_second = arrived_second.reshape(dom_size, fsdp_size, slot_cap, second_cols, block_len)

    core = lax.axis_index("dom") % 2
    pair = [(d, d ^ 1) for d in range(dom_size)]
    partner_grad = lax.ppermute(out_grad, "dom", pair)

    back_second = jnp.einsum(
        "ab,vbn->van", second_full, out_grad, preferred_element_type=jnp.float32
    ).astype(jnp.bfloat16)
    back_hidden = spread_back(back_second, tile_src, tile_count, tile_values)

    def halves(x):
        split = x.reshape(x.shape[0], fsdp_size, 2, x.shape[1] // (2 * fsdp_size), x.shape[2])
        mine = lax.dynamic_index_in_dim(split, core, axis=2, keepdims=False)
        theirs = lax.dynamic_index_in_dim(split, 1 - core, axis=2, keepdims=False)
        return mine, theirs

    agg_first = aggregate(features, pulled_first, tile_src, tile_count, slot_live, tile_values)
    pre_act = (
        jnp.einsum("fh,vfn->vhn", first_full, agg_first, preferred_element_type=jnp.float32)
        + bias_full[None, :, None]
    )
    hidden_new = gelu_tanh(pre_act).astype(jnp.bfloat16)
    _, pullback = jax.vjp(gelu_tanh, pre_act)
    back_pre = pullback(back_hidden)[0].astype(jnp.bfloat16)
    bias_term = jnp.sum(back_pre.astype(jnp.float32), axis=(0, 2))
    first_mine, first_theirs = halves(agg_first)
    first_got, back_got = lax.ppermute((first_theirs, back_pre), "dom", pair)
    first_term = jnp.einsum(
        "vprn,vhn->prh", first_mine, back_pre, preferred_element_type=jnp.float32
    ) + jnp.einsum("vprn,vhn->prh", first_got, back_got, preferred_element_type=jnp.float32)

    half_rows = first_term.shape[1]
    lanes = 128
    agg_second = aggregate(hidden_new, pulled_second, tile_src, tile_count, slot_live, tile_values)
    second_mine, second_theirs = halves(agg_second)
    second_got = lax.ppermute(second_theirs, "dom", pair)
    second_term = jnp.einsum(
        "vprn,vbn->prb", second_mine, out_grad, preferred_element_type=jnp.float32
    ) + jnp.einsum("vprn,vbn->prb", second_got, partner_grad, preferred_element_type=jnp.float32)

    bias_cols = jnp.zeros((fsdp_size, 2 * half_rows, lanes), jnp.float32)
    bias_cols = bias_cols.at[:, 0, : hidden // fsdp_size].set(bias_term.reshape(fsdp_size, hidden // fsdp_size))
    packed_terms = jnp.concatenate([jnp.concatenate([first_term, second_term], axis=1), bias_cols], axis=2)
    arrived_terms = lax.all_to_all(packed_terms.astype(jnp.bfloat16), "fsdp", split_axis=0, concat_axis=0, tiled=True)
    shard = jnp.sum(arrived_terms.astype(jnp.float32), axis=0)
    for flip in (2, 4):
        shard = shard + lax.ppermute(shard, "dom", [(d, d ^ flip) for d in range(dom_size)])
    other = lax.ppermute(shard, "dom", pair)
    low = jnp.where(core == 0, shard, other)
    high = jnp.where(core == 0, other, shard)
    first_total = jnp.concatenate([low[:half_rows, :hidden], high[:half_rows, :hidden]], axis=0)
    second_total = jnp.concatenate([low[half_rows:, :hidden], high[half_rows:, :hidden]], axis=0)
    bias_total = (shard + other)[0, hidden : hidden + hidden // fsdp_size]
    return (hidden_new, first_total, second_total, bias_total)


def solution(mesh):
    return jax.shard_map(
        on_device,
        mesh=mesh,
        in_specs=(
            P(("dom", "fsdp"), None, None),
            P("dom", "fsdp", None),
            P("dom", "fsdp", None),
            P("dom", None, None),
            P("dom", None),
            P(("dom", "fsdp"), None),
            P(("dom", "fsdp")),
            P(("dom", "fsdp"), None, None, None),
            P("fsdp", None),
            P("fsdp", None),
            P("fsdp"),
            P(("dom", "fsdp"), None, None),
        ),
        out_specs=(P(("dom", "fsdp"), None, None), P("fsdp", None), P("fsdp", None), P("fsdp")),
        check_vma=False,
    )
```

```python
import functools

import jax
import jax.numpy as jnp
from jax import lax
from jax.experimental import pallas as pl
from jax.experimental.pallas import tpu as pltpu
from jax.sharding import PartitionSpec as P


def gelu_tanh(inputs):
    return jax.nn.gelu(inputs, approximate=True)


def _agg_kernel(own_count, last_tile, src_ref, cnt_ref, live_ref, own_ref, pulled_ref, tile_ref, out_ref, acc_ref):
    v = pl.program_id(0)
    t = pl.program_id(1)

    @pl.when(t == 0)
    def _():
        acc_ref[...] = jnp.zeros_like(acc_ref)

    src = src_ref[v, t]
    tile_live = t < cnt_ref[v]
    own_ok = tile_live & (src < own_count)
    pull_ok = tile_live & (src >= own_count) & (live_ref[jnp.maximum(src - own_count, 0)] > 0)

    @pl.when(own_ok)
    def _():
        acc_ref[...] += jnp.dot(own_ref[0], tile_ref[0, 0], preferred_element_type=jnp.float32)

    @pl.when(pull_ok)
    def _():
        block = pulled_ref[0]
        block = block.reshape(block.shape[0] * block.shape[1], block.shape[2])
        acc_ref[...] += jnp.dot(block, tile_ref[0, 0], preferred_element_type=jnp.float32)

    @pl.when(t == last_tile)
    def _():
        out_ref[0] = acc_ref[...].astype(out_ref.dtype)


def aggregate(own, pulled, cap, tile_src, tile_count, slot_live, tile_values):
    nb, feat, blk = own.shape
    dom, fsdp = pulled.shape[0], pulled.shape[1]
    cols = feat // fsdp
    tiles = tile_src.shape[1]

    def eff(v, t, src_ref, cnt_ref):
        return jnp.minimum(t, cnt_ref[v] - 1)

    def own_map(v, t, src_ref, cnt_ref, live_ref):
        s = src_ref[v, eff(v, t, src_ref, cnt_ref)]
        return (jnp.clip(s, 0, nb - 1), 0, 0)

    def pulled_map(v, t, src_ref, cnt_ref, live_ref):
        s = jnp.clip(src_ref[v, eff(v, t, src_ref, cnt_ref)] - nb, 0, cap * dom - 1)
        return (s % dom, 0, s // dom, 0)

    def tile_map(v, t, src_ref, cnt_ref, live_ref):
        return (v, eff(v, t, src_ref, cnt_ref), 0, 0)

    def out_map(v, t, src_ref, cnt_ref, live_ref):
        return (v, 0, 0)

    grid_spec = pltpu.PrefetchScalarGridSpec(
        num_scalar_prefetch=3,
        grid=(nb, tiles),
        in_specs=[
            pl.BlockSpec((1, feat, blk), own_map),
            pl.BlockSpec((1, fsdp, cols, blk), pulled_map),
            pl.BlockSpec((1, 1, blk, blk), tile_map),
        ],
        out_specs=pl.BlockSpec((1, feat, blk), out_map),
        scratch_shapes=[pltpu.VMEM((feat, blk), jnp.float32)],
    )
    flops = 2 * nb * tiles * feat * blk * blk
    return pl.pallas_call(
        functools.partial(_agg_kernel, nb, tiles - 1),
        grid_spec=grid_spec,
        out_shape=jax.ShapeDtypeStruct(own.shape, jnp.bfloat16),
        compiler_params=pltpu.CompilerParams(dimension_semantics=("arbitrary", "arbitrary")),
        cost_estimate=pl.CostEstimate(
            flops=flops, transcendentals=0, bytes_accessed=nb * tiles * (2 * feat * blk * 2 + blk * blk * 2) + own.size * 2
        ),
    )(tile_src, tile_count, slot_live, own, pulled, tile_values)


def _spread_kernel(own_count, src_ref, cnt_ref, back_ref, tile_ref, out_ref):
    v = pl.program_id(0)
    t = pl.program_id(1)

    @pl.when((v == 0) & (t == 0))
    def _():
        out_ref[...] = jnp.zeros_like(out_ref)

    src = src_ref[v, t]

    @pl.when((t < cnt_ref[v]) & (src < own_count))
    def _():
        term = lax.dot_general(
            back_ref[0], tile_ref[0, 0], (((1,), (1,)), ((), ())), preferred_element_type=jnp.float32
        )
        out_ref[src] = out_ref[src] + term


def spread_back(back_second, tile_src, tile_count, tile_values):
    nb, width, blk = back_second.shape
    tiles = tile_src.shape[1]

    def eff(v, t, cnt_ref):
        return jnp.minimum(t, cnt_ref[v] - 1)

    grid_spec = pltpu.PrefetchScalarGridSpec(
        num_scalar_prefetch=2,
        grid=(nb, tiles),
        in_specs=[
            pl.BlockSpec((1, width, blk), lambda v, t, s, c: (v, 0, 0)),
            pl.BlockSpec((1, 1, blk, blk), lambda v, t, s, c: (v, eff(v, t, c), 0, 0)),
        ],
        out_specs=pl.BlockSpec((nb, width, blk), lambda v, t, s, c: (0, 0, 0)),
    )
    return pl.pallas_call(
        functools.partial(_spread_kernel, nb),
        grid_spec=grid_spec,
        out_shape=jax.ShapeDtypeStruct(back_second.shape, jnp.float32),
        compiler_params=pltpu.CompilerParams(dimension_semantics=("arbitrary", "arbitrary")),
        cost_estimate=pl.CostEstimate(
            flops=2 * nb * tiles * width * blk * blk,
            transcendentals=0,
            bytes_accessed=back_second.size * 2 + nb * tiles * blk * blk * 2 + back_second.size * 4,
        ),
    )(tile_src, tile_count, back_second, tile_values)


def on_device(
    features,
    history_first,
    history_second,
    pull_list,
    pull_count,
    tile_src,
    tile_count,
    tile_values,
    w_first,
    w_second,
    bias_first,
    out_grad,
):
    dom_size = lax.axis_size("dom")
    fsdp_size = lax.axis_size("fsdp")
    dom_idx = lax.axis_index("dom")
    me = dom_idx * fsdp_size + lax.axis_index("fsdp")
    rows, hidden = w_first.shape
    chosen = pull_list[0]
    requesters, slot_cap = chosen.shape
    block_len = features.shape[2]
    first_cols = history_first.shape[1]
    second_cols = history_second.shape[1]
    piece = rows // dom_size
    piece_rows = piece * hidden // block_len

    def weight_piece(w):
        part = lax.dynamic_slice_in_dim(w, dom_idx * piece, piece, axis=0).reshape(1, piece_rows, block_len)
        return jnp.broadcast_to(part, (requesters, piece_rows, block_len))

    misc = jnp.zeros((requesters, 8, block_len), jnp.bfloat16)
    misc = misc.at[:, 0, :piece].set(lax.dynamic_slice_in_dim(bias_first, dom_idx * piece, piece)[None, :])
    misc = misc.at[:, 0, piece].set(pull_count[0].astype(jnp.bfloat16))
    taken_first = jnp.take(history_first, chosen.reshape(-1), axis=0, mode="clip")
    sent_first = jnp.concatenate(
        [
            taken_first.reshape(requesters, slot_cap * first_cols, block_len),
            weight_piece(w_first),
            weight_piece(w_second),
            misc,
        ],
        axis=1,
    )
    sent_second = jnp.take(history_second, chosen.reshape(-1), axis=0, mode="clip").reshape(requesters, slot_cap, second_cols, block_len)
    arrived_first = lax.all_to_all(sent_first, ("dom", "fsdp"), split_axis=0, concat_axis=0, tiled=True)
    arrived_second = lax.all_to_all(sent_second, ("dom", "fsdp"), split_axis=0, concat_axis=0, tiled=True)
    by_source = arrived_first.reshape(dom_size, fsdp_size, arrived_first.shape[1], block_len)
    pulled_first = by_source
    pulled_second = arrived_second.reshape(dom_size, fsdp_size, slot_cap * second_cols, block_len)

    def weight_from(offset):
        got = by_source[:, :, offset : offset + piece_rows].reshape(dom_size, fsdp_size, piece, hidden)
        return jnp.transpose(got, (1, 0, 2, 3)).reshape(fsdp_size * dom_size * piece, hidden)

    hist_rows = slot_cap * first_cols
    first_full = weight_from(hist_rows)
    second_full = weight_from(hist_rows + piece_rows)
    misc_rows = by_source[:, :, hist_rows + 2 * piece_rows]
    bias_full = jnp.transpose(misc_rows[:, :, :piece], (1, 0, 2)).reshape(-1).astype(jnp.float32)
    my_counts = misc_rows[:, 0, piece].astype(jnp.int32)
    slot_live = (lax.broadcasted_iota(jnp.int32, (slot_cap, dom_size), 0) < my_counts[None, :]).astype(jnp.int32)
    slot_live = slot_live.reshape(-1)

    core = lax.axis_index("dom") % 2
    pair = [(d, d ^ 1) for d in range(dom_size)]
    partner_grad = lax.ppermute(out_grad, "dom", pair)

    back_second = jnp.einsum(
        "ab,vbn->van", second_full, out_grad, preferred_element_type=jnp.float32
    ).astype(jnp.bfloat16)
    back_hidden = spread_back(back_second, tile_src, tile_count, tile_values)

    def halves(x):
        split = x.reshape(x.shape[0], fsdp_size, 2, x.shape[1] // (2 * fsdp_size), x.shape[2])
        mine = lax.dynamic_index_in_dim(split, core, axis=2, keepdims=False)
        theirs = lax.dynamic_index_in_dim(split, 1 - core, axis=2, keepdims=False)
        return mine, theirs

    agg_first = aggregate(features, pulled_first, slot_cap, tile_src, tile_count, slot_live, tile_values)
    pre_act = (
        jnp.einsum("fh,vfn->vhn", first_full, agg_first, preferred_element_type=jnp.float32)
        + bias_full[None, :, None]
    )
    hidden_new = gelu_tanh(pre_act).astype(jnp.bfloat16)
    _, pullback = jax.vjp(gelu_tanh, pre_act)
    back_pre = pullback(back_hidden)[0].astype(jnp.bfloat16)
    bias_term = jnp.sum(back_pre.astype(jnp.float32), axis=(0, 2))
    first_mine, first_theirs = halves(agg_first)
    first_got, back_got = lax.ppermute((first_theirs, back_pre), "dom", pair)
    first_term = jnp.einsum(
        "vprn,vhn->prh", first_mine, back_pre, preferred_element_type=jnp.float32
    ) + jnp.einsum("vprn,vhn->prh", first_got, back_got, preferred_element_type=jnp.float32)

    half_rows = first_term.shape[1]
    lanes = 128
    agg_second = aggregate(hidden_new, pulled_second, slot_cap, tile_src, tile_count, slot_live, tile_values)
    second_mine, second_theirs = halves(agg_second)
    second_got = lax.ppermute(second_theirs, "dom", pair)
    second_term = jnp.einsum(
        "vprn,vbn->prb", second_mine, out_grad, preferred_element_type=jnp.float32
    ) + jnp.einsum("vprn,vbn->prb", second_got, partner_grad, preferred_element_type=jnp.float32)

    bias_cols = jnp.zeros((fsdp_size, 2 * half_rows, lanes), jnp.float32)
    bias_cols = bias_cols.at[:, 0, : hidden // fsdp_size].set(bias_term.reshape(fsdp_size, hidden // fsdp_size))
    packed_terms = jnp.concatenate([jnp.concatenate([first_term, second_term], axis=1), bias_cols], axis=2)
    arrived_terms = lax.all_to_all(packed_terms.astype(jnp.bfloat16), "fsdp", split_axis=0, concat_axis=0, tiled=True)
    shard = jnp.sum(arrived_terms.astype(jnp.float32), axis=0)
    for flip in (2, 4):
        shard = shard + lax.ppermute(shard, "dom", [(d, d ^ flip) for d in range(dom_size)])
    other = lax.ppermute(shard, "dom", pair)
    low = jnp.where(core == 0, shard, other)
    high = jnp.where(core == 0, other, shard)
    first_total = jnp.concatenate([low[:half_rows, :hidden], high[:half_rows, :hidden]], axis=0)
    second_total = jnp.concatenate([low[half_rows:, :hidden], high[half_rows:, :hidden]], axis=0)
    bias_total = (shard + other)[0, hidden : hidden + hidden // fsdp_size]
    return (hidden_new, first_total, second_total, bias_total)


def solution(mesh):
    return jax.shard_map(
        on_device,
        mesh=mesh,
        in_specs=(
            P(("dom", "fsdp"), None, None),
            P("dom", "fsdp", None),
            P("dom", "fsdp", None),
            P("dom", None, None),
            P("dom", None),
            P(("dom", "fsdp"), None),
            P(("dom", "fsdp")),
            P(("dom", "fsdp"), None, None, None),
            P("fsdp", None),
            P("fsdp", None),
            P("fsdp"),
            P(("dom", "fsdp"), None, None),
        ),
        out_specs=(P(("dom", "fsdp"), None, None), P("fsdp", None), P("fsdp", None), P("fsdp")),
        check_vma=False,
    )
```

```python
import functools

import jax
import jax.numpy as jnp
from jax import lax
from jax.experimental import pallas as pl
from jax.experimental.pallas import tpu as pltpu
from jax.sharding import PartitionSpec as P


def gelu_tanh(inputs):
    return jax.nn.gelu(inputs, approximate=True)


def _agg_kernel(own_count, last_tile, src_ref, cnt_ref, live_ref, own_ref, pulled_ref, tile_ref, out_ref, acc_ref):
    v = pl.program_id(0)
    t = pl.program_id(1)

    @pl.when(t == 0)
    def _():
        acc_ref[...] = jnp.zeros_like(acc_ref)

    src = src_ref[v, t]
    tile_live = t < cnt_ref[v]
    own_ok = tile_live & (src < own_count)
    pull_ok = tile_live & (src >= own_count) & (live_ref[jnp.maximum(src - own_count, 0)] > 0)

    @pl.when(own_ok)
    def _():
        acc_ref[...] += jnp.dot(own_ref[0], tile_ref[0, 0], preferred_element_type=jnp.float32)

    @pl.when(pull_ok)
    def _():
        block = pulled_ref[0, :, 0]
        block = block.reshape(block.shape[0] * block.shape[1], block.shape[2])
        acc_ref[...] += jnp.dot(block, tile_ref[0, 0], preferred_element_type=jnp.float32)

    @pl.when(t == last_tile)
    def _():
        out_ref[0] = acc_ref[...].astype(out_ref.dtype)


def aggregate(own, pulled, tile_src, tile_count, slot_live, tile_values):
    nb, feat, blk = own.shape
    dom, fsdp, cap = pulled.shape[0], pulled.shape[1], pulled.shape[2]
    tiles = tile_src.shape[1]

    def eff(v, t, src_ref, cnt_ref):
        return jnp.minimum(t, cnt_ref[v] - 1)

    def own_map(v, t, src_ref, cnt_ref, live_ref):
        s = src_ref[v, eff(v, t, src_ref, cnt_ref)]
        return (jnp.clip(s, 0, nb - 1), 0, 0)

    def pulled_map(v, t, src_ref, cnt_ref, live_ref):
        s = jnp.clip(src_ref[v, eff(v, t, src_ref, cnt_ref)] - nb, 0, cap * dom - 1)
        return (s % dom, 0, s // dom, 0, 0)

    def tile_map(v, t, src_ref, cnt_ref, live_ref):
        return (v, eff(v, t, src_ref, cnt_ref), 0, 0)

    def out_map(v, t, src_ref, cnt_ref, live_ref):
        return (v, 0, 0)

    grid_spec = pltpu.PrefetchScalarGridSpec(
        num_scalar_prefetch=3,
        grid=(nb, tiles),
        in_specs=[
            pl.BlockSpec((1, feat, blk), own_map),
            pl.BlockSpec((1, fsdp, 1) + pulled.shape[3:], pulled_map),
            pl.BlockSpec((1, 1, blk, blk), tile_map),
        ],
        out_specs=pl.BlockSpec((1, feat, blk), out_map),
        scratch_shapes=[pltpu.VMEM((feat, blk), jnp.float32)],
    )
    flops = 2 * nb * tiles * feat * blk * blk
    return pl.pallas_call(
        functools.partial(_agg_kernel, nb, tiles - 1),
        grid_spec=grid_spec,
        out_shape=jax.ShapeDtypeStruct(own.shape, jnp.bfloat16),
        compiler_params=pltpu.CompilerParams(dimension_semantics=("arbitrary", "arbitrary")),
        cost_estimate=pl.CostEstimate(
            flops=flops, transcendentals=0, bytes_accessed=nb * tiles * (2 * feat * blk * 2 + blk * blk * 2) + own.size * 2
        ),
    )(tile_src, tile_count, slot_live, own, pulled, tile_values)


def _spread_kernel(own_count, src_ref, cnt_ref, back_ref, tile_ref, out_ref):
    v = pl.program_id(0)
    t = pl.program_id(1)

    @pl.when((v == 0) & (t == 0))
    def _():
        out_ref[...] = jnp.zeros_like(out_ref)

    src = src_ref[v, t]

    @pl.when((t < cnt_ref[v]) & (src < own_count))
    def _():
        term = lax.dot_general(
            back_ref[0], tile_ref[0, 0], (((1,), (1,)), ((), ())), preferred_element_type=jnp.float32
        )
        out_ref[src] = out_ref[src] + term


def spread_back(back_second, tile_src, tile_count, tile_values):
    nb, width, blk = back_second.shape
    tiles = tile_src.shape[1]

    def eff(v, t, cnt_ref):
        return jnp.minimum(t, cnt_ref[v] - 1)

    grid_spec = pltpu.PrefetchScalarGridSpec(
        num_scalar_prefetch=2,
        grid=(nb, tiles),
        in_specs=[
            pl.BlockSpec((1, width, blk), lambda v, t, s, c: (v, 0, 0)),
            pl.BlockSpec((1, 1, blk, blk), lambda v, t, s, c: (v, eff(v, t, c), 0, 0)),
        ],
        out_specs=pl.BlockSpec((nb, width, blk), lambda v, t, s, c: (0, 0, 0)),
    )
    return pl.pallas_call(
        functools.partial(_spread_kernel, nb),
        grid_spec=grid_spec,
        out_shape=jax.ShapeDtypeStruct(back_second.shape, jnp.float32),
        compiler_params=pltpu.CompilerParams(dimension_semantics=("arbitrary", "arbitrary")),
        cost_estimate=pl.CostEstimate(
            flops=2 * nb * tiles * width * blk * blk,
            transcendentals=0,
            bytes_accessed=back_second.size * 2 + nb * tiles * blk * blk * 2 + back_second.size * 4,
        ),
    )(tile_src, tile_count, back_second, tile_values)


def gather_rows(x, axis):
    n = lax.axis_size(axis)
    spread = lax.all_to_all(jnp.broadcast_to(x[None], (n,) + x.shape), axis, split_axis=0, concat_axis=0, tiled=True)
    return spread.reshape((n * x.shape[0],) + x.shape[1:])


def on_device(
    features,
    history_first,
    history_second,
    pull_list,
    pull_count,
    tile_src,
    tile_count,
    tile_values,
    w_first,
    w_second,
    bias_first,
    out_grad,
):
    dom_size = lax.axis_size("dom")
    fsdp_size = lax.axis_size("fsdp")
    me = lax.axis_index("dom") * fsdp_size + lax.axis_index("fsdp")
    rows, hidden = w_first.shape
    bias_cols = jnp.broadcast_to(bias_first[:, None], (rows, 128))
    packed = gather_rows(jnp.concatenate([w_first, w_second, bias_cols], axis=1), "fsdp")
    first_full = packed[:, :hidden]
    second_full = packed[:, hidden : 2 * hidden]
    bias_full = packed[:, 2 * hidden].astype(jnp.float32)

    chosen = pull_list[0]
    requesters, slot_cap = chosen.shape
    counts_all = lax.all_gather(pull_count, "dom", axis=0, tiled=True)
    counts_all, chosen = lax.optimization_barrier((counts_all, chosen))
    my_counts = lax.dynamic_index_in_dim(counts_all, me, axis=1, keepdims=False)
    slot_live = (lax.broadcasted_iota(jnp.int32, (slot_cap, dom_size), 0) < my_counts[None, :]).astype(jnp.int32)
    slot_live = slot_live.reshape(-1)

    block_len = features.shape[2]
    first_cols = history_first.shape[1]
    second_cols = history_second.shape[1]
    sent_first = jnp.take(history_first, chosen.reshape(-1), axis=0, mode="clip").reshape(requesters, slot_cap, first_cols, block_len)
    sent_second = jnp.take(history_second, chosen.reshape(-1), axis=0, mode="clip").reshape(requesters, slot_cap, second_cols, block_len)
    arrived_first = lax.all_to_all(sent_first, ("dom", "fsdp"), split_axis=0, concat_axis=0, tiled=True)
    arrived_second = lax.all_to_all(sent_second, ("dom", "fsdp"), split_axis=0, concat_axis=0, tiled=True)
    pulled_first = arrived_first.reshape(dom_size, fsdp_size, slot_cap, first_cols, block_len)
    pulled_second = arrived_second.reshape(dom_size, fsdp_size, slot_cap, second_cols, block_len)

    core = lax.axis_index("dom") % 2
    pair = [(d, d ^ 1) for d in range(dom_size)]
    partner_grad = lax.ppermute(out_grad, "dom", pair)

    back_second = jnp.einsum(
        "ab,vbn->van", second_full, out_grad, preferred_element_type=jnp.float32
    ).astype(jnp.bfloat16)
    back_hidden = spread_back(back_second, tile_src, tile_count, tile_values)

    def halves(x):
        split = x.reshape(x.shape[0], fsdp_size, 2, x.shape[1] // (2 * fsdp_size), x.shape[2])
        mine = lax.dynamic_index_in_dim(split, core, axis=2, keepdims=False)
        theirs = lax.dynamic_index_in_dim(split, 1 - core, axis=2, keepdims=False)
        return mine, theirs

    agg_first = aggregate(features, pulled_first, tile_src, tile_count, slot_live, tile_values)
    pre_act = (
        jnp.einsum("fh,vfn->vhn", first_full, agg_first, preferred_element_type=jnp.float32)
        + bias_full[None, :, None]
    )
    hidden_new = gelu_tanh(pre_act).astype(jnp.bfloat16)
    _, pullback = jax.vjp(gelu_tanh, pre_act)
    back_pre = pullback(back_hidden)[0].astype(jnp.bfloat16)
    bias_term = jnp.sum(back_pre.astype(jnp.float32), axis=(0, 2))
    first_mine, first_theirs = halves(agg_first)
    first_got, back_got = lax.ppermute((first_theirs, back_pre), "dom", pair)
    first_term = jnp.einsum(
        "vprn,vhn->prh", first_mine, back_pre, preferred_element_type=jnp.float32
    ) + jnp.einsum("vprn,vhn->prh", first_got, back_got, preferred_element_type=jnp.float32)

    half_rows = first_term.shape[1]
    lanes = 128
    agg_second = aggregate(hidden_new, pulled_second, tile_src, tile_count, slot_live, tile_values)
    second_mine, second_theirs = halves(agg_second)
    second_got = lax.ppermute(second_theirs, "dom", pair)
    second_term = jnp.einsum(
        "vprn,vbn->prb", second_mine, out_grad, preferred_element_type=jnp.float32
    ) + jnp.einsum("vprn,vbn->prb", second_got, partner_grad, preferred_element_type=jnp.float32)

    bias_cols = jnp.zeros((fsdp_size, 2 * half_rows, lanes), jnp.float32)
    bias_cols = bias_cols.at[:, 0, : hidden // fsdp_size].set(bias_term.reshape(fsdp_size, hidden // fsdp_size))
    packed_terms = jnp.concatenate([jnp.concatenate([first_term, second_term], axis=1), bias_cols], axis=2)
    arrived_terms = lax.all_to_all(packed_terms.astype(jnp.bfloat16), "fsdp", split_axis=0, concat_axis=0, tiled=True)
    shard = jnp.sum(arrived_terms.astype(jnp.float32), axis=0)
    for flip in (2, 4):
        shard = shard + lax.ppermute(shard, "dom", [(d, d ^ flip) for d in range(dom_size)])
    other = lax.ppermute(shard, "dom", pair)
    low = jnp.where(core == 0, shard, other)
    high = jnp.where(core == 0, other, shard)
    first_total = jnp.concatenate([low[:half_rows, :hidden], high[:half_rows, :hidden]], axis=0)
    second_total = jnp.concatenate([low[half_rows:, :hidden], high[half_rows:, :hidden]], axis=0)
    bias_total = (shard + other)[0, hidden : hidden + hidden // fsdp_size]
    return (hidden_new, first_total, second_total, bias_total)


def solution(mesh):
    return jax.shard_map(
        on_device,
        mesh=mesh,
        in_specs=(
            P(("dom", "fsdp"), None, None),
            P("dom", "fsdp", None),
            P("dom", "fsdp", None),
            P("dom", None, None),
            P("dom", None),
            P(("dom", "fsdp"), None),
            P(("dom", "fsdp")),
            P(("dom", "fsdp"), None, None, None),
            P("fsdp", None),
            P("fsdp", None),
            P("fsdp"),
            P(("dom", "fsdp"), None, None),
        ),
        out_specs=(P(("dom", "fsdp"), None, None), P("fsdp", None), P("fsdp", None), P("fsdp")),
        check_vma=False,
    )
```

```python
import functools

import jax
import jax.numpy as jnp
from jax import lax
from jax.experimental import pallas as pl
from jax.experimental.pallas import tpu as pltpu
from jax.sharding import PartitionSpec as P


def gelu_tanh(inputs):
    return jax.nn.gelu(inputs, approximate=True)


def _agg_kernel(own_count, last_tile, src_ref, cnt_ref, live_ref, own_ref, pulled_ref, tile_ref, out_ref, acc_ref):
    v = pl.program_id(0)
    t = pl.program_id(1)

    @pl.when(t == 0)
    def _():
        acc_ref[...] = jnp.zeros_like(acc_ref)

    src = src_ref[v, t]
    tile_live = t < cnt_ref[v]
    own_ok = tile_live & (src < own_count)
    pull_ok = tile_live & (src >= own_count) & (live_ref[jnp.maximum(src - own_count, 0)] > 0)

    @pl.when(own_ok)
    def _():
        acc_ref[...] += jnp.dot(own_ref[0], tile_ref[0, 0], preferred_element_type=jnp.float32)

    @pl.when(pull_ok)
    def _():
        block = pulled_ref[0, :, 0]
        block = block.reshape(block.shape[0] * block.shape[1], block.shape[2])
        acc_ref[...] += jnp.dot(block, tile_ref[0, 0], preferred_element_type=jnp.float32)

    @pl.when(t == last_tile)
    def _():
        out_ref[0] = acc_ref[...].astype(out_ref.dtype)


def aggregate(own, pulled, tile_src, tile_count, slot_live, tile_values):
    nb, feat, blk = own.shape
    dom, fsdp, cap = pulled.shape[0], pulled.shape[1], pulled.shape[2]
    tiles = tile_src.shape[1]

    def eff(v, t, src_ref, cnt_ref):
        return jnp.minimum(t, cnt_ref[v] - 1)

    def own_map(v, t, src_ref, cnt_ref, live_ref):
        s = src_ref[v, eff(v, t, src_ref, cnt_ref)]
        return (jnp.clip(s, 0, nb - 1), 0, 0)

    def pulled_map(v, t, src_ref, cnt_ref, live_ref):
        s = jnp.clip(src_ref[v, eff(v, t, src_ref, cnt_ref)] - nb, 0, cap * dom - 1)
        return (s % dom, 0, s // dom, 0, 0)

    def tile_map(v, t, src_ref, cnt_ref, live_ref):
        return (v, eff(v, t, src_ref, cnt_ref), 0, 0)

    def out_map(v, t, src_ref, cnt_ref, live_ref):
        return (v, 0, 0)

    grid_spec = pltpu.PrefetchScalarGridSpec(
        num_scalar_prefetch=3,
        grid=(nb, tiles),
        in_specs=[
            pl.BlockSpec((1, feat, blk), own_map),
            pl.BlockSpec((1, fsdp, 1) + pulled.shape[3:], pulled_map),
            pl.BlockSpec((1, 1, blk, blk), tile_map),
        ],
        out_specs=pl.BlockSpec((1, feat, blk), out_map),
        scratch_shapes=[pltpu.VMEM((feat, blk), jnp.float32)],
    )
    flops = 2 * nb * tiles * feat * blk * blk
    return pl.pallas_call(
        functools.partial(_agg_kernel, nb, tiles - 1),
        grid_spec=grid_spec,
        out_shape=jax.ShapeDtypeStruct(own.shape, jnp.bfloat16),
        compiler_params=pltpu.CompilerParams(dimension_semantics=("arbitrary", "arbitrary")),
        cost_estimate=pl.CostEstimate(
            flops=flops, transcendentals=0, bytes_accessed=nb * tiles * (2 * feat * blk * 2 + blk * blk * 2) + own.size * 2
        ),
    )(tile_src, tile_count, slot_live, own, pulled, tile_values)


def _spread_kernel(own_count, src_ref, cnt_ref, back_ref, tile_ref, out_ref):
    v = pl.program_id(0)
    t = pl.program_id(1)

    @pl.when((v == 0) & (t == 0))
    def _():
        out_ref[...] = jnp.zeros_like(out_ref)

    src = src_ref[v, t]

    @pl.when((t < cnt_ref[v]) & (src < own_count))
    def _():
        term = lax.dot_general(
            back_ref[0], tile_ref[0, 0], (((1,), (1,)), ((), ())), preferred_element_type=jnp.float32
        )
        out_ref[src] = out_ref[src] + term


def spread_back(back_second, tile_src, tile_count, tile_values):
    nb, width, blk = back_second.shape
    tiles = tile_src.shape[1]

    def eff(v, t, cnt_ref):
        return jnp.minimum(t, cnt_ref[v] - 1)

    grid_spec = pltpu.PrefetchScalarGridSpec(
        num_scalar_prefetch=2,
        grid=(nb, tiles),
        in_specs=[
            pl.BlockSpec((1, width, blk), lambda v, t, s, c: (v, 0, 0)),
            pl.BlockSpec((1, 1, blk, blk), lambda v, t, s, c: (v, eff(v, t, c), 0, 0)),
        ],
        out_specs=pl.BlockSpec((nb, width, blk), lambda v, t, s, c: (0, 0, 0)),
    )
    return pl.pallas_call(
        functools.partial(_spread_kernel, nb),
        grid_spec=grid_spec,
        out_shape=jax.ShapeDtypeStruct(back_second.shape, jnp.float32),
        compiler_params=pltpu.CompilerParams(dimension_semantics=("arbitrary", "arbitrary")),
        cost_estimate=pl.CostEstimate(
            flops=2 * nb * tiles * width * blk * blk,
            transcendentals=0,
            bytes_accessed=back_second.size * 2 + nb * tiles * blk * blk * 2 + back_second.size * 4,
        ),
    )(tile_src, tile_count, back_second, tile_values)


def gather_rows(x, axis):
    n = lax.axis_size(axis)
    spread = lax.all_to_all(jnp.broadcast_to(x[None], (n,) + x.shape), axis, split_axis=0, concat_axis=0, tiled=True)
    return spread.reshape((n * x.shape[0],) + x.shape[1:])


def on_device(
    features,
    history_first,
    history_second,
    pull_list,
    pull_count,
    tile_src,
    tile_count,
    tile_values,
    w_first,
    w_second,
    bias_first,
    out_grad,
):
    dom_size = lax.axis_size("dom")
    fsdp_size = lax.axis_size("fsdp")
    me = lax.axis_index("dom") * fsdp_size + lax.axis_index("fsdp")
    rows, hidden = w_first.shape
    bias_cols = jnp.broadcast_to(bias_first[:, None], (rows, 128))
    packed = lax.all_gather(jnp.concatenate([w_first, w_second, bias_cols], axis=1), "fsdp", axis=0, tiled=True)
    first_full = packed[:, :hidden]
    second_full = packed[:, hidden : 2 * hidden]
    bias_full = packed[:, 2 * hidden].astype(jnp.float32)

    chosen = pull_list[0]
    requesters, slot_cap = chosen.shape
    counts_all = lax.all_gather(pull_count, "dom", axis=0, tiled=True)
    counts_all, chosen = lax.optimization_barrier((counts_all, chosen))
    my_counts = lax.dynamic_index_in_dim(counts_all, me, axis=1, keepdims=False)
    slot_live = (lax.broadcasted_iota(jnp.int32, (slot_cap, dom_size), 0) < my_counts[None, :]).astype(jnp.int32)
    slot_live = slot_live.reshape(-1)

    block_len = features.shape[2]
    first_cols = history_first.shape[1]
    second_cols = history_second.shape[1]
    sent_first = jnp.take(history_first, chosen.reshape(-1), axis=0, mode="clip").reshape(requesters, slot_cap, first_cols, block_len)
    sent_second = jnp.take(history_second, chosen.reshape(-1), axis=0, mode="clip").reshape(requesters, slot_cap, second_cols, block_len)
    arrived_first = lax.all_to_all(sent_first, ("dom", "fsdp"), split_axis=0, concat_axis=0, tiled=True)
    arrived_second = lax.all_to_all(sent_second, ("dom", "fsdp"), split_axis=0, concat_axis=0, tiled=True)
    pulled_first = arrived_first.reshape(dom_size, fsdp_size, slot_cap, first_cols, block_len)
    pulled_second = arrived_second.reshape(dom_size, fsdp_size, slot_cap, second_cols, block_len)

    core = lax.axis_index("dom") % 2
    pair = [(d, d ^ 1) for d in range(dom_size)]
    partner_grad = lax.ppermute(out_grad, "dom", pair)

    back_second = jnp.einsum(
        "ab,vbn->van", second_full, out_grad, preferred_element_type=jnp.float32
    ).astype(jnp.bfloat16)
    back_hidden = spread_back(back_second, tile_src, tile_count, tile_values)

    def halves(x):
        split = x.reshape(x.shape[0], fsdp_size, 2, x.shape[1] // (2 * fsdp_size), x.shape[2])
        mine = lax.dynamic_index_in_dim(split, core, axis=2, keepdims=False)
        theirs = lax.dynamic_index_in_dim(split, 1 - core, axis=2, keepdims=False)
        return mine, theirs

    agg_first = aggregate(features, pulled_first, tile_src, tile_count, slot_live, tile_values)
    pre_act = (
        jnp.einsum("fh,vfn->vhn", first_full, agg_first, preferred_element_type=jnp.float32)
        + bias_full[None, :, None]
    )
    hidden_new = gelu_tanh(pre_act).astype(jnp.bfloat16)
    _, pullback = jax.vjp(gelu_tanh, pre_act)
    back_pre = pullback(back_hidden)[0].astype(jnp.bfloat16)
    bias_term = jnp.sum(back_pre.astype(jnp.float32), axis=(0, 2))
    first_mine, first_theirs = halves(agg_first)
    first_got, back_got = lax.ppermute((first_theirs, back_pre), "dom", pair)
    first_term = jnp.einsum(
        "vprn,vhn->prh", first_mine, back_pre, preferred_element_type=jnp.float32
    ) + jnp.einsum("vprn,vhn->prh", first_got, back_got, preferred_element_type=jnp.float32)

    half_rows = first_term.shape[1]
    lanes = 128
    agg_second = aggregate(hidden_new, pulled_second, tile_src, tile_count, slot_live, tile_values)
    second_mine, second_theirs = halves(agg_second)
    second_got = lax.ppermute(second_theirs, "dom", pair)
    second_term = jnp.einsum(
        "vprn,vbn->prb", second_mine, out_grad, preferred_element_type=jnp.float32
    ) + jnp.einsum("vprn,vbn->prb", second_got, partner_grad, preferred_element_type=jnp.float32)

    bias_cols = jnp.zeros((fsdp_size, 2 * half_rows, lanes), jnp.float32)
    bias_cols = bias_cols.at[:, 0, : hidden // fsdp_size].set(bias_term.reshape(fsdp_size, hidden // fsdp_size))
    packed_terms = jnp.concatenate([jnp.concatenate([first_term, second_term], axis=1), bias_cols], axis=2)
    arrived_terms = lax.all_to_all(packed_terms.astype(jnp.bfloat16), "fsdp", split_axis=0, concat_axis=0, tiled=True)
    shard = jnp.sum(arrived_terms.astype(jnp.float32), axis=0)
    for flip in (2, 4):
        shard = shard + lax.ppermute(shard, "dom", [(d, d ^ flip) for d in range(dom_size)])
    other = lax.ppermute(shard, "dom", pair)
    low = jnp.where(core == 0, shard, other)
    high = jnp.where(core == 0, other, shard)
    first_total = jnp.concatenate([low[:half_rows, :hidden], high[:half_rows, :hidden]], axis=0)
    second_total = jnp.concatenate([low[half_rows:, :hidden], high[half_rows:, :hidden]], axis=0)
    bias_total = (shard + other)[0, hidden : hidden + hidden // fsdp_size]
    return (hidden_new, first_total, second_total, bias_total)


def solution(mesh):
    return jax.shard_map(
        on_device,
        mesh=mesh,
        in_specs=(
            P(("dom", "fsdp"), None, None),
            P("dom", "fsdp", None),
            P("dom", "fsdp", None),
            P("dom", None, None),
            P("dom", None),
            P(("dom", "fsdp"), None),
            P(("dom", "fsdp")),
            P(("dom", "fsdp"), None, None, None),
            P("fsdp", None),
            P("fsdp", None),
            P("fsdp"),
            P(("dom", "fsdp"), None, None),
        ),
        out_specs=(P(("dom", "fsdp"), None, None), P("fsdp", None), P("fsdp", None), P("fsdp")),
        check_vma=False,
    )
```

```python
import functools

import jax
import jax.numpy as jnp
from jax import lax
from jax.experimental import pallas as pl
from jax.experimental.pallas import tpu as pltpu
from jax.sharding import PartitionSpec as P


def gelu_tanh(inputs):
    return jax.nn.gelu(inputs, approximate=True)


def _agg_kernel(own_count, last_tile, src_ref, cnt_ref, live_ref, own_ref, pulled_ref, tile_ref, out_ref, acc_ref):
    v = pl.program_id(0)
    t = pl.program_id(1)

    @pl.when(t == 0)
    def _():
        acc_ref[...] = jnp.zeros_like(acc_ref)

    src = src_ref[v, t]
    tile_live = t < cnt_ref[v]
    own_ok = tile_live & (src < own_count)
    pull_ok = tile_live & (src >= own_count) & (live_ref[jnp.maximum(src - own_count, 0)] > 0)

    @pl.when(own_ok)
    def _():
        acc_ref[...] += jnp.dot(own_ref[0], tile_ref[0, 0], preferred_element_type=jnp.float32)

    @pl.when(pull_ok)
    def _():
        block = pulled_ref[0, :, 0]
        block = block.reshape(block.shape[0] * block.shape[1], block.shape[2])
        acc_ref[...] += jnp.dot(block, tile_ref[0, 0], preferred_element_type=jnp.float32)

    @pl.when(t == last_tile)
    def _():
        out_ref[0] = acc_ref[...].astype(out_ref.dtype)


def aggregate(own, pulled, tile_src, tile_count, slot_live, tile_values):
    nb, feat, blk = own.shape
    dom, fsdp, cap = pulled.shape[0], pulled.shape[1], pulled.shape[2]
    tiles = tile_src.shape[1]

    def eff(v, t, src_ref, cnt_ref):
        return jnp.minimum(t, cnt_ref[v] - 1)

    def own_map(v, t, src_ref, cnt_ref, live_ref):
        s = src_ref[v, eff(v, t, src_ref, cnt_ref)]
        return (jnp.clip(s, 0, nb - 1), 0, 0)

    def pulled_map(v, t, src_ref, cnt_ref, live_ref):
        s = jnp.clip(src_ref[v, eff(v, t, src_ref, cnt_ref)] - nb, 0, cap * dom - 1)
        return (s % dom, 0, s // dom, 0, 0)

    def tile_map(v, t, src_ref, cnt_ref, live_ref):
        return (v, eff(v, t, src_ref, cnt_ref), 0, 0)

    def out_map(v, t, src_ref, cnt_ref, live_ref):
        return (v, 0, 0)

    grid_spec = pltpu.PrefetchScalarGridSpec(
        num_scalar_prefetch=3,
        grid=(nb, tiles),
        in_specs=[
            pl.BlockSpec((1, feat, blk), own_map),
            pl.BlockSpec((1, fsdp, 1) + pulled.shape[3:], pulled_map),
            pl.BlockSpec((1, 1, blk, blk), tile_map),
        ],
        out_specs=pl.BlockSpec((1, feat, blk), out_map),
        scratch_shapes=[pltpu.VMEM((feat, blk), jnp.float32)],
    )
    flops = 2 * nb * tiles * feat * blk * blk
    return pl.pallas_call(
        functools.partial(_agg_kernel, nb, tiles - 1),
        grid_spec=grid_spec,
        out_shape=jax.ShapeDtypeStruct(own.shape, jnp.bfloat16),
        compiler_params=pltpu.CompilerParams(dimension_semantics=("arbitrary", "arbitrary")),
        cost_estimate=pl.CostEstimate(
            flops=flops, transcendentals=0, bytes_accessed=nb * tiles * (2 * feat * blk * 2 + blk * blk * 2) + own.size * 2
        ),
    )(tile_src, tile_count, slot_live, own, pulled, tile_values)


def _spread_kernel(own_count, src_ref, cnt_ref, back_ref, tile_ref, out_ref):
    v = pl.program_id(0)
    t = pl.program_id(1)

    @pl.when((v == 0) & (t == 0))
    def _():
        out_ref[...] = jnp.zeros_like(out_ref)

    src = src_ref[v, t]

    @pl.when((t < cnt_ref[v]) & (src < own_count))
    def _():
        term = lax.dot_general(
            back_ref[0], tile_ref[0, 0], (((1,), (1,)), ((), ())), preferred_element_type=jnp.float32
        )
        out_ref[src] = out_ref[src] + term


def spread_back(back_second, tile_src, tile_count, tile_values):
    nb, width, blk = back_second.shape
    tiles = tile_src.shape[1]

    def eff(v, t, cnt_ref):
        return jnp.minimum(t, cnt_ref[v] - 1)

    grid_spec = pltpu.PrefetchScalarGridSpec(
        num_scalar_prefetch=2,
        grid=(nb, tiles),
        in_specs=[
            pl.BlockSpec((1, width, blk), lambda v, t, s, c: (v, 0, 0)),
            pl.BlockSpec((1, 1, blk, blk), lambda v, t, s, c: (v, eff(v, t, c), 0, 0)),
        ],
        out_specs=pl.BlockSpec((nb, width, blk), lambda v, t, s, c: (0, 0, 0)),
    )
    return pl.pallas_call(
        functools.partial(_spread_kernel, nb),
        grid_spec=grid_spec,
        out_shape=jax.ShapeDtypeStruct(back_second.shape, jnp.float32),
        compiler_params=pltpu.CompilerParams(dimension_semantics=("arbitrary", "arbitrary")),
        cost_estimate=pl.CostEstimate(
            flops=2 * nb * tiles * width * blk * blk,
            transcendentals=0,
            bytes_accessed=back_second.size * 2 + nb * tiles * blk * blk * 2 + back_second.size * 4,
        ),
    )(tile_src, tile_count, back_second, tile_values)


def gather_rows(x, axis):
    n = lax.axis_size(axis)
    spread = lax.all_to_all(jnp.broadcast_to(x[None], (n,) + x.shape), axis, split_axis=0, concat_axis=0, tiled=True)
    return spread.reshape((n * x.shape[0],) + x.shape[1:])


def on_device(
    features,
    history_first,
    history_second,
    pull_list,
    pull_count,
    tile_src,
    tile_count,
    tile_values,
    w_first,
    w_second,
    bias_first,
    out_grad,
):
    dom_size = lax.axis_size("dom")
    fsdp_size = lax.axis_size("fsdp")
    me = lax.axis_index("dom") * fsdp_size + lax.axis_index("fsdp")
    rows, hidden = w_first.shape
    core = lax.axis_index("dom") % 2
    pair = [(d, d ^ 1) for d in range(dom_size)]
    bias_cols = jnp.broadcast_to(bias_first[:, None], (rows, 128))
    own_weight = jnp.where(core == 0, w_first, w_second)
    mine = lax.all_gather(jnp.concatenate([own_weight, bias_cols], axis=1), "fsdp", axis=0, tiled=True)
    theirs = lax.ppermute(mine[:, :hidden], "dom", pair)
    first_full = jnp.where(core == 0, mine[:, :hidden], theirs)
    second_full = jnp.where(core == 0, theirs, mine[:, :hidden])
    bias_full = mine[:, hidden].astype(jnp.float32)

    chosen = pull_list[0]
    requesters, slot_cap = chosen.shape
    counts_all = lax.all_gather(pull_count, "dom", axis=0, tiled=True)
    counts_all, chosen = lax.optimization_barrier((counts_all, chosen))
    my_counts = lax.dynamic_index_in_dim(counts_all, me, axis=1, keepdims=False)
    slot_live = (lax.broadcasted_iota(jnp.int32, (slot_cap, dom_size), 0) < my_counts[None, :]).astype(jnp.int32)
    slot_live = slot_live.reshape(-1)

    block_len = features.shape[2]
    first_cols = history_first.shape[1]
    second_cols = history_second.shape[1]
    sent_first = jnp.take(history_first, chosen.reshape(-1), axis=0, mode="clip").reshape(requesters, slot_cap, first_cols, block_len)
    sent_second = jnp.take(history_second, chosen.reshape(-1), axis=0, mode="clip").reshape(requesters, slot_cap, second_cols, block_len)
    arrived_first = lax.all_to_all(sent_first, ("dom", "fsdp"), split_axis=0, concat_axis=0, tiled=True)
    arrived_second = lax.all_to_all(sent_second, ("dom", "fsdp"), split_axis=0, concat_axis=0, tiled=True)
    pulled_first = arrived_first.reshape(dom_size, fsdp_size, slot_cap, first_cols, block_len)
    pulled_second = arrived_second.reshape(dom_size, fsdp_size, slot_cap, second_cols, block_len)

    partner_grad = lax.ppermute(out_grad, "dom", pair)

    back_second = jnp.einsum(
        "ab,vbn->van", second_full, out_grad, preferred_element_type=jnp.float32
    ).astype(jnp.bfloat16)
    back_hidden = spread_back(back_second, tile_src, tile_count, tile_values)

    def halves(x):
        split = x.reshape(x.shape[0], fsdp_size, 2, x.shape[1] // (2 * fsdp_size), x.shape[2])
        mine = lax.dynamic_index_in_dim(split, core, axis=2, keepdims=False)
        theirs = lax.dynamic_index_in_dim(split, 1 - core, axis=2, keepdims=False)
        return mine, theirs

    agg_first = aggregate(features, pulled_first, tile_src, tile_count, slot_live, tile_values)
    pre_act = (
        jnp.einsum("fh,vfn->vhn", first_full, agg_first, preferred_element_type=jnp.float32)
        + bias_full[None, :, None]
    )
    hidden_new = gelu_tanh(pre_act).astype(jnp.bfloat16)
    _, pullback = jax.vjp(gelu_tanh, pre_act)
    back_pre = pullback(back_hidden)[0].astype(jnp.bfloat16)
    bias_term = jnp.sum(back_pre.astype(jnp.float32), axis=(0, 2))
    first_mine, first_theirs = halves(agg_first)
    first_got, back_got = lax.ppermute((first_theirs, back_pre), "dom", pair)
    first_term = jnp.einsum(
        "vprn,vhn->prh", first_mine, back_pre, preferred_element_type=jnp.float32
    ) + jnp.einsum("vprn,vhn->prh", first_got, back_got, preferred_element_type=jnp.float32)

    half_rows = first_term.shape[1]
    lanes = 128
    agg_second = aggregate(hidden_new, pulled_second, tile_src, tile_count, slot_live, tile_values)
    second_mine, second_theirs = halves(agg_second)
    second_got = lax.ppermute(second_theirs, "dom", pair)
    second_term = jnp.einsum(
        "vprn,vbn->prb", second_mine, out_grad, preferred_element_type=jnp.float32
    ) + jnp.einsum("vprn,vbn->prb", second_got, partner_grad, preferred_element_type=jnp.float32)

    bias_cols = jnp.zeros((fsdp_size, 2 * half_rows, lanes), jnp.float32)
    bias_cols = bias_cols.at[:, 0, : hidden // fsdp_size].set(bias_term.reshape(fsdp_size, hidden // fsdp_size))
    packed_terms = jnp.concatenate([jnp.concatenate([first_term, second_term], axis=1), bias_cols], axis=2)
    arrived_terms = lax.all_to_all(packed_terms.astype(jnp.bfloat16), "fsdp", split_axis=0, concat_axis=0, tiled=True)
    shard = jnp.sum(arrived_terms.astype(jnp.float32), axis=0)
    for flip in (2, 4):
        shard = shard + lax.ppermute(shard, "dom", [(d, d ^ flip) for d in range(dom_size)])
    other = lax.ppermute(shard, "dom", pair)
    low = jnp.where(core == 0, shard, other)
    high = jnp.where(core == 0, other, shard)
    first_total = jnp.concatenate([low[:half_rows, :hidden], high[:half_rows, :hidden]], axis=0)
    second_total = jnp.concatenate([low[half_rows:, :hidden], high[half_rows:, :hidden]], axis=0)
    bias_total = (shard + other)[0, hidden : hidden + hidden // fsdp_size]
    return (hidden_new, first_total, second_total, bias_total)


def solution(mesh):
    return jax.shard_map(
        on_device,
        mesh=mesh,
        in_specs=(
            P(("dom", "fsdp"), None, None),
            P("dom", "fsdp", None),
            P("dom", "fsdp", None),
            P("dom", None, None),
            P("dom", None),
            P(("dom", "fsdp"), None),
            P(("dom", "fsdp")),
            P(("dom", "fsdp"), None, None, None),
            P("fsdp", None),
            P("fsdp", None),
            P("fsdp"),
            P(("dom", "fsdp"), None, None),
        ),
        out_specs=(P(("dom", "fsdp"), None, None), P("fsdp", None), P("fsdp", None), P("fsdp")),
        check_vma=False,
    )
```

```python
import functools

import jax
import jax.numpy as jnp
from jax import lax
from jax.experimental import pallas as pl
from jax.experimental.pallas import tpu as pltpu
from jax.sharding import PartitionSpec as P


def gelu_tanh(inputs):
    return jax.nn.gelu(inputs, approximate=True)


def _agg_kernel(own_count, last_tile, src_ref, cnt_ref, live_ref, own_ref, pulled_ref, tile_ref, out_ref, acc_ref):
    v = pl.program_id(0)
    t = pl.program_id(1)

    @pl.when(t == 0)
    def _():
        acc_ref[...] = jnp.zeros_like(acc_ref)

    src = src_ref[v, t]
    tile_live = t < cnt_ref[v]
    own_ok = tile_live & (src < own_count)
    pull_ok = tile_live & (src >= own_count) & (live_ref[jnp.maximum(src - own_count, 0)] > 0)

    @pl.when(own_ok)
    def _():
        acc_ref[...] += jnp.dot(own_ref[0], tile_ref[0, 0], preferred_element_type=jnp.float32)

    @pl.when(pull_ok)
    def _():
        block = pulled_ref[0, :, 0]
        block = block.reshape(block.shape[0] * block.shape[1], block.shape[2])
        acc_ref[...] += jnp.dot(block, tile_ref[0, 0], preferred_element_type=jnp.float32)

    @pl.when(t == last_tile)
    def _():
        out_ref[0] = acc_ref[...].astype(out_ref.dtype)


def aggregate(own, pulled, tile_src, tile_count, slot_live, tile_values):
    nb, feat, blk = own.shape
    dom, fsdp, cap = pulled.shape[0], pulled.shape[1], pulled.shape[2]
    tiles = tile_src.shape[1]

    def eff(v, t, src_ref, cnt_ref):
        return jnp.minimum(t, cnt_ref[v] - 1)

    def own_map(v, t, src_ref, cnt_ref, live_ref):
        s = src_ref[v, eff(v, t, src_ref, cnt_ref)]
        return (jnp.clip(s, 0, nb - 1), 0, 0)

    def pulled_map(v, t, src_ref, cnt_ref, live_ref):
        s = jnp.clip(src_ref[v, eff(v, t, src_ref, cnt_ref)] - nb, 0, cap * dom - 1)
        return (s % dom, 0, s // dom, 0, 0)

    def tile_map(v, t, src_ref, cnt_ref, live_ref):
        return (v, eff(v, t, src_ref, cnt_ref), 0, 0)

    def out_map(v, t, src_ref, cnt_ref, live_ref):
        return (v, 0, 0)

    grid_spec = pltpu.PrefetchScalarGridSpec(
        num_scalar_prefetch=3,
        grid=(nb, tiles),
        in_specs=[
            pl.BlockSpec((1, feat, blk), own_map),
            pl.BlockSpec((1, fsdp, 1) + pulled.shape[3:], pulled_map),
            pl.BlockSpec((1, 1, blk, blk), tile_map),
        ],
        out_specs=pl.BlockSpec((1, feat, blk), out_map),
        scratch_shapes=[pltpu.VMEM((feat, blk), jnp.float32)],
    )
    flops = 2 * nb * tiles * feat * blk * blk
    return pl.pallas_call(
        functools.partial(_agg_kernel, nb, tiles - 1),
        grid_spec=grid_spec,
        out_shape=jax.ShapeDtypeStruct(own.shape, jnp.bfloat16),
        compiler_params=pltpu.CompilerParams(dimension_semantics=("arbitrary", "arbitrary")),
        cost_estimate=pl.CostEstimate(
            flops=flops, transcendentals=0, bytes_accessed=nb * tiles * (2 * feat * blk * 2 + blk * blk * 2) + own.size * 2
        ),
    )(tile_src, tile_count, slot_live, own, pulled, tile_values)


def _spread_kernel(own_count, src_ref, cnt_ref, back_ref, tile_ref, out_ref):
    v = pl.program_id(0)
    t = pl.program_id(1)

    @pl.when((v == 0) & (t == 0))
    def _():
        out_ref[...] = jnp.zeros_like(out_ref)

    src = src_ref[v, t]

    @pl.when((t < cnt_ref[v]) & (src < own_count))
    def _():
        term = lax.dot_general(
            back_ref[0], tile_ref[0, 0], (((1,), (1,)), ((), ())), preferred_element_type=jnp.float32
        )
        out_ref[src] = out_ref[src] + term


def spread_back(back_second, tile_src, tile_count, tile_values):
    nb, width, blk = back_second.shape
    tiles = tile_src.shape[1]

    def eff(v, t, cnt_ref):
        return jnp.minimum(t, cnt_ref[v] - 1)

    grid_spec = pltpu.PrefetchScalarGridSpec(
        num_scalar_prefetch=2,
        grid=(nb, tiles),
        in_specs=[
            pl.BlockSpec((1, width, blk), lambda v, t, s, c: (v, 0, 0)),
            pl.BlockSpec((1, 1, blk, blk), lambda v, t, s, c: (v, eff(v, t, c), 0, 0)),
        ],
        out_specs=pl.BlockSpec((nb, width, blk), lambda v, t, s, c: (0, 0, 0)),
    )
    return pl.pallas_call(
        functools.partial(_spread_kernel, nb),
        grid_spec=grid_spec,
        out_shape=jax.ShapeDtypeStruct(back_second.shape, jnp.float32),
        compiler_params=pltpu.CompilerParams(dimension_semantics=("arbitrary", "arbitrary")),
        cost_estimate=pl.CostEstimate(
            flops=2 * nb * tiles * width * blk * blk,
            transcendentals=0,
            bytes_accessed=back_second.size * 2 + nb * tiles * blk * blk * 2 + back_second.size * 4,
        ),
    )(tile_src, tile_count, back_second, tile_values)


def gather_rows(x, axis):
    n = lax.axis_size(axis)
    spread = lax.all_to_all(jnp.broadcast_to(x[None], (n,) + x.shape), axis, split_axis=0, concat_axis=0, tiled=True)
    return spread.reshape((n * x.shape[0],) + x.shape[1:])


def on_device(
    features,
    history_first,
    history_second,
    pull_list,
    pull_count,
    tile_src,
    tile_count,
    tile_values,
    w_first,
    w_second,
    bias_first,
    out_grad,
):
    dom_size = lax.axis_size("dom")
    fsdp_size = lax.axis_size("fsdp")
    me = lax.axis_index("dom") * fsdp_size + lax.axis_index("fsdp")
    rows, hidden = w_first.shape
    bias_cols = jnp.broadcast_to(bias_first[:, None], (rows, 128))
    packed = lax.all_gather(jnp.concatenate([w_first, w_second, bias_cols], axis=1), "fsdp", axis=0, tiled=True)
    first_full = packed[:, :hidden]
    second_full = packed[:, hidden : 2 * hidden]
    bias_full = packed[:, 2 * hidden].astype(jnp.float32)

    chosen = pull_list[0]
    requesters, slot_cap = chosen.shape
    counts_all = pull_count
    for flip in (1, 2, 4):
        other = lax.ppermute(counts_all, "dom", [(d, d ^ flip) for d in range(dom_size)])
        low_half = (lax.axis_index("dom") & flip) == 0
        counts_all = jnp.where(
            low_half, jnp.concatenate([counts_all, other], 0), jnp.concatenate([other, counts_all], 0)
        )
    my_counts = lax.dynamic_index_in_dim(counts_all, me, axis=1, keepdims=False)
    slot_live = (lax.broadcasted_iota(jnp.int32, (slot_cap, dom_size), 0) < my_counts[None, :]).astype(jnp.int32)
    slot_live = slot_live.reshape(-1)

    block_len = features.shape[2]
    first_cols = history_first.shape[1]
    second_cols = history_second.shape[1]
    sent_first = jnp.take(history_first, chosen.reshape(-1), axis=0, mode="clip").reshape(requesters, slot_cap, first_cols, block_len)
    sent_second = jnp.take(history_second, chosen.reshape(-1), axis=0, mode="clip").reshape(requesters, slot_cap, second_cols, block_len)
    arrived_first = lax.all_to_all(sent_first, ("dom", "fsdp"), split_axis=0, concat_axis=0, tiled=True)
    arrived_second = lax.all_to_all(sent_second, ("dom", "fsdp"), split_axis=0, concat_axis=0, tiled=True)
    pulled_first = arrived_first.reshape(dom_size, fsdp_size, slot_cap, first_cols, block_len)
    pulled_second = arrived_second.reshape(dom_size, fsdp_size, slot_cap, second_cols, block_len)

    core = lax.axis_index("dom") % 2
    pair = [(d, d ^ 1) for d in range(dom_size)]
    partner_grad = lax.ppermute(out_grad, "dom", pair)

    back_second = jnp.einsum(
        "ab,vbn->van", second_full, out_grad, preferred_element_type=jnp.float32
    ).astype(jnp.bfloat16)
    back_hidden = spread_back(back_second, tile_src, tile_count, tile_values)

    def halves(x):
        split = x.reshape(x.shape[0], fsdp_size, 2, x.shape[1] // (2 * fsdp_size), x.shape[2])
        mine = lax.dynamic_index_in_dim(split, core, axis=2, keepdims=False)
        theirs = lax.dynamic_index_in_dim(split, 1 - core, axis=2, keepdims=False)
        return mine, theirs

    agg_first = aggregate(features, pulled_first, tile_src, tile_count, slot_live, tile_values)
    pre_act = (
        jnp.einsum("fh,vfn->vhn", first_full, agg_first, preferred_element_type=jnp.float32)
        + bias_full[None, :, None]
    )
    hidden_new = gelu_tanh(pre_act).astype(jnp.bfloat16)
    _, pullback = jax.vjp(gelu_tanh, pre_act)
    back_pre = pullback(back_hidden)[0].astype(jnp.bfloat16)
    bias_term = jnp.sum(back_pre.astype(jnp.float32), axis=(0, 2))
    first_mine, first_theirs = halves(agg_first)
    first_got, back_got = lax.ppermute((first_theirs, back_pre), "dom", pair)
    first_term = jnp.einsum(
        "vprn,vhn->prh", first_mine, back_pre, preferred_element_type=jnp.float32
    ) + jnp.einsum("vprn,vhn->prh", first_got, back_got, preferred_element_type=jnp.float32)

    half_rows = first_term.shape[1]
    lanes = 128
    agg_second = aggregate(hidden_new, pulled_second, tile_src, tile_count, slot_live, tile_values)
    second_mine, second_theirs = halves(agg_second)
    second_got = lax.ppermute(second_theirs, "dom", pair)
    second_term = jnp.einsum(
        "vprn,vbn->prb", second_mine, out_grad, preferred_element_type=jnp.float32
    ) + jnp.einsum("vprn,vbn->prb", second_got, partner_grad, preferred_element_type=jnp.float32)

    bias_cols = jnp.zeros((fsdp_size, 2 * half_rows, lanes), jnp.float32)
    bias_cols = bias_cols.at[:, 0, : hidden // fsdp_size].set(bias_term.reshape(fsdp_size, hidden // fsdp_size))
    packed_terms = jnp.concatenate([jnp.concatenate([first_term, second_term], axis=1), bias_cols], axis=2)
    arrived_terms = lax.all_to_all(packed_terms.astype(jnp.bfloat16), "fsdp", split_axis=0, concat_axis=0, tiled=True)
    shard = jnp.sum(arrived_terms.astype(jnp.float32), axis=0)
    for flip in (2, 4):
        shard = shard + lax.ppermute(shard, "dom", [(d, d ^ flip) for d in range(dom_size)])
    other = lax.ppermute(shard, "dom", pair)
    low = jnp.where(core == 0, shard, other)
    high = jnp.where(core == 0, other, shard)
    first_total = jnp.concatenate([low[:half_rows, :hidden], high[:half_rows, :hidden]], axis=0)
    second_total = jnp.concatenate([low[half_rows:, :hidden], high[half_rows:, :hidden]], axis=0)
    bias_total = (shard + other)[0, hidden : hidden + hidden // fsdp_size]
    return (hidden_new, first_total, second_total, bias_total)


def solution(mesh):
    return jax.shard_map(
        on_device,
        mesh=mesh,
        in_specs=(
            P(("dom", "fsdp"), None, None),
            P("dom", "fsdp", None),
            P("dom", "fsdp", None),
            P("dom", None, None),
            P("dom", None),
            P(("dom", "fsdp"), None),
            P(("dom", "fsdp")),
            P(("dom", "fsdp"), None, None, None),
            P("fsdp", None),
            P("fsdp", None),
            P("fsdp"),
            P(("dom", "fsdp"), None, None),
        ),
        out_specs=(P(("dom", "fsdp"), None, None), P("fsdp", None), P("fsdp", None), P("fsdp")),
        check_vma=False,
    )
```

```python
import functools

import jax
import jax.numpy as jnp
from jax import lax
from jax.experimental import pallas as pl
from jax.experimental.pallas import tpu as pltpu
from jax.sharding import PartitionSpec as P


def gelu_tanh(inputs):
    return jax.nn.gelu(inputs, approximate=True)


def _agg_kernel(own_count, last_tile, src_ref, cnt_ref, live_ref, own_ref, pulled_ref, tile_ref, out_ref, acc_ref):
    v = pl.program_id(0)
    t = pl.program_id(1)

    @pl.when(t == 0)
    def _():
        acc_ref[...] = jnp.zeros_like(acc_ref)

    src = src_ref[v, t]
    tile_live = t < cnt_ref[v]
    own_ok = tile_live & (src < own_count)
    pull_ok = tile_live & (src >= own_count) & (live_ref[jnp.maximum(src - own_count, 0)] > 0)

    @pl.when(own_ok)
    def _():
        acc_ref[...] += jnp.dot(own_ref[0], tile_ref[0, 0], preferred_element_type=jnp.float32)

    @pl.when(pull_ok)
    def _():
        block = pulled_ref[0, :, 0]
        block = block.reshape(block.shape[0] * block.shape[1], block.shape[2])
        acc_ref[...] += jnp.dot(block, tile_ref[0, 0], preferred_element_type=jnp.float32)

    @pl.when(t == last_tile)
    def _():
        out_ref[0] = acc_ref[...].astype(out_ref.dtype)


def aggregate(own, pulled, tile_src, tile_count, slot_live, tile_values):
    nb, feat, blk = own.shape
    dom, fsdp, cap = pulled.shape[0], pulled.shape[1], pulled.shape[2]
    tiles = tile_src.shape[1]

    def eff(v, t, src_ref, cnt_ref):
        return jnp.minimum(t, cnt_ref[v] - 1)

    def own_map(v, t, src_ref, cnt_ref, live_ref):
        s = src_ref[v, eff(v, t, src_ref, cnt_ref)]
        return (jnp.clip(s, 0, nb - 1), 0, 0)

    def pulled_map(v, t, src_ref, cnt_ref, live_ref):
        s = jnp.clip(src_ref[v, eff(v, t, src_ref, cnt_ref)] - nb, 0, cap * dom - 1)
        return (s % dom, 0, s // dom, 0, 0)

    def tile_map(v, t, src_ref, cnt_ref, live_ref):
        return (v, eff(v, t, src_ref, cnt_ref), 0, 0)

    def out_map(v, t, src_ref, cnt_ref, live_ref):
        return (v, 0, 0)

    grid_spec = pltpu.PrefetchScalarGridSpec(
        num_scalar_prefetch=3,
        grid=(nb, tiles),
        in_specs=[
            pl.BlockSpec((1, feat, blk), own_map),
            pl.BlockSpec((1, fsdp, 1) + pulled.shape[3:], pulled_map),
            pl.BlockSpec((1, 1, blk, blk), tile_map),
        ],
        out_specs=pl.BlockSpec((1, feat, blk), out_map),
        scratch_shapes=[pltpu.VMEM((feat, blk), jnp.float32)],
    )
    flops = 2 * nb * tiles * feat * blk * blk
    return pl.pallas_call(
        functools.partial(_agg_kernel, nb, tiles - 1),
        grid_spec=grid_spec,
        out_shape=jax.ShapeDtypeStruct(own.shape, jnp.bfloat16),
        compiler_params=pltpu.CompilerParams(dimension_semantics=("arbitrary", "arbitrary")),
        cost_estimate=pl.CostEstimate(
            flops=flops, transcendentals=0, bytes_accessed=nb * tiles * (2 * feat * blk * 2 + blk * blk * 2) + own.size * 2
        ),
    )(tile_src, tile_count, slot_live, own, pulled, tile_values)


def _spread_kernel(own_count, src_ref, cnt_ref, back_ref, tile_ref, out_ref):
    v = pl.program_id(0)
    t = pl.program_id(1)

    @pl.when((v == 0) & (t == 0))
    def _():
        out_ref[...] = jnp.zeros_like(out_ref)

    src = src_ref[v, t]

    @pl.when((t < cnt_ref[v]) & (src < own_count))
    def _():
        term = lax.dot_general(
            back_ref[0], tile_ref[0, 0], (((1,), (1,)), ((), ())), preferred_element_type=jnp.float32
        )
        out_ref[src] = out_ref[src] + term


def spread_back(back_second, tile_src, tile_count, tile_values):
    nb, width, blk = back_second.shape
    tiles = tile_src.shape[1]

    def eff(v, t, cnt_ref):
        return jnp.minimum(t, cnt_ref[v] - 1)

    grid_spec = pltpu.PrefetchScalarGridSpec(
        num_scalar_prefetch=2,
        grid=(nb, tiles),
        in_specs=[
            pl.BlockSpec((1, width, blk), lambda v, t, s, c: (v, 0, 0)),
            pl.BlockSpec((1, 1, blk, blk), lambda v, t, s, c: (v, eff(v, t, c), 0, 0)),
        ],
        out_specs=pl.BlockSpec((nb, width, blk), lambda v, t, s, c: (0, 0, 0)),
    )
    return pl.pallas_call(
        functools.partial(_spread_kernel, nb),
        grid_spec=grid_spec,
        out_shape=jax.ShapeDtypeStruct(back_second.shape, jnp.float32),
        compiler_params=pltpu.CompilerParams(dimension_semantics=("arbitrary", "arbitrary")),
        cost_estimate=pl.CostEstimate(
            flops=2 * nb * tiles * width * blk * blk,
            transcendentals=0,
            bytes_accessed=back_second.size * 2 + nb * tiles * blk * blk * 2 + back_second.size * 4,
        ),
    )(tile_src, tile_count, back_second, tile_values)


def gather_rows(x, axis):
    n = lax.axis_size(axis)
    spread = lax.all_to_all(jnp.broadcast_to(x[None], (n,) + x.shape), axis, split_axis=0, concat_axis=0, tiled=True)
    return spread.reshape((n * x.shape[0],) + x.shape[1:])


def on_device(
    features,
    history_first,
    history_second,
    pull_list,
    pull_count,
    tile_src,
    tile_count,
    tile_values,
    w_first,
    w_second,
    bias_first,
    out_grad,
):
    dom_size = lax.axis_size("dom")
    fsdp_size = lax.axis_size("fsdp")
    me = lax.axis_index("dom") * fsdp_size + lax.axis_index("fsdp")
    rows, hidden = w_first.shape
    bias_cols = jnp.broadcast_to(bias_first[:, None], (rows, 128))
    packed = lax.all_gather(jnp.concatenate([w_first, w_second, bias_cols], axis=1), "fsdp", axis=0, tiled=True)
    first_full = packed[:, :hidden]
    second_full = packed[:, hidden : 2 * hidden]
    bias_full = packed[:, 2 * hidden].astype(jnp.float32)

    chosen = pull_list[0]
    requesters, slot_cap = chosen.shape
    counts_all = pull_count
    for flip in (1, 2, 4):
        other = lax.ppermute(counts_all, "dom", [(d, d ^ flip) for d in range(dom_size)])
        low_half = (lax.axis_index("dom") & flip) == 0
        counts_all = jnp.where(
            low_half, jnp.concatenate([counts_all, other], 0), jnp.concatenate([other, counts_all], 0)
        )
    counts_all, chosen = lax.optimization_barrier((counts_all, chosen))
    my_counts = lax.dynamic_index_in_dim(counts_all, me, axis=1, keepdims=False)
    slot_live = (lax.broadcasted_iota(jnp.int32, (slot_cap, dom_size), 0) < my_counts[None, :]).astype(jnp.int32)
    slot_live = slot_live.reshape(-1)

    block_len = features.shape[2]
    first_cols = history_first.shape[1]
    second_cols = history_second.shape[1]
    sent_first = jnp.take(history_first, chosen.reshape(-1), axis=0, mode="clip").reshape(requesters, slot_cap, first_cols, block_len)
    sent_second = jnp.take(history_second, chosen.reshape(-1), axis=0, mode="clip").reshape(requesters, slot_cap, second_cols, block_len)
    arrived_first = lax.all_to_all(sent_first, ("dom", "fsdp"), split_axis=0, concat_axis=0, tiled=True)
    arrived_second = lax.all_to_all(sent_second, ("dom", "fsdp"), split_axis=0, concat_axis=0, tiled=True)
    pulled_first = arrived_first.reshape(dom_size, fsdp_size, slot_cap, first_cols, block_len)
    pulled_second = arrived_second.reshape(dom_size, fsdp_size, slot_cap, second_cols, block_len)

    core = lax.axis_index("dom") % 2
    pair = [(d, d ^ 1) for d in range(dom_size)]
    partner_grad = lax.ppermute(out_grad, "dom", pair)

    back_second = jnp.einsum(
        "ab,vbn->van", second_full, out_grad, preferred_element_type=jnp.float32
    ).astype(jnp.bfloat16)
    back_hidden = spread_back(back_second, tile_src, tile_count, tile_values)

    def halves(x):
        split = x.reshape(x.shape[0], fsdp_size, 2, x.shape[1] // (2 * fsdp_size), x.shape[2])
        mine = lax.dynamic_index_in_dim(split, core, axis=2, keepdims=False)
        theirs = lax.dynamic_index_in_dim(split, 1 - core, axis=2, keepdims=False)
        return mine, theirs

    agg_first = aggregate(features, pulled_first, tile_src, tile_count, slot_live, tile_values)
    pre_act = (
        jnp.einsum("fh,vfn->vhn", first_full, agg_first, preferred_element_type=jnp.float32)
        + bias_full[None, :, None]
    )
    hidden_new = gelu_tanh(pre_act).astype(jnp.bfloat16)
    _, pullback = jax.vjp(gelu_tanh, pre_act)
    back_pre = pullback(back_hidden)[0].astype(jnp.bfloat16)
    bias_term = jnp.sum(back_pre.astype(jnp.float32), axis=(0, 2))
    first_mine, first_theirs = halves(agg_first)
    first_got, back_got = lax.ppermute((first_theirs, back_pre), "dom", pair)
    first_term = jnp.einsum(
        "vprn,vhn->prh", first_mine, back_pre, preferred_element_type=jnp.float32
    ) + jnp.einsum("vprn,vhn->prh", first_got, back_got, preferred_element_type=jnp.float32)

    half_rows = first_term.shape[1]
    lanes = 128
    agg_second = aggregate(hidden_new, pulled_second, tile_src, tile_count, slot_live, tile_values)
    second_mine, second_theirs = halves(agg_second)
    second_got = lax.ppermute(second_theirs, "dom", pair)
    second_term = jnp.einsum(
        "vprn,vbn->prb", second_mine, out_grad, preferred_element_type=jnp.float32
    ) + jnp.einsum("vprn,vbn->prb", second_got, partner_grad, preferred_element_type=jnp.float32)

    bias_cols = jnp.zeros((fsdp_size, 2 * half_rows, lanes), jnp.float32)
    bias_cols = bias_cols.at[:, 0, : hidden // fsdp_size].set(bias_term.reshape(fsdp_size, hidden // fsdp_size))
    packed_terms = jnp.concatenate([jnp.concatenate([first_term, second_term], axis=1), bias_cols], axis=2)
    arrived_terms = lax.all_to_all(packed_terms.astype(jnp.bfloat16), "fsdp", split_axis=0, concat_axis=0, tiled=True)
    shard = jnp.sum(arrived_terms.astype(jnp.float32), axis=0)
    for flip in (2, 4):
        shard = shard + lax.ppermute(shard, "dom", [(d, d ^ flip) for d in range(dom_size)])
    other = lax.ppermute(shard, "dom", pair)
    low = jnp.where(core == 0, shard, other)
    high = jnp.where(core == 0, other, shard)
    first_total = jnp.concatenate([low[:half_rows, :hidden], high[:half_rows, :hidden]], axis=0)
    second_total = jnp.concatenate([low[half_rows:, :hidden], high[half_rows:, :hidden]], axis=0)
    bias_total = (shard + other)[0, hidden : hidden + hidden // fsdp_size]
    return (hidden_new, first_total, second_total, bias_total)


def solution(mesh):
    return jax.shard_map(
        on_device,
        mesh=mesh,
        in_specs=(
            P(("dom", "fsdp"), None, None),
            P("dom", "fsdp", None),
            P("dom", "fsdp", None),
            P("dom", None, None),
            P("dom", None),
            P(("dom", "fsdp"), None),
            P(("dom", "fsdp")),
            P(("dom", "fsdp"), None, None, None),
            P("fsdp", None),
            P("fsdp", None),
            P("fsdp"),
            P(("dom", "fsdp"), None, None),
        ),
        out_specs=(P(("dom", "fsdp"), None, None), P("fsdp", None), P("fsdp", None), P("fsdp")),
        check_vma=False,
    )
```

```python
import functools

import jax
import jax.numpy as jnp
from jax import lax
from jax.experimental import pallas as pl
from jax.experimental.pallas import tpu as pltpu
from jax.sharding import PartitionSpec as P


def gelu_tanh(inputs):
    return jax.nn.gelu(inputs, approximate=True)


def _agg_kernel(own_count, last_tile, src_ref, cnt_ref, live_ref, own_ref, pulled_ref, tile_ref, out_ref, acc_ref):
    v = pl.program_id(0)
    t = pl.program_id(1)

    @pl.when(t == 0)
    def _():
        acc_ref[...] = jnp.zeros_like(acc_ref)

    src = src_ref[v, t]
    tile_live = t < cnt_ref[v]
    own_ok = tile_live & (src < own_count)
    pull_ok = tile_live & (src >= own_count) & (live_ref[jnp.maximum(src - own_count, 0)] > 0)

    @pl.when(own_ok)
    def _():
        acc_ref[...] += jnp.dot(own_ref[0], tile_ref[0, 0], preferred_element_type=jnp.float32)

    @pl.when(pull_ok)
    def _():
        block = pulled_ref[0, :, 0]
        block = block.reshape(block.shape[0] * block.shape[1], block.shape[2])
        acc_ref[...] += jnp.dot(block, tile_ref[0, 0], preferred_element_type=jnp.float32)

    @pl.when(t == last_tile)
    def _():
        out_ref[0] = acc_ref[...].astype(out_ref.dtype)


def aggregate(own, pulled, tile_src, tile_count, slot_live, tile_values):
    nb, feat, blk = own.shape
    dom, fsdp, cap = pulled.shape[0], pulled.shape[1], pulled.shape[2]
    tiles = tile_src.shape[1]

    def eff(v, t, src_ref, cnt_ref):
        return jnp.minimum(t, cnt_ref[v] - 1)

    def own_map(v, t, src_ref, cnt_ref, live_ref):
        s = src_ref[v, eff(v, t, src_ref, cnt_ref)]
        return (jnp.clip(s, 0, nb - 1), 0, 0)

    def pulled_map(v, t, src_ref, cnt_ref, live_ref):
        s = jnp.clip(src_ref[v, eff(v, t, src_ref, cnt_ref)] - nb, 0, cap * dom - 1)
        return (s % dom, 0, s // dom, 0, 0)

    def tile_map(v, t, src_ref, cnt_ref, live_ref):
        return (v, eff(v, t, src_ref, cnt_ref), 0, 0)

    def out_map(v, t, src_ref, cnt_ref, live_ref):
        return (v, 0, 0)

    grid_spec = pltpu.PrefetchScalarGridSpec(
        num_scalar_prefetch=3,
        grid=(nb, tiles),
        in_specs=[
            pl.BlockSpec((1, feat, blk), own_map),
            pl.BlockSpec((1, fsdp, 1) + pulled.shape[3:], pulled_map),
            pl.BlockSpec((1, 1, blk, blk), tile_map),
        ],
        out_specs=pl.BlockSpec((1, feat, blk), out_map),
        scratch_shapes=[pltpu.VMEM((feat, blk), jnp.float32)],
    )
    flops = 2 * nb * tiles * feat * blk * blk
    return pl.pallas_call(
        functools.partial(_agg_kernel, nb, tiles - 1),
        grid_spec=grid_spec,
        out_shape=jax.ShapeDtypeStruct(own.shape, jnp.bfloat16),
        compiler_params=pltpu.CompilerParams(dimension_semantics=("arbitrary", "arbitrary")),
        cost_estimate=pl.CostEstimate(
            flops=flops, transcendentals=0, bytes_accessed=nb * tiles * (2 * feat * blk * 2 + blk * blk * 2) + own.size * 2
        ),
    )(tile_src, tile_count, slot_live, own, pulled, tile_values)


def _spread_kernel(own_count, src_ref, cnt_ref, back_ref, tile_ref, out_ref):
    v = pl.program_id(0)
    t = pl.program_id(1)

    @pl.when((v == 0) & (t == 0))
    def _():
        out_ref[...] = jnp.zeros_like(out_ref)

    src = src_ref[v, t]

    @pl.when((t < cnt_ref[v]) & (src < own_count))
    def _():
        term = lax.dot_general(
            back_ref[0], tile_ref[0, 0], (((1,), (1,)), ((), ())), preferred_element_type=jnp.float32
        )
        out_ref[src] = out_ref[src] + term


def spread_back(back_second, tile_src, tile_count, tile_values):
    nb, width, blk = back_second.shape
    tiles = tile_src.shape[1]

    def eff(v, t, cnt_ref):
        return jnp.minimum(t, cnt_ref[v] - 1)

    grid_spec = pltpu.PrefetchScalarGridSpec(
        num_scalar_prefetch=2,
        grid=(nb, tiles),
        in_specs=[
            pl.BlockSpec((1, width, blk), lambda v, t, s, c: (v, 0, 0)),
            pl.BlockSpec((1, 1, blk, blk), lambda v, t, s, c: (v, eff(v, t, c), 0, 0)),
        ],
        out_specs=pl.BlockSpec((nb, width, blk), lambda v, t, s, c: (0, 0, 0)),
    )
    return pl.pallas_call(
        functools.partial(_spread_kernel, nb),
        grid_spec=grid_spec,
        out_shape=jax.ShapeDtypeStruct(back_second.shape, jnp.float32),
        compiler_params=pltpu.CompilerParams(dimension_semantics=("arbitrary", "arbitrary")),
        cost_estimate=pl.CostEstimate(
            flops=2 * nb * tiles * width * blk * blk,
            transcendentals=0,
            bytes_accessed=back_second.size * 2 + nb * tiles * blk * blk * 2 + back_second.size * 4,
        ),
    )(tile_src, tile_count, back_second, tile_values)


def gather_rows(x, axis):
    n = lax.axis_size(axis)
    spread = lax.all_to_all(jnp.broadcast_to(x[None], (n,) + x.shape), axis, split_axis=0, concat_axis=0, tiled=True)
    return spread.reshape((n * x.shape[0],) + x.shape[1:])


def on_device(
    features,
    history_first,
    history_second,
    pull_list,
    pull_count,
    tile_src,
    tile_count,
    tile_values,
    w_first,
    w_second,
    bias_first,
    out_grad,
):
    dom_size = lax.axis_size("dom")
    fsdp_size = lax.axis_size("fsdp")
    me = lax.axis_index("dom") * fsdp_size + lax.axis_index("fsdp")
    rows, hidden = w_first.shape
    bias_cols = jnp.broadcast_to(bias_first[:, None], (rows, 128))
    packed = lax.all_gather(jnp.concatenate([w_first, w_second, bias_cols], axis=1), "fsdp", axis=0, tiled=True)
    first_full = packed[:, :hidden]
    second_full = packed[:, hidden : 2 * hidden]
    bias_full = packed[:, 2 * hidden].astype(jnp.float32)

    chosen = pull_list[0]
    requesters, slot_cap = chosen.shape
    counts_all = lax.all_gather(pull_count, "dom", axis=0, tiled=True)
    counts_all, chosen = lax.optimization_barrier((counts_all, chosen))
    my_counts = lax.dynamic_index_in_dim(counts_all, me, axis=1, keepdims=False)
    slot_live = (lax.broadcasted_iota(jnp.int32, (slot_cap, dom_size), 0) < my_counts[None, :]).astype(jnp.int32)
    slot_live = slot_live.reshape(-1)

    block_len = features.shape[2]
    first_cols = history_first.shape[1]
    second_cols = history_second.shape[1]
    sent_first = jnp.take(history_first, chosen.reshape(-1), axis=0, mode="clip").reshape(requesters, slot_cap, first_cols, block_len)
    sent_second = jnp.take(history_second, chosen.reshape(-1), axis=0, mode="clip").reshape(requesters, slot_cap, second_cols, block_len)
    arrived_first = lax.all_to_all(sent_first, ("dom", "fsdp"), split_axis=0, concat_axis=0, tiled=True)
    arrived_second = lax.all_to_all(sent_second, ("dom", "fsdp"), split_axis=0, concat_axis=0, tiled=True)
    pulled_first = arrived_first.reshape(dom_size, fsdp_size, slot_cap, first_cols, block_len)
    pulled_second = arrived_second.reshape(dom_size, fsdp_size, slot_cap, second_cols, block_len)

    core = lax.axis_index("dom") % 2
    pair = [(d, d ^ 1) for d in range(dom_size)]
    partner_grad = lax.ppermute(out_grad, "dom", pair)

    back_second = jnp.einsum(
        "ab,vbn->van", second_full, out_grad, preferred_element_type=jnp.float32
    ).astype(jnp.bfloat16)
    back_hidden = spread_back(back_second, tile_src, tile_count, tile_values)

    def halves(x):
        split = x.reshape(x.shape[0], fsdp_size, 2, x.shape[1] // (2 * fsdp_size), x.shape[2])
        mine = lax.dynamic_index_in_dim(split, core, axis=2, keepdims=False)
        theirs = lax.dynamic_index_in_dim(split, 1 - core, axis=2, keepdims=False)
        return mine, theirs

    agg_first = aggregate(features, pulled_first, tile_src, tile_count, slot_live, tile_values)
    pre_act = (
        jnp.einsum("fh,vfn->vhn", first_full, agg_first, preferred_element_type=jnp.float32)
        + bias_full[None, :, None]
    )
    hidden_new = gelu_tanh(pre_act).astype(jnp.bfloat16)
    _, pullback = jax.vjp(gelu_tanh, pre_act)
    back_pre = pullback(back_hidden)[0].astype(jnp.bfloat16)
    bias_term = jnp.sum(back_pre.astype(jnp.float32), axis=(0, 2))
    first_mine, first_theirs = halves(agg_first)
    first_got, back_got = lax.ppermute((first_theirs, back_pre), "dom", pair)
    first_term = jnp.einsum(
        "vprn,vhn->prh", first_mine, back_pre, preferred_element_type=jnp.float32
    ) + jnp.einsum("vprn,vhn->prh", first_got, back_got, preferred_element_type=jnp.float32)

    half_rows = first_term.shape[1]
    lanes = 128
    agg_second = aggregate(hidden_new, pulled_second, tile_src, tile_count, slot_live, tile_values)
    second_mine, second_theirs = halves(agg_second)
    second_got = lax.ppermute(second_theirs, "dom", pair)
    second_term = jnp.einsum(
        "vprn,vbn->prb", second_mine, out_grad, preferred_element_type=jnp.float32
    ) + jnp.einsum("vprn,vbn->prb", second_got, partner_grad, preferred_element_type=jnp.float32)

    sub = half_rows // dom_size
    bias_share = hidden // fsdp_size // dom_size

    def by_destination(term):
        split = term.reshape(fsdp_size, dom_size, sub, hidden)
        return jnp.transpose(split, (1, 0, 2, 3)).reshape(dom_size * fsdp_size, sub, hidden)

    bias_part = jnp.transpose(bias_term.reshape(fsdp_size, dom_size, bias_share), (1, 0, 2))
    bias_part = jnp.pad(bias_part.reshape(dom_size * fsdp_size, 1, bias_share), ((0, 0), (0, 2 * sub - 1), (0, lanes - bias_share)))
    packed_terms = jnp.concatenate(
        [jnp.concatenate([by_destination(first_term), by_destination(second_term)], axis=1), bias_part], axis=2
    )
    arrived_terms = lax.all_to_all(packed_terms.astype(jnp.bfloat16), ("dom", "fsdp"), split_axis=0, concat_axis=0, tiled=True)
    arrived_terms = arrived_terms.astype(jnp.float32).reshape(dom_size // 2, 2, fsdp_size, 2 * sub, hidden + lanes)
    reduced = jnp.sum(arrived_terms, axis=(0, 2))
    pieces = reduced[None]
    for flip in (1, 2, 4):
        other = lax.ppermute(pieces, "dom", [(d, d ^ flip) for d in range(dom_size)])
        low_half = (lax.axis_index("dom") & flip) == 0
        pieces = jnp.where(low_half, jnp.concatenate([pieces, other], 0), jnp.concatenate([other, pieces], 0))
    ordered = jnp.transpose(pieces, (1, 0, 2, 3))
    first_total = ordered[:, :, :sub, :hidden].reshape(2 * half_rows, hidden)
    second_total = ordered[:, :, sub:, :hidden].reshape(2 * half_rows, hidden)
    bias_total = jnp.sum(pieces[:, :, 0, hidden : hidden + bias_share], axis=1).reshape(-1)
    return (hidden_new, first_total, second_total, bias_total)


def solution(mesh):
    return jax.shard_map(
        on_device,
        mesh=mesh,
        in_specs=(
            P(("dom", "fsdp"), None, None),
            P("dom", "fsdp", None),
            P("dom", "fsdp", None),
            P("dom", None, None),
            P("dom", None),
            P(("dom", "fsdp"), None),
            P(("dom", "fsdp")),
            P(("dom", "fsdp"), None, None, None),
            P("fsdp", None),
            P("fsdp", None),
            P("fsdp"),
            P(("dom", "fsdp"), None, None),
        ),
        out_specs=(P(("dom", "fsdp"), None, None), P("fsdp", None), P("fsdp", None), P("fsdp")),
        check_vma=False,
    )
```

```python
import functools

import jax
import jax.numpy as jnp
from jax import lax
from jax.experimental import pallas as pl
from jax.experimental.pallas import tpu as pltpu
from jax.sharding import PartitionSpec as P


def gelu_tanh(inputs):
    return jax.nn.gelu(inputs, approximate=True)


def _agg_kernel(own_count, last_tile, src_ref, cnt_ref, live_ref, own_ref, pulled_ref, tile_ref, out_ref, acc_ref):
    v = pl.program_id(0)
    t = pl.program_id(1)

    @pl.when(t == 0)
    def _():
        acc_ref[...] = jnp.zeros_like(acc_ref)

    src = src_ref[v, t]
    tile_live = t < cnt_ref[v]
    own_ok = tile_live & (src < own_count)
    pull_ok = tile_live & (src >= own_count) & (live_ref[jnp.maximum(src - own_count, 0)] > 0)

    @pl.when(own_ok)
    def _():
        acc_ref[...] += jnp.dot(own_ref[0], tile_ref[0, 0], preferred_element_type=jnp.float32)

    @pl.when(pull_ok)
    def _():
        block = pulled_ref[0, :, 0]
        block = block.reshape(block.shape[0] * block.shape[1], block.shape[2])
        acc_ref[...] += jnp.dot(block, tile_ref[0, 0], preferred_element_type=jnp.float32)

    @pl.when(t == last_tile)
    def _():
        out_ref[0] = acc_ref[...].astype(out_ref.dtype)


def aggregate(own, pulled, tile_src, tile_count, slot_live, tile_values):
    nb, feat, blk = own.shape
    dom, fsdp, cap = pulled.shape[0], pulled.shape[1], pulled.shape[2]
    tiles = tile_src.shape[1]

    def eff(v, t, src_ref, cnt_ref):
        return jnp.minimum(t, cnt_ref[v] - 1)

    def latest(v, t, src_ref, cnt_ref, own_kind):
        te = eff(v, t, src_ref, cnt_ref)
        pick = jnp.int32(0)
        for slot in range(tiles):
            s = src_ref[v, slot]
            kind_ok = (s < nb) if own_kind else (s >= nb)
            pick = jnp.where((slot <= te) & kind_ok, s, pick)
        return pick

    def own_map(v, t, src_ref, cnt_ref, live_ref):
        s = latest(v, t, src_ref, cnt_ref, True)
        return (jnp.clip(s, 0, nb - 1), 0, 0)

    def pulled_map(v, t, src_ref, cnt_ref, live_ref):
        s = jnp.clip(latest(v, t, src_ref, cnt_ref, False) - nb, 0, cap * dom - 1)
        return (s % dom, 0, s // dom, 0, 0)

    def tile_map(v, t, src_ref, cnt_ref, live_ref):
        return (v, eff(v, t, src_ref, cnt_ref), 0, 0)

    def out_map(v, t, src_ref, cnt_ref, live_ref):
        return (v, 0, 0)

    grid_spec = pltpu.PrefetchScalarGridSpec(
        num_scalar_prefetch=3,
        grid=(nb, tiles),
        in_specs=[
            pl.BlockSpec((1, feat, blk), own_map),
            pl.BlockSpec((1, fsdp, 1) + pulled.shape[3:], pulled_map),
            pl.BlockSpec((1, 1, blk, blk), tile_map),
        ],
        out_specs=pl.BlockSpec((1, feat, blk), out_map),
        scratch_shapes=[pltpu.VMEM((feat, blk), jnp.float32)],
    )
    flops = 2 * nb * tiles * feat * blk * blk
    return pl.pallas_call(
        functools.partial(_agg_kernel, nb, tiles - 1),
        grid_spec=grid_spec,
        out_shape=jax.ShapeDtypeStruct(own.shape, jnp.bfloat16),
        compiler_params=pltpu.CompilerParams(dimension_semantics=("arbitrary", "arbitrary")),
        cost_estimate=pl.CostEstimate(
            flops=flops, transcendentals=0, bytes_accessed=nb * tiles * (2 * feat * blk * 2 + blk * blk * 2) + own.size * 2
        ),
    )(tile_src, tile_count, slot_live, own, pulled, tile_values)


def _spread_kernel(own_count, src_ref, cnt_ref, back_ref, tile_ref, out_ref):
    v = pl.program_id(0)
    t = pl.program_id(1)

    @pl.when((v == 0) & (t == 0))
    def _():
        out_ref[...] = jnp.zeros_like(out_ref)

    src = src_ref[v, t]

    @pl.when((t < cnt_ref[v]) & (src < own_count))
    def _():
        term = lax.dot_general(
            back_ref[0], tile_ref[0, 0], (((1,), (1,)), ((), ())), preferred_element_type=jnp.float32
        )
        out_ref[src] = out_ref[src] + term


def spread_back(back_second, tile_src, tile_count, tile_values):
    nb, width, blk = back_second.shape
    tiles = tile_src.shape[1]

    def eff(v, t, cnt_ref):
        return jnp.minimum(t, cnt_ref[v] - 1)

    grid_spec = pltpu.PrefetchScalarGridSpec(
        num_scalar_prefetch=2,
        grid=(nb, tiles),
        in_specs=[
            pl.BlockSpec((1, width, blk), lambda v, t, s, c: (v, 0, 0)),
            pl.BlockSpec((1, 1, blk, blk), lambda v, t, s, c: (v, eff(v, t, c), 0, 0)),
        ],
        out_specs=pl.BlockSpec((nb, width, blk), lambda v, t, s, c: (0, 0, 0)),
    )
    return pl.pallas_call(
        functools.partial(_spread_kernel, nb),
        grid_spec=grid_spec,
        out_shape=jax.ShapeDtypeStruct(back_second.shape, jnp.float32),
        compiler_params=pltpu.CompilerParams(dimension_semantics=("arbitrary", "arbitrary")),
        cost_estimate=pl.CostEstimate(
            flops=2 * nb * tiles * width * blk * blk,
            transcendentals=0,
            bytes_accessed=back_second.size * 2 + nb * tiles * blk * blk * 2 + back_second.size * 4,
        ),
    )(tile_src, tile_count, back_second, tile_values)


def gather_rows(x, axis):
    n = lax.axis_size(axis)
    spread = lax.all_to_all(jnp.broadcast_to(x[None], (n,) + x.shape), axis, split_axis=0, concat_axis=0, tiled=True)
    return spread.reshape((n * x.shape[0],) + x.shape[1:])


def on_device(
    features,
    history_first,
    history_second,
    pull_list,
    pull_count,
    tile_src,
    tile_count,
    tile_values,
    w_first,
    w_second,
    bias_first,
    out_grad,
):
    dom_size = lax.axis_size("dom")
    fsdp_size = lax.axis_size("fsdp")
    me = lax.axis_index("dom") * fsdp_size + lax.axis_index("fsdp")
    rows, hidden = w_first.shape
    bias_cols = jnp.broadcast_to(bias_first[:, None], (rows, 128))
    packed = lax.all_gather(jnp.concatenate([w_first, w_second, bias_cols], axis=1), "fsdp", axis=0, tiled=True)
    first_full = packed[:, :hidden]
    second_full = packed[:, hidden : 2 * hidden]
    bias_full = packed[:, 2 * hidden].astype(jnp.float32)

    chosen = pull_list[0]
    requesters, slot_cap = chosen.shape
    counts_all = lax.all_gather(pull_count, "dom", axis=0, tiled=True)
    counts_all, chosen = lax.optimization_barrier((counts_all, chosen))
    my_counts = lax.dynamic_index_in_dim(counts_all, me, axis=1, keepdims=False)
    slot_live = (lax.broadcasted_iota(jnp.int32, (slot_cap, dom_size), 0) < my_counts[None, :]).astype(jnp.int32)
    slot_live = slot_live.reshape(-1)

    block_len = features.shape[2]
    first_cols = history_first.shape[1]
    second_cols = history_second.shape[1]
    sent_first = jnp.take(history_first, chosen.reshape(-1), axis=0, mode="clip").reshape(requesters, slot_cap, first_cols, block_len)
    sent_second = jnp.take(history_second, chosen.reshape(-1), axis=0, mode="clip").reshape(requesters, slot_cap, second_cols, block_len)
    arrived_first = lax.all_to_all(sent_first, ("dom", "fsdp"), split_axis=0, concat_axis=0, tiled=True)
    arrived_second = lax.all_to_all(sent_second, ("dom", "fsdp"), split_axis=0, concat_axis=0, tiled=True)
    pulled_first = arrived_first.reshape(dom_size, fsdp_size, slot_cap, first_cols, block_len)
    pulled_second = arrived_second.reshape(dom_size, fsdp_size, slot_cap, second_cols, block_len)

    core = lax.axis_index("dom") % 2
    pair = [(d, d ^ 1) for d in range(dom_size)]
    partner_grad = lax.ppermute(out_grad, "dom", pair)

    back_second = jnp.einsum(
        "ab,vbn->van", second_full, out_grad, preferred_element_type=jnp.float32
    ).astype(jnp.bfloat16)
    back_hidden = spread_back(back_second, tile_src, tile_count, tile_values)

    def halves(x):
        split = x.reshape(x.shape[0], fsdp_size, 2, x.shape[1] // (2 * fsdp_size), x.shape[2])
        mine = lax.dynamic_index_in_dim(split, core, axis=2, keepdims=False)
        theirs = lax.dynamic_index_in_dim(split, 1 - core, axis=2, keepdims=False)
        return mine, theirs

    agg_first = aggregate(features, pulled_first, tile_src, tile_count, slot_live, tile_values)
    pre_act = (
        jnp.einsum("fh,vfn->vhn", first_full, agg_first, preferred_element_type=jnp.float32)
        + bias_full[None, :, None]
    )
    hidden_new = gelu_tanh(pre_act).astype(jnp.bfloat16)
    _, pullback = jax.vjp(gelu_tanh, pre_act)
    back_pre = pullback(back_hidden)[0].astype(jnp.bfloat16)
    bias_term = jnp.sum(back_pre.astype(jnp.float32), axis=(0, 2))
    first_mine, first_theirs = halves(agg_first)
    first_got, back_got = lax.ppermute((first_theirs, back_pre), "dom", pair)
    first_term = jnp.einsum(
        "vprn,vhn->prh", first_mine, back_pre, preferred_element_type=jnp.float32
    ) + jnp.einsum("vprn,vhn->prh", first_got, back_got, preferred_element_type=jnp.float32)

    half_rows = first_term.shape[1]
    lanes = 128
    agg_second = aggregate(hidden_new, pulled_second, tile_src, tile_count, slot_live, tile_values)
    second_mine, second_theirs = halves(agg_second)
    second_got = lax.ppermute(second_theirs, "dom", pair)
    second_term = jnp.einsum(
        "vprn,vbn->prb", second_mine, out_grad, preferred_element_type=jnp.float32
    ) + jnp.einsum("vprn,vbn->prb", second_got, partner_grad, preferred_element_type=jnp.float32)

    bias_cols = jnp.zeros((fsdp_size, 2 * half_rows, lanes), jnp.float32)
    bias_cols = bias_cols.at[:, 0, : hidden // fsdp_size].set(bias_term.reshape(fsdp_size, hidden // fsdp_size))
    packed_terms = jnp.concatenate([jnp.concatenate([first_term, second_term], axis=1), bias_cols], axis=2)
    arrived_terms = lax.all_to_all(packed_terms.astype(jnp.bfloat16), "fsdp", split_axis=0, concat_axis=0, tiled=True)
    shard = jnp.sum(arrived_terms.astype(jnp.float32), axis=0)
    for flip in (2, 4):
        shard = shard + lax.ppermute(shard, "dom", [(d, d ^ flip) for d in range(dom_size)])
    other = lax.ppermute(shard, "dom", pair)
    low = jnp.where(core == 0, shard, other)
    high = jnp.where(core == 0, other, shard)
    first_total = jnp.concatenate([low[:half_rows, :hidden], high[:half_rows, :hidden]], axis=0)
    second_total = jnp.concatenate([low[half_rows:, :hidden], high[half_rows:, :hidden]], axis=0)
    bias_total = (shard + other)[0, hidden : hidden + hidden // fsdp_size]
    return (hidden_new, first_total, second_total, bias_total)


def solution(mesh):
    return jax.shard_map(
        on_device,
        mesh=mesh,
        in_specs=(
            P(("dom", "fsdp"), None, None),
            P("dom", "fsdp", None),
            P("dom", "fsdp", None),
            P("dom", None, None),
            P("dom", None),
            P(("dom", "fsdp"), None),
            P(("dom", "fsdp")),
            P(("dom", "fsdp"), None, None, None),
            P("fsdp", None),
            P("fsdp", None),
            P("fsdp"),
            P(("dom", "fsdp"), None, None),
        ),
        out_specs=(P(("dom", "fsdp"), None, None), P("fsdp", None), P("fsdp", None), P("fsdp")),
        check_vma=False,
    )
```

```python
import functools

import jax
import jax.numpy as jnp
from jax import lax
from jax.experimental import pallas as pl
from jax.experimental.pallas import tpu as pltpu
from jax.sharding import PartitionSpec as P


def gelu_tanh(inputs):
    return jax.nn.gelu(inputs, approximate=True)


def _agg_kernel(own_count, last_step, src_ref, cnt_ref, live_ref, own_a, own_b, pulled_a, pulled_b, tile_ref, out_ref, acc_ref):
    v = pl.program_id(0)
    k = pl.program_id(1)

    @pl.when(k == 0)
    def _():
        acc_ref[...] = jnp.zeros_like(acc_ref)

    for j, own_ref, pulled_ref in ((0, own_a, pulled_a), (1, own_b, pulled_b)):
        t = 2 * k + j
        src = src_ref[v, t]
        tile_live = t < cnt_ref[v]
        own_ok = tile_live & (src < own_count)
        pull_ok = tile_live & (src >= own_count) & (live_ref[jnp.maximum(src - own_count, 0)] > 0)

        @pl.when(own_ok)
        def _():
            acc_ref[...] += jnp.dot(own_ref[0], tile_ref[0, j], preferred_element_type=jnp.float32)

        @pl.when(pull_ok)
        def _():
            block = pulled_ref[0, :, 0]
            block = block.reshape(block.shape[0] * block.shape[1], block.shape[2])
            acc_ref[...] += jnp.dot(block, tile_ref[0, j], preferred_element_type=jnp.float32)

    @pl.when(k == last_step)
    def _():
        out_ref[0] = acc_ref[...].astype(out_ref.dtype)


def aggregate(own, pulled, tile_src, tile_count, slot_live, tile_values):
    nb, feat, blk = own.shape
    dom, fsdp, cap = pulled.shape[0], pulled.shape[1], pulled.shape[2]
    tiles = tile_src.shape[1]
    steps = tiles // 2

    def eff(v, t, cnt_ref):
        return jnp.minimum(t, cnt_ref[v] - 1)

    def own_map(j):
        def index(v, k, src_ref, cnt_ref, live_ref):
            s = src_ref[v, eff(v, 2 * k + j, cnt_ref)]
            return (jnp.clip(s, 0, nb - 1), 0, 0)

        return index

    def pulled_map(j):
        def index(v, k, src_ref, cnt_ref, live_ref):
            s = jnp.clip(src_ref[v, eff(v, 2 * k + j, cnt_ref)] - nb, 0, cap * dom - 1)
            return (s % dom, 0, s // dom, 0, 0)

        return index

    grid_spec = pltpu.PrefetchScalarGridSpec(
        num_scalar_prefetch=3,
        grid=(nb, steps),
        in_specs=[
            pl.BlockSpec((1, feat, blk), own_map(0)),
            pl.BlockSpec((1, feat, blk), own_map(1)),
            pl.BlockSpec((1, fsdp, 1) + pulled.shape[3:], pulled_map(0)),
            pl.BlockSpec((1, fsdp, 1) + pulled.shape[3:], pulled_map(1)),
            pl.BlockSpec((1, 2, blk, blk), lambda v, k, s, c, l: (v, k, 0, 0)),
        ],
        out_specs=pl.BlockSpec((1, feat, blk), lambda v, k, s, c, l: (v, 0, 0)),
        scratch_shapes=[pltpu.VMEM((feat, blk), jnp.float32)],
    )
    flops = 2 * nb * tiles * feat * blk * blk
    return pl.pallas_call(
        functools.partial(_agg_kernel, nb, steps - 1),
        grid_spec=grid_spec,
        out_shape=jax.ShapeDtypeStruct(own.shape, jnp.bfloat16),
        compiler_params=pltpu.CompilerParams(dimension_semantics=("arbitrary", "arbitrary")),
        cost_estimate=pl.CostEstimate(
            flops=flops, transcendentals=0, bytes_accessed=nb * tiles * (2 * feat * blk * 2 + blk * blk * 2) + own.size * 2
        ),
    )(tile_src, tile_count, slot_live, own, own, pulled, pulled, tile_values)


def _spread_kernel(own_count, src_ref, cnt_ref, back_ref, tile_ref, out_ref):
    v = pl.program_id(0)
    t = pl.program_id(1)

    @pl.when((v == 0) & (t == 0))
    def _():
        out_ref[...] = jnp.zeros_like(out_ref)

    src = src_ref[v, t]

    @pl.when((t < cnt_ref[v]) & (src < own_count))
    def _():
        term = lax.dot_general(
            back_ref[0], tile_ref[0, 0], (((1,), (1,)), ((), ())), preferred_element_type=jnp.float32
        )
        out_ref[src] = out_ref[src] + term


def spread_back(back_second, tile_src, tile_count, tile_values):
    nb, width, blk = back_second.shape
    tiles = tile_src.shape[1]

    def eff(v, t, cnt_ref):
        return jnp.minimum(t, cnt_ref[v] - 1)

    grid_spec = pltpu.PrefetchScalarGridSpec(
        num_scalar_prefetch=2,
        grid=(nb, tiles),
        in_specs=[
            pl.BlockSpec((1, width, blk), lambda v, t, s, c: (v, 0, 0)),
            pl.BlockSpec((1, 1, blk, blk), lambda v, t, s, c: (v, eff(v, t, c), 0, 0)),
        ],
        out_specs=pl.BlockSpec((nb, width, blk), lambda v, t, s, c: (0, 0, 0)),
    )
    return pl.pallas_call(
        functools.partial(_spread_kernel, nb),
        grid_spec=grid_spec,
        out_shape=jax.ShapeDtypeStruct(back_second.shape, jnp.float32),
        compiler_params=pltpu.CompilerParams(dimension_semantics=("arbitrary", "arbitrary")),
        cost_estimate=pl.CostEstimate(
            flops=2 * nb * tiles * width * blk * blk,
            transcendentals=0,
            bytes_accessed=back_second.size * 2 + nb * tiles * blk * blk * 2 + back_second.size * 4,
        ),
    )(tile_src, tile_count, back_second, tile_values)


def gather_rows(x, axis):
    n = lax.axis_size(axis)
    spread = lax.all_to_all(jnp.broadcast_to(x[None], (n,) + x.shape), axis, split_axis=0, concat_axis=0, tiled=True)
    return spread.reshape((n * x.shape[0],) + x.shape[1:])


def on_device(
    features,
    history_first,
    history_second,
    pull_list,
    pull_count,
    tile_src,
    tile_count,
    tile_values,
    w_first,
    w_second,
    bias_first,
    out_grad,
):
    dom_size = lax.axis_size("dom")
    fsdp_size = lax.axis_size("fsdp")
    me = lax.axis_index("dom") * fsdp_size + lax.axis_index("fsdp")
    rows, hidden = w_first.shape
    bias_cols = jnp.broadcast_to(bias_first[:, None], (rows, 128))
    packed = lax.all_gather(jnp.concatenate([w_first, w_second, bias_cols], axis=1), "fsdp", axis=0, tiled=True)
    first_full = packed[:, :hidden]
    second_full = packed[:, hidden : 2 * hidden]
    bias_full = packed[:, 2 * hidden].astype(jnp.float32)

    chosen = pull_list[0]
    requesters, slot_cap = chosen.shape
    counts_all = lax.all_gather(pull_count, "dom", axis=0, tiled=True)
    counts_all, chosen = lax.optimization_barrier((counts_all, chosen))
    my_counts = lax.dynamic_index_in_dim(counts_all, me, axis=1, keepdims=False)
    slot_live = (lax.broadcasted_iota(jnp.int32, (slot_cap, dom_size), 0) < my_counts[None, :]).astype(jnp.int32)
    slot_live = slot_live.reshape(-1)

    block_len = features.shape[2]
    first_cols = history_first.shape[1]
    second_cols = history_second.shape[1]
    sent_first = jnp.take(history_first, chosen.reshape(-1), axis=0, mode="clip").reshape(requesters, slot_cap, first_cols, block_len)
    sent_second = jnp.take(history_second, chosen.reshape(-1), axis=0, mode="clip").reshape(requesters, slot_cap, second_cols, block_len)
    arrived_first = lax.all_to_all(sent_first, ("dom", "fsdp"), split_axis=0, concat_axis=0, tiled=True)
    arrived_second = lax.all_to_all(sent_second, ("dom", "fsdp"), split_axis=0, concat_axis=0, tiled=True)
    pulled_first = arrived_first.reshape(dom_size, fsdp_size, slot_cap, first_cols, block_len)
    pulled_second = arrived_second.reshape(dom_size, fsdp_size, slot_cap, second_cols, block_len)

    core = lax.axis_index("dom") % 2
    pair = [(d, d ^ 1) for d in range(dom_size)]
    partner_grad = lax.ppermute(out_grad, "dom", pair)

    back_second = jnp.einsum(
        "ab,vbn->van", second_full, out_grad, preferred_element_type=jnp.float32
    ).astype(jnp.bfloat16)
    back_hidden = spread_back(back_second, tile_src, tile_count, tile_values)

    def halves(x):
        split = x.reshape(x.shape[0], fsdp_size, 2, x.shape[1] // (2 * fsdp_size), x.shape[2])
        mine = lax.dynamic_index_in_dim(split, core, axis=2, keepdims=False)
        theirs = lax.dynamic_index_in_dim(split, 1 - core, axis=2, keepdims=False)
        return mine, theirs

    agg_first = aggregate(features, pulled_first, tile_src, tile_count, slot_live, tile_values)
    pre_act = (
        jnp.einsum("fh,vfn->vhn", first_full, agg_first, preferred_element_type=jnp.float32)
        + bias_full[None, :, None]
    )
    hidden_new = gelu_tanh(pre_act).astype(jnp.bfloat16)
    _, pullback = jax.vjp(gelu_tanh, pre_act)
    back_pre = pullback(back_hidden)[0].astype(jnp.bfloat16)
    bias_term = jnp.sum(back_pre.astype(jnp.float32), axis=(0, 2))
    first_mine, first_theirs = halves(agg_first)
    first_got, back_got = lax.ppermute((first_theirs, back_pre), "dom", pair)
    first_term = jnp.einsum(
        "vprn,vhn->prh", first_mine, back_pre, preferred_element_type=jnp.float32
    ) + jnp.einsum("vprn,vhn->prh", first_got, back_got, preferred_element_type=jnp.float32)

    half_rows = first_term.shape[1]
    lanes = 128
    agg_second = aggregate(hidden_new, pulled_second, tile_src, tile_count, slot_live, tile_values)
    second_mine, second_theirs = halves(agg_second)
    second_got = lax.ppermute(second_theirs, "dom", pair)
    second_term = jnp.einsum(
        "vprn,vbn->prb", second_mine, out_grad, preferred_element_type=jnp.float32
    ) + jnp.einsum("vprn,vbn->prb", second_got, partner_grad, preferred_element_type=jnp.float32)

    bias_cols = jnp.zeros((fsdp_size, 2 * half_rows, lanes), jnp.float32)
    bias_cols = bias_cols.at[:, 0, : hidden // fsdp_size].set(bias_term.reshape(fsdp_size, hidden // fsdp_size))
    packed_terms = jnp.concatenate([jnp.concatenate([first_term, second_term], axis=1), bias_cols], axis=2)
    arrived_terms = lax.all_to_all(packed_terms.astype(jnp.bfloat16), "fsdp", split_axis=0, concat_axis=0, tiled=True)
    shard = jnp.sum(arrived_terms.astype(jnp.float32), axis=0)
    for flip in (2, 4):
        shard = shard + lax.ppermute(shard, "dom", [(d, d ^ flip) for d in range(dom_size)])
    other = lax.ppermute(shard, "dom", pair)
    low = jnp.where(core == 0, shard, other)
    high = jnp.where(core == 0, other, shard)
    first_total = jnp.concatenate([low[:half_rows, :hidden], high[:half_rows, :hidden]], axis=0)
    second_total = jnp.concatenate([low[half_rows:, :hidden], high[half_rows:, :hidden]], axis=0)
    bias_total = (shard + other)[0, hidden : hidden + hidden // fsdp_size]
    return (hidden_new, first_total, second_total, bias_total)


def solution(mesh):
    return jax.shard_map(
        on_device,
        mesh=mesh,
        in_specs=(
            P(("dom", "fsdp"), None, None),
            P("dom", "fsdp", None),
            P("dom", "fsdp", None),
            P("dom", None, None),
            P("dom", None),
            P(("dom", "fsdp"), None),
            P(("dom", "fsdp")),
            P(("dom", "fsdp"), None, None, None),
            P("fsdp", None),
            P("fsdp", None),
            P("fsdp"),
            P(("dom", "fsdp"), None, None),
        ),
        out_specs=(P(("dom", "fsdp"), None, None), P("fsdp", None), P("fsdp", None), P("fsdp")),
        check_vma=False,
    )
```

```python
import functools

import jax
import jax.numpy as jnp
from jax import lax
from jax.experimental import pallas as pl
from jax.experimental.pallas import tpu as pltpu
from jax.sharding import PartitionSpec as P


def gelu_tanh(inputs):
    return jax.nn.gelu(inputs, approximate=True)


def _agg_kernel(own_count, last_step, per, src_ref, cnt_ref, live_ref, *refs):
    own_refs, pulled_refs = refs[:per], refs[per : 2 * per]
    tile_ref, out_ref, acc_ref = refs[2 * per :]
    v = pl.program_id(0)
    k = pl.program_id(1)

    @pl.when(k == 0)
    def _():
        acc_ref[...] = jnp.zeros_like(acc_ref)

    for j, own_ref, pulled_ref in zip(range(per), own_refs, pulled_refs):
        t = per * k + j
        src = src_ref[v, t]
        tile_live = t < cnt_ref[v]
        own_ok = tile_live & (src < own_count)
        pull_ok = tile_live & (src >= own_count) & (live_ref[jnp.maximum(src - own_count, 0)] > 0)

        @pl.when(own_ok)
        def _():
            acc_ref[...] += jnp.dot(own_ref[0], tile_ref[0, j], preferred_element_type=jnp.float32)

        @pl.when(pull_ok)
        def _():
            block = pulled_ref[0, :, 0]
            block = block.reshape(block.shape[0] * block.shape[1], block.shape[2])
            acc_ref[...] += jnp.dot(block, tile_ref[0, j], preferred_element_type=jnp.float32)

    @pl.when(k == last_step)
    def _():
        out_ref[0] = acc_ref[...].astype(out_ref.dtype)


def aggregate(own, pulled, tile_src, tile_count, slot_live, tile_values):
    nb, feat, blk = own.shape
    dom, fsdp, cap = pulled.shape[0], pulled.shape[1], pulled.shape[2]
    tiles = tile_src.shape[1]
    per = tiles
    steps = tiles // per

    def eff(v, t, cnt_ref):
        return jnp.minimum(t, cnt_ref[v] - 1)

    def own_map(j):
        def index(v, k, src_ref, cnt_ref, live_ref):
            s = src_ref[v, eff(v, per * k + j, cnt_ref)]
            return (jnp.clip(s, 0, nb - 1), 0, 0)

        return index

    def pulled_map(j):
        def index(v, k, src_ref, cnt_ref, live_ref):
            s = jnp.clip(src_ref[v, eff(v, per * k + j, cnt_ref)] - nb, 0, cap * dom - 1)
            return (s % dom, 0, s // dom, 0, 0)

        return index

    grid_spec = pltpu.PrefetchScalarGridSpec(
        num_scalar_prefetch=3,
        grid=(nb, steps),
        in_specs=[pl.BlockSpec((1, feat, blk), own_map(j)) for j in range(per)]
        + [pl.BlockSpec((1, fsdp, 1) + pulled.shape[3:], pulled_map(j)) for j in range(per)]
        + [pl.BlockSpec((1, per, blk, blk), lambda v, k, s, c, l: (v, k, 0, 0))],
        out_specs=pl.BlockSpec((1, feat, blk), lambda v, k, s, c, l: (v, 0, 0)),
        scratch_shapes=[pltpu.VMEM((feat, blk), jnp.float32)],
    )
    flops = 2 * nb * tiles * feat * blk * blk
    return pl.pallas_call(
        functools.partial(_agg_kernel, nb, steps - 1, per),
        grid_spec=grid_spec,
        out_shape=jax.ShapeDtypeStruct(own.shape, jnp.bfloat16),
        compiler_params=pltpu.CompilerParams(dimension_semantics=("arbitrary", "arbitrary")),
        cost_estimate=pl.CostEstimate(
            flops=flops, transcendentals=0, bytes_accessed=nb * tiles * (2 * feat * blk * 2 + blk * blk * 2) + own.size * 2
        ),
    )(tile_src, tile_count, slot_live, *([own] * per), *([pulled] * per), tile_values)


def _spread_kernel(own_count, src_ref, cnt_ref, back_ref, tile_ref, out_ref):
    v = pl.program_id(0)
    t = pl.program_id(1)

    @pl.when((v == 0) & (t == 0))
    def _():
        out_ref[...] = jnp.zeros_like(out_ref)

    src = src_ref[v, t]

    @pl.when((t < cnt_ref[v]) & (src < own_count))
    def _():
        term = lax.dot_general(
            back_ref[0], tile_ref[0, 0], (((1,), (1,)), ((), ())), preferred_element_type=jnp.float32
        )
        out_ref[src] = out_ref[src] + term


def spread_back(back_second, tile_src, tile_count, tile_values):
    nb, width, blk = back_second.shape
    tiles = tile_src.shape[1]

    def eff(v, t, cnt_ref):
        return jnp.minimum(t, cnt_ref[v] - 1)

    grid_spec = pltpu.PrefetchScalarGridSpec(
        num_scalar_prefetch=2,
        grid=(nb, tiles),
        in_specs=[
            pl.BlockSpec((1, width, blk), lambda v, t, s, c: (v, 0, 0)),
            pl.BlockSpec((1, 1, blk, blk), lambda v, t, s, c: (v, eff(v, t, c), 0, 0)),
        ],
        out_specs=pl.BlockSpec((nb, width, blk), lambda v, t, s, c: (0, 0, 0)),
    )
    return pl.pallas_call(
        functools.partial(_spread_kernel, nb),
        grid_spec=grid_spec,
        out_shape=jax.ShapeDtypeStruct(back_second.shape, jnp.float32),
        compiler_params=pltpu.CompilerParams(dimension_semantics=("arbitrary", "arbitrary")),
        cost_estimate=pl.CostEstimate(
            flops=2 * nb * tiles * width * blk * blk,
            transcendentals=0,
            bytes_accessed=back_second.size * 2 + nb * tiles * blk * blk * 2 + back_second.size * 4,
        ),
    )(tile_src, tile_count, back_second, tile_values)


def gather_rows(x, axis):
    n = lax.axis_size(axis)
    spread = lax.all_to_all(jnp.broadcast_to(x[None], (n,) + x.shape), axis, split_axis=0, concat_axis=0, tiled=True)
    return spread.reshape((n * x.shape[0],) + x.shape[1:])


def on_device(
    features,
    history_first,
    history_second,
    pull_list,
    pull_count,
    tile_src,
    tile_count,
    tile_values,
    w_first,
    w_second,
    bias_first,
    out_grad,
):
    dom_size = lax.axis_size("dom")
    fsdp_size = lax.axis_size("fsdp")
    me = lax.axis_index("dom") * fsdp_size + lax.axis_index("fsdp")
    rows, hidden = w_first.shape
    bias_cols = jnp.broadcast_to(bias_first[:, None], (rows, 128))
    packed = lax.all_gather(jnp.concatenate([w_first, w_second, bias_cols], axis=1), "fsdp", axis=0, tiled=True)
    first_full = packed[:, :hidden]
    second_full = packed[:, hidden : 2 * hidden]
    bias_full = packed[:, 2 * hidden].astype(jnp.float32)

    chosen = pull_list[0]
    requesters, slot_cap = chosen.shape
    counts_all = lax.all_gather(pull_count, "dom", axis=0, tiled=True)
    counts_all, chosen = lax.optimization_barrier((counts_all, chosen))
    my_counts = lax.dynamic_index_in_dim(counts_all, me, axis=1, keepdims=False)
    slot_live = (lax.broadcasted_iota(jnp.int32, (slot_cap, dom_size), 0) < my_counts[None, :]).astype(jnp.int32)
    slot_live = slot_live.reshape(-1)

    block_len = features.shape[2]
    first_cols = history_first.shape[1]
    second_cols = history_second.shape[1]
    sent_first = jnp.take(history_first, chosen.reshape(-1), axis=0, mode="clip").reshape(requesters, slot_cap, first_cols, block_len)
    sent_second = jnp.take(history_second, chosen.reshape(-1), axis=0, mode="clip").reshape(requesters, slot_cap, second_cols, block_len)
    arrived_first = lax.all_to_all(sent_first, ("dom", "fsdp"), split_axis=0, concat_axis=0, tiled=True)
    arrived_second = lax.all_to_all(sent_second, ("dom", "fsdp"), split_axis=0, concat_axis=0, tiled=True)
    pulled_first = arrived_first.reshape(dom_size, fsdp_size, slot_cap, first_cols, block_len)
    pulled_second = arrived_second.reshape(dom_size, fsdp_size, slot_cap, second_cols, block_len)

    core = lax.axis_index("dom") % 2
    pair = [(d, d ^ 1) for d in range(dom_size)]
    partner_grad = lax.ppermute(out_grad, "dom", pair)

    back_second = jnp.einsum(
        "ab,vbn->van", second_full, out_grad, preferred_element_type=jnp.float32
    ).astype(jnp.bfloat16)
    back_hidden = spread_back(back_second, tile_src, tile_count, tile_values)

    def halves(x):
        split = x.reshape(x.shape[0], fsdp_size, 2, x.shape[1] // (2 * fsdp_size), x.shape[2])
        mine = lax.dynamic_index_in_dim(split, core, axis=2, keepdims=False)
        theirs = lax.dynamic_index_in_dim(split, 1 - core, axis=2, keepdims=False)
        return mine, theirs

    agg_first = aggregate(features, pulled_first, tile_src, tile_count, slot_live, tile_values)
    pre_act = (
        jnp.einsum("fh,vfn->vhn", first_full, agg_first, preferred_element_type=jnp.float32)
        + bias_full[None, :, None]
    )
    hidden_new = gelu_tanh(pre_act).astype(jnp.bfloat16)
    _, pullback = jax.vjp(gelu_tanh, pre_act)
    back_pre = pullback(back_hidden)[0].astype(jnp.bfloat16)
    bias_term = jnp.sum(back_pre.astype(jnp.float32), axis=(0, 2))
    first_mine, first_theirs = halves(agg_first)
    first_got, back_got = lax.ppermute((first_theirs, back_pre), "dom", pair)
    first_term = jnp.einsum(
        "vprn,vhn->prh", first_mine, back_pre, preferred_element_type=jnp.float32
    ) + jnp.einsum("vprn,vhn->prh", first_got, back_got, preferred_element_type=jnp.float32)

    half_rows = first_term.shape[1]
    lanes = 128
    agg_second = aggregate(hidden_new, pulled_second, tile_src, tile_count, slot_live, tile_values)
    second_mine, second_theirs = halves(agg_second)
    second_got = lax.ppermute(second_theirs, "dom", pair)
    second_term = jnp.einsum(
        "vprn,vbn->prb", second_mine, out_grad, preferred_element_type=jnp.float32
    ) + jnp.einsum("vprn,vbn->prb", second_got, partner_grad, preferred_element_type=jnp.float32)

    bias_cols = jnp.zeros((fsdp_size, 2 * half_rows, lanes), jnp.float32)
    bias_cols = bias_cols.at[:, 0, : hidden // fsdp_size].set(bias_term.reshape(fsdp_size, hidden // fsdp_size))
    packed_terms = jnp.concatenate([jnp.concatenate([first_term, second_term], axis=1), bias_cols], axis=2)
    arrived_terms = lax.all_to_all(packed_terms.astype(jnp.bfloat16), "fsdp", split_axis=0, concat_axis=0, tiled=True)
    shard = jnp.sum(arrived_terms.astype(jnp.float32), axis=0)
    for flip in (2, 4):
        shard = shard + lax.ppermute(shard, "dom", [(d, d ^ flip) for d in range(dom_size)])
    other = lax.ppermute(shard, "dom", pair)
    low = jnp.where(core == 0, shard, other)
    high = jnp.where(core == 0, other, shard)
    first_total = jnp.concatenate([low[:half_rows, :hidden], high[:half_rows, :hidden]], axis=0)
    second_total = jnp.concatenate([low[half_rows:, :hidden], high[half_rows:, :hidden]], axis=0)
    bias_total = (shard + other)[0, hidden : hidden + hidden // fsdp_size]
    return (hidden_new, first_total, second_total, bias_total)


def solution(mesh):
    return jax.shard_map(
        on_device,
        mesh=mesh,
        in_specs=(
            P(("dom", "fsdp"), None, None),
            P("dom", "fsdp", None),
            P("dom", "fsdp", None),
            P("dom", None, None),
            P("dom", None),
            P(("dom", "fsdp"), None),
            P(("dom", "fsdp")),
            P(("dom", "fsdp"), None, None, None),
            P("fsdp", None),
            P("fsdp", None),
            P("fsdp"),
            P(("dom", "fsdp"), None, None),
        ),
        out_specs=(P(("dom", "fsdp"), None, None), P("fsdp", None), P("fsdp", None), P("fsdp")),
        check_vma=False,
    )
```

```python
import functools

import jax
import jax.numpy as jnp
from jax import lax
from jax.experimental import pallas as pl
from jax.experimental.pallas import tpu as pltpu
from jax.sharding import PartitionSpec as P


def gelu_tanh(inputs):
    return jax.nn.gelu(inputs, approximate=True)


def _agg_kernel(own_count, last_step, per, src_ref, cnt_ref, live_ref, own_ref, *refs):
    pulled_refs = refs[:per]
    tile_ref, out_ref, acc_ref = refs[per:]
    v = pl.program_id(0)
    k = pl.program_id(1)

    @pl.when(k == 0)
    def _():
        acc_ref[...] = jnp.zeros_like(acc_ref)

    for j, pulled_ref in zip(range(per), pulled_refs):
        t = per * k + j
        src = src_ref[v, t]
        tile_live = t < cnt_ref[v]
        own_ok = tile_live & (src < own_count)
        pull_ok = tile_live & (src >= own_count) & (live_ref[jnp.maximum(src - own_count, 0)] > 0)

        @pl.when(own_ok)
        def _():
            acc_ref[...] += jnp.dot(
                own_ref[jnp.clip(src, 0, own_count - 1)], tile_ref[0, j], preferred_element_type=jnp.float32
            )

        @pl.when(pull_ok)
        def _():
            block = pulled_ref[0, :, 0]
            block = block.reshape(block.shape[0] * block.shape[1], block.shape[2])
            acc_ref[...] += jnp.dot(block, tile_ref[0, j], preferred_element_type=jnp.float32)

    @pl.when(k == last_step)
    def _():
        out_ref[0] = acc_ref[...].astype(out_ref.dtype)


def aggregate(own, pulled, tile_src, tile_count, slot_live, tile_values):
    nb, feat, blk = own.shape
    dom, fsdp, cap = pulled.shape[0], pulled.shape[1], pulled.shape[2]
    tiles = tile_src.shape[1]
    per = tiles
    steps = tiles // per

    def eff(v, t, cnt_ref):
        return jnp.minimum(t, cnt_ref[v] - 1)

    def pulled_map(j):
        def index(v, k, src_ref, cnt_ref, live_ref):
            s = jnp.clip(src_ref[v, eff(v, per * k + j, cnt_ref)] - nb, 0, cap * dom - 1)
            return (s % dom, 0, s // dom, 0, 0)

        return index

    grid_spec = pltpu.PrefetchScalarGridSpec(
        num_scalar_prefetch=3,
        grid=(nb, steps),
        in_specs=[pl.BlockSpec((nb, feat, blk), lambda v, k, s, c, l: (0, 0, 0))]
        + [pl.BlockSpec((1, fsdp, 1) + pulled.shape[3:], pulled_map(j)) for j in range(per)]
        + [pl.BlockSpec((1, per, blk, blk), lambda v, k, s, c, l: (v, k, 0, 0))],
        out_specs=pl.BlockSpec((1, feat, blk), lambda v, k, s, c, l: (v, 0, 0)),
        scratch_shapes=[pltpu.VMEM((feat, blk), jnp.float32)],
    )
    flops = 2 * nb * tiles * feat * blk * blk
    return pl.pallas_call(
        functools.partial(_agg_kernel, nb, steps - 1, per),
        grid_spec=grid_spec,
        out_shape=jax.ShapeDtypeStruct(own.shape, jnp.bfloat16),
        compiler_params=pltpu.CompilerParams(dimension_semantics=("arbitrary", "arbitrary")),
        cost_estimate=pl.CostEstimate(
            flops=flops, transcendentals=0, bytes_accessed=nb * tiles * (2 * feat * blk * 2 + blk * blk * 2) + own.size * 2
        ),
    )(tile_src, tile_count, slot_live, own, *([pulled] * per), tile_values)


def _spread_kernel(own_count, src_ref, cnt_ref, back_ref, tile_ref, out_ref):
    v = pl.program_id(0)
    t = pl.program_id(1)

    @pl.when((v == 0) & (t == 0))
    def _():
        out_ref[...] = jnp.zeros_like(out_ref)

    src = src_ref[v, t]

    @pl.when((t < cnt_ref[v]) & (src < own_count))
    def _():
        term = lax.dot_general(
            back_ref[0], tile_ref[0, 0], (((1,), (1,)), ((), ())), preferred_element_type=jnp.float32
        )
        out_ref[src] = out_ref[src] + term


def spread_back(back_second, tile_src, tile_count, tile_values):
    nb, width, blk = back_second.shape
    tiles = tile_src.shape[1]

    def eff(v, t, cnt_ref):
        return jnp.minimum(t, cnt_ref[v] - 1)

    grid_spec = pltpu.PrefetchScalarGridSpec(
        num_scalar_prefetch=2,
        grid=(nb, tiles),
        in_specs=[
            pl.BlockSpec((1, width, blk), lambda v, t, s, c: (v, 0, 0)),
            pl.BlockSpec((1, 1, blk, blk), lambda v, t, s, c: (v, eff(v, t, c), 0, 0)),
        ],
        out_specs=pl.BlockSpec((nb, width, blk), lambda v, t, s, c: (0, 0, 0)),
    )
    return pl.pallas_call(
        functools.partial(_spread_kernel, nb),
        grid_spec=grid_spec,
        out_shape=jax.ShapeDtypeStruct(back_second.shape, jnp.float32),
        compiler_params=pltpu.CompilerParams(dimension_semantics=("arbitrary", "arbitrary")),
        cost_estimate=pl.CostEstimate(
            flops=2 * nb * tiles * width * blk * blk,
            transcendentals=0,
            bytes_accessed=back_second.size * 2 + nb * tiles * blk * blk * 2 + back_second.size * 4,
        ),
    )(tile_src, tile_count, back_second, tile_values)


def gather_rows(x, axis):
    n = lax.axis_size(axis)
    spread = lax.all_to_all(jnp.broadcast_to(x[None], (n,) + x.shape), axis, split_axis=0, concat_axis=0, tiled=True)
    return spread.reshape((n * x.shape[0],) + x.shape[1:])


def on_device(
    features,
    history_first,
    history_second,
    pull_list,
    pull_count,
    tile_src,
    tile_count,
    tile_values,
    w_first,
    w_second,
    bias_first,
    out_grad,
):
    dom_size = lax.axis_size("dom")
    fsdp_size = lax.axis_size("fsdp")
    me = lax.axis_index("dom") * fsdp_size + lax.axis_index("fsdp")
    rows, hidden = w_first.shape
    bias_cols = jnp.broadcast_to(bias_first[:, None], (rows, 128))
    packed = lax.all_gather(jnp.concatenate([w_first, w_second, bias_cols], axis=1), "fsdp", axis=0, tiled=True)
    first_full = packed[:, :hidden]
    second_full = packed[:, hidden : 2 * hidden]
    bias_full = packed[:, 2 * hidden].astype(jnp.float32)

    chosen = pull_list[0]
    requesters, slot_cap = chosen.shape
    counts_all = lax.all_gather(pull_count, "dom", axis=0, tiled=True)
    counts_all, chosen = lax.optimization_barrier((counts_all, chosen))
    my_counts = lax.dynamic_index_in_dim(counts_all, me, axis=1, keepdims=False)
    slot_live = (lax.broadcasted_iota(jnp.int32, (slot_cap, dom_size), 0) < my_counts[None, :]).astype(jnp.int32)
    slot_live = slot_live.reshape(-1)

    block_len = features.shape[2]
    first_cols = history_first.shape[1]
    second_cols = history_second.shape[1]
    sent_first = jnp.take(history_first, chosen.reshape(-1), axis=0, mode="clip").reshape(requesters, slot_cap, first_cols, block_len)
    sent_second = jnp.take(history_second, chosen.reshape(-1), axis=0, mode="clip").reshape(requesters, slot_cap, second_cols, block_len)
    arrived_first = lax.all_to_all(sent_first, ("dom", "fsdp"), split_axis=0, concat_axis=0, tiled=True)
    arrived_second = lax.all_to_all(sent_second, ("dom", "fsdp"), split_axis=0, concat_axis=0, tiled=True)
    pulled_first = arrived_first.reshape(dom_size, fsdp_size, slot_cap, first_cols, block_len)
    pulled_second = arrived_second.reshape(dom_size, fsdp_size, slot_cap, second_cols, block_len)

    core = lax.axis_index("dom") % 2
    pair = [(d, d ^ 1) for d in range(dom_size)]
    partner_grad = lax.ppermute(out_grad, "dom", pair)

    back_second = jnp.einsum(
        "ab,vbn->van", second_full, out_grad, preferred_element_type=jnp.float32
    ).astype(jnp.bfloat16)
    back_hidden = spread_back(back_second, tile_src, tile_count, tile_values)

    def halves(x):
        split = x.reshape(x.shape[0], fsdp_size, 2, x.shape[1] // (2 * fsdp_size), x.shape[2])
        mine = lax.dynamic_index_in_dim(split, core, axis=2, keepdims=False)
        theirs = lax.dynamic_index_in_dim(split, 1 - core, axis=2, keepdims=False)
        return mine, theirs

    agg_first = aggregate(features, pulled_first, tile_src, tile_count, slot_live, tile_values)
    pre_act = (
        jnp.einsum("fh,vfn->vhn", first_full, agg_first, preferred_element_type=jnp.float32)
        + bias_full[None, :, None]
    )
    hidden_new = gelu_tanh(pre_act).astype(jnp.bfloat16)
    _, pullback = jax.vjp(gelu_tanh, pre_act)
    back_pre = pullback(back_hidden)[0].astype(jnp.bfloat16)
    bias_term = jnp.sum(back_pre.astype(jnp.float32), axis=(0, 2))
    first_mine, first_theirs = halves(agg_first)
    first_got, back_got = lax.ppermute((first_theirs, back_pre), "dom", pair)
    first_term = jnp.einsum(
        "vprn,vhn->prh", first_mine, back_pre, preferred_element_type=jnp.float32
    ) + jnp.einsum("vprn,vhn->prh", first_got, back_got, preferred_element_type=jnp.float32)

    half_rows = first_term.shape[1]
    lanes = 128
    agg_second = aggregate(hidden_new, pulled_second, tile_src, tile_count, slot_live, tile_values)
    second_mine, second_theirs = halves(agg_second)
    second_got = lax.ppermute(second_theirs, "dom", pair)
    second_term = jnp.einsum(
        "vprn,vbn->prb", second_mine, out_grad, preferred_element_type=jnp.float32
    ) + jnp.einsum("vprn,vbn->prb", second_got, partner_grad, preferred_element_type=jnp.float32)

    bias_cols = jnp.zeros((fsdp_size, 2 * half_rows, lanes), jnp.float32)
    bias_cols = bias_cols.at[:, 0, : hidden // fsdp_size].set(bias_term.reshape(fsdp_size, hidden // fsdp_size))
    packed_terms = jnp.concatenate([jnp.concatenate([first_term, second_term], axis=1), bias_cols], axis=2)
    arrived_terms = lax.all_to_all(packed_terms.astype(jnp.bfloat16), "fsdp", split_axis=0, concat_axis=0, tiled=True)
    shard = jnp.sum(arrived_terms.astype(jnp.float32), axis=0)
    for flip in (2, 4):
        shard = shard + lax.ppermute(shard, "dom", [(d, d ^ flip) for d in range(dom_size)])
    other = lax.ppermute(shard, "dom", pair)
    low = jnp.where(core == 0, shard, other)
    high = jnp.where(core == 0, other, shard)
    first_total = jnp.concatenate([low[:half_rows, :hidden], high[:half_rows, :hidden]], axis=0)
    second_total = jnp.concatenate([low[half_rows:, :hidden], high[half_rows:, :hidden]], axis=0)
    bias_total = (shard + other)[0, hidden : hidden + hidden // fsdp_size]
    return (hidden_new, first_total, second_total, bias_total)


def solution(mesh):
    return jax.shard_map(
        on_device,
        mesh=mesh,
        in_specs=(
            P(("dom", "fsdp"), None, None),
            P("dom", "fsdp", None),
            P("dom", "fsdp", None),
            P("dom", None, None),
            P("dom", None),
            P(("dom", "fsdp"), None),
            P(("dom", "fsdp")),
            P(("dom", "fsdp"), None, None, None),
            P("fsdp", None),
            P("fsdp", None),
            P("fsdp"),
            P(("dom", "fsdp"), None, None),
        ),
        out_specs=(P(("dom", "fsdp"), None, None), P("fsdp", None), P("fsdp", None), P("fsdp")),
        check_vma=False,
    )
```

```python
import functools

import jax
import jax.numpy as jnp
from jax import lax
from jax.experimental import pallas as pl
from jax.experimental.pallas import tpu as pltpu
from jax.sharding import PartitionSpec as P


def gelu_tanh(inputs):
    return jax.nn.gelu(inputs, approximate=True)


def _agg_kernel(own_count, last_step, per, src_ref, cnt_ref, live_ref, own_ref, *refs):
    pulled_refs = refs[:per]
    tile_ref, out_ref, acc_ref = refs[per:]
    v = pl.program_id(0)
    k = pl.program_id(1)

    @pl.when(k == 0)
    def _():
        acc_ref[...] = jnp.zeros_like(acc_ref)

    for j, pulled_ref in zip(range(per), pulled_refs):
        t = per * k + j
        src = src_ref[v, t]
        tile_live = t < cnt_ref[v]
        own_ok = tile_live & (src < own_count)
        pull_ok = tile_live & (src >= own_count) & (live_ref[jnp.maximum(src - own_count, 0)] > 0)

        @pl.when(own_ok)
        def _():
            acc_ref[...] += jnp.dot(
                own_ref[jnp.clip(src, 0, own_count - 1)], tile_ref[0, j], preferred_element_type=jnp.float32
            )

        @pl.when(pull_ok)
        def _():
            block = pulled_ref[0, :, 0]
            block = block.reshape(block.shape[0] * block.shape[1], block.shape[2])
            acc_ref[...] += jnp.dot(block, tile_ref[0, j], preferred_element_type=jnp.float32)

    @pl.when(k == last_step)
    def _():
        out_ref[0] = acc_ref[...].astype(out_ref.dtype)


def aggregate(own, pulled, tile_src, tile_count, slot_live, tile_values):
    nb, feat, blk = own.shape
    dom, fsdp, cap = pulled.shape[0], pulled.shape[1], pulled.shape[2]
    tiles = tile_src.shape[1]
    per = tiles
    steps = tiles // per

    def eff(v, t, cnt_ref):
        return jnp.minimum(t, cnt_ref[v] - 1)

    def pulled_map(j):
        def index(v, k, src_ref, cnt_ref, live_ref):
            t = per * k + j
            pick = jnp.int32(0)
            for earlier in range(nb):
                s = src_ref[earlier, t]
                use = (earlier <= v) & (t < cnt_ref[earlier]) & (s >= nb)
                pick = jnp.where(use, s - nb, pick)
            pick = jnp.clip(pick, 0, cap * dom - 1)
            return (pick % dom, 0, pick // dom, 0, 0)

        return index

    grid_spec = pltpu.PrefetchScalarGridSpec(
        num_scalar_prefetch=3,
        grid=(nb, steps),
        in_specs=[pl.BlockSpec((nb, feat, blk), lambda v, k, s, c, l: (0, 0, 0))]
        + [pl.BlockSpec((1, fsdp, 1) + pulled.shape[3:], pulled_map(j)) for j in range(per)]
        + [pl.BlockSpec((1, per, blk, blk), lambda v, k, s, c, l: (v, k, 0, 0))],
        out_specs=pl.BlockSpec((1, feat, blk), lambda v, k, s, c, l: (v, 0, 0)),
        scratch_shapes=[pltpu.VMEM((feat, blk), jnp.float32)],
    )
    flops = 2 * nb * tiles * feat * blk * blk
    return pl.pallas_call(
        functools.partial(_agg_kernel, nb, steps - 1, per),
        grid_spec=grid_spec,
        out_shape=jax.ShapeDtypeStruct(own.shape, jnp.bfloat16),
        compiler_params=pltpu.CompilerParams(dimension_semantics=("arbitrary", "arbitrary")),
        cost_estimate=pl.CostEstimate(
            flops=flops, transcendentals=0, bytes_accessed=nb * tiles * (2 * feat * blk * 2 + blk * blk * 2) + own.size * 2
        ),
    )(tile_src, tile_count, slot_live, own, *([pulled] * per), tile_values)


def _spread_kernel(own_count, src_ref, cnt_ref, back_ref, tile_ref, out_ref):
    v = pl.program_id(0)
    t = pl.program_id(1)

    @pl.when((v == 0) & (t == 0))
    def _():
        out_ref[...] = jnp.zeros_like(out_ref)

    src = src_ref[v, t]

    @pl.when((t < cnt_ref[v]) & (src < own_count))
    def _():
        term = lax.dot_general(
            back_ref[0], tile_ref[0, 0], (((1,), (1,)), ((), ())), preferred_element_type=jnp.float32
        )
        out_ref[src] = out_ref[src] + term


def spread_back(back_second, tile_src, tile_count, tile_values):
    nb, width, blk = back_second.shape
    tiles = tile_src.shape[1]

    def eff(v, t, cnt_ref):
        return jnp.minimum(t, cnt_ref[v] - 1)

    grid_spec = pltpu.PrefetchScalarGridSpec(
        num_scalar_prefetch=2,
        grid=(nb, tiles),
        in_specs=[
            pl.BlockSpec((1, width, blk), lambda v, t, s, c: (v, 0, 0)),
            pl.BlockSpec((1, 1, blk, blk), lambda v, t, s, c: (v, eff(v, t, c), 0, 0)),
        ],
        out_specs=pl.BlockSpec((nb, width, blk), lambda v, t, s, c: (0, 0, 0)),
    )
    return pl.pallas_call(
        functools.partial(_spread_kernel, nb),
        grid_spec=grid_spec,
        out_shape=jax.ShapeDtypeStruct(back_second.shape, jnp.float32),
        compiler_params=pltpu.CompilerParams(dimension_semantics=("arbitrary", "arbitrary")),
        cost_estimate=pl.CostEstimate(
            flops=2 * nb * tiles * width * blk * blk,
            transcendentals=0,
            bytes_accessed=back_second.size * 2 + nb * tiles * blk * blk * 2 + back_second.size * 4,
        ),
    )(tile_src, tile_count, back_second, tile_values)


def gather_rows(x, axis):
    n = lax.axis_size(axis)
    spread = lax.all_to_all(jnp.broadcast_to(x[None], (n,) + x.shape), axis, split_axis=0, concat_axis=0, tiled=True)
    return spread.reshape((n * x.shape[0],) + x.shape[1:])


def on_device(
    features,
    history_first,
    history_second,
    pull_list,
    pull_count,
    tile_src,
    tile_count,
    tile_values,
    w_first,
    w_second,
    bias_first,
    out_grad,
):
    dom_size = lax.axis_size("dom")
    fsdp_size = lax.axis_size("fsdp")
    me = lax.axis_index("dom") * fsdp_size + lax.axis_index("fsdp")
    rows, hidden = w_first.shape
    bias_cols = jnp.broadcast_to(bias_first[:, None], (rows, 128))
    packed = lax.all_gather(jnp.concatenate([w_first, w_second, bias_cols], axis=1), "fsdp", axis=0, tiled=True)
    first_full = packed[:, :hidden]
    second_full = packed[:, hidden : 2 * hidden]
    bias_full = packed[:, 2 * hidden].astype(jnp.float32)

    chosen = pull_list[0]
    requesters, slot_cap = chosen.shape
    counts_all = lax.all_gather(pull_count, "dom", axis=0, tiled=True)
    counts_all, chosen = lax.optimization_barrier((counts_all, chosen))
    my_counts = lax.dynamic_index_in_dim(counts_all, me, axis=1, keepdims=False)
    slot_live = (lax.broadcasted_iota(jnp.int32, (slot_cap, dom_size), 0) < my_counts[None, :]).astype(jnp.int32)
    slot_live = slot_live.reshape(-1)

    block_len = features.shape[2]
    first_cols = history_first.shape[1]
    second_cols = history_second.shape[1]
    sent_first = jnp.take(history_first, chosen.reshape(-1), axis=0, mode="clip").reshape(requesters, slot_cap, first_cols, block_len)
    sent_second = jnp.take(history_second, chosen.reshape(-1), axis=0, mode="clip").reshape(requesters, slot_cap, second_cols, block_len)
    arrived_first = lax.all_to_all(sent_first, ("dom", "fsdp"), split_axis=0, concat_axis=0, tiled=True)
    arrived_second = lax.all_to_all(sent_second, ("dom", "fsdp"), split_axis=0, concat_axis=0, tiled=True)
    pulled_first = arrived_first.reshape(dom_size, fsdp_size, slot_cap, first_cols, block_len)
    pulled_second = arrived_second.reshape(dom_size, fsdp_size, slot_cap, second_cols, block_len)

    core = lax.axis_index("dom") % 2
    pair = [(d, d ^ 1) for d in range(dom_size)]
    partner_grad = lax.ppermute(out_grad, "dom", pair)

    back_second = jnp.einsum(
        "ab,vbn->van", second_full, out_grad, preferred_element_type=jnp.float32
    ).astype(jnp.bfloat16)
    back_hidden = spread_back(back_second, tile_src, tile_count, tile_values)

    def halves(x):
        split = x.reshape(x.shape[0], fsdp_size, 2, x.shape[1] // (2 * fsdp_size), x.shape[2])
        mine = lax.dynamic_index_in_dim(split, core, axis=2, keepdims=False)
        theirs = lax.dynamic_index_in_dim(split, 1 - core, axis=2, keepdims=False)
        return mine, theirs

    agg_first = aggregate(features, pulled_first, tile_src, tile_count, slot_live, tile_values)
    pre_act = (
        jnp.einsum("fh,vfn->vhn", first_full, agg_first, preferred_element_type=jnp.float32)
        + bias_full[None, :, None]
    )
    hidden_new = gelu_tanh(pre_act).astype(jnp.bfloat16)
    _, pullback = jax.vjp(gelu_tanh, pre_act)
    back_pre = pullback(back_hidden)[0].astype(jnp.bfloat16)
    bias_term = jnp.sum(back_pre.astype(jnp.float32), axis=(0, 2))
    first_mine, first_theirs = halves(agg_first)
    first_got, back_got = lax.ppermute((first_theirs, back_pre), "dom", pair)
    first_term = jnp.einsum(
        "vprn,vhn->prh", first_mine, back_pre, preferred_element_type=jnp.float32
    ) + jnp.einsum("vprn,vhn->prh", first_got, back_got, preferred_element_type=jnp.float32)

    half_rows = first_term.shape[1]
    lanes = 128
    agg_second = aggregate(hidden_new, pulled_second, tile_src, tile_count, slot_live, tile_values)
    second_mine, second_theirs = halves(agg_second)
    second_got = lax.ppermute(second_theirs, "dom", pair)
    second_term = jnp.einsum(
        "vprn,vbn->prb", second_mine, out_grad, preferred_element_type=jnp.float32
    ) + jnp.einsum("vprn,vbn->prb", second_got, partner_grad, preferred_element_type=jnp.float32)

    bias_cols = jnp.zeros((fsdp_size, 2 * half_rows, lanes), jnp.float32)
    bias_cols = bias_cols.at[:, 0, : hidden // fsdp_size].set(bias_term.reshape(fsdp_size, hidden // fsdp_size))
    packed_terms = jnp.concatenate([jnp.concatenate([first_term, second_term], axis=1), bias_cols], axis=2)
    arrived_terms = lax.all_to_all(packed_terms.astype(jnp.bfloat16), "fsdp", split_axis=0, concat_axis=0, tiled=True)
    shard = jnp.sum(arrived_terms.astype(jnp.float32), axis=0)
    for flip in (2, 4):
        shard = shard + lax.ppermute(shard, "dom", [(d, d ^ flip) for d in range(dom_size)])
    other = lax.ppermute(shard, "dom", pair)
    low = jnp.where(core == 0, shard, other)
    high = jnp.where(core == 0, other, shard)
    first_total = jnp.concatenate([low[:half_rows, :hidden], high[:half_rows, :hidden]], axis=0)
    second_total = jnp.concatenate([low[half_rows:, :hidden], high[half_rows:, :hidden]], axis=0)
    bias_total = (shard + other)[0, hidden : hidden + hidden // fsdp_size]
    return (hidden_new, first_total, second_total, bias_total)


def solution(mesh):
    return jax.shard_map(
        on_device,
        mesh=mesh,
        in_specs=(
            P(("dom", "fsdp"), None, None),
            P("dom", "fsdp", None),
            P("dom", "fsdp", None),
            P("dom", None, None),
            P("dom", None),
            P(("dom", "fsdp"), None),
            P(("dom", "fsdp")),
            P(("dom", "fsdp"), None, None, None),
            P("fsdp", None),
            P("fsdp", None),
            P("fsdp"),
            P(("dom", "fsdp"), None, None),
        ),
        out_specs=(P(("dom", "fsdp"), None, None), P("fsdp", None), P("fsdp", None), P("fsdp")),
        check_vma=False,
    )
```

```python
import functools

import jax
import jax.numpy as jnp
from jax import lax
from jax.experimental import pallas as pl
from jax.experimental.pallas import tpu as pltpu
from jax.sharding import PartitionSpec as P


def gelu_tanh(inputs):
    return jax.nn.gelu(inputs, approximate=True)


def _agg_kernel(own_count, last_step, per, src_ref, cnt_ref, live_ref, own_ref, *refs):
    pulled_refs = refs[:per]
    tile_ref, out_ref, acc_ref = refs[per:]
    v = pl.program_id(0)
    k = pl.program_id(1)

    @pl.when(k == 0)
    def _():
        acc_ref[...] = jnp.zeros_like(acc_ref)

    for j, pulled_ref in zip(range(per), pulled_refs):
        t = per * k + j
        src = src_ref[v, t]
        tile_live = t < cnt_ref[v]
        own_ok = tile_live & (src < own_count)
        pull_ok = tile_live & (src >= own_count) & (live_ref[jnp.maximum(src - own_count, 0)] > 0)

        @pl.when(own_ok)
        def _():
            acc_ref[...] += jnp.dot(
                own_ref[jnp.clip(src, 0, own_count - 1)], tile_ref[0, j], preferred_element_type=jnp.float32
            )

        @pl.when(pull_ok)
        def _():
            block = pulled_ref[0, :, 0]
            block = block.reshape(block.shape[0] * block.shape[1], block.shape[2])
            acc_ref[...] += jnp.dot(block, tile_ref[0, j], preferred_element_type=jnp.float32)

    @pl.when(k == last_step)
    def _():
        out_ref[0] = acc_ref[...].astype(out_ref.dtype)


def aggregate(own, pulled, tile_src, tile_count, slot_live, tile_values):
    nb, feat, blk = own.shape
    dom, fsdp, cap = pulled.shape[0], pulled.shape[1], pulled.shape[2]
    tiles = tile_src.shape[1]
    per = tiles
    steps = tiles // per

    def eff(v, t, cnt_ref):
        return jnp.minimum(t, cnt_ref[v] - 1)

    def pulled_map(j):
        def index(v, k, src_ref, cnt_ref, live_ref):
            s = jnp.clip(src_ref[v, eff(v, per * k + j, cnt_ref)] - nb, 0, cap * dom - 1)
            return (s % dom, 0, s // dom, 0, 0)

        return index

    grid_spec = pltpu.PrefetchScalarGridSpec(
        num_scalar_prefetch=3,
        grid=(nb, steps),
        in_specs=[pl.BlockSpec((nb, feat, blk), lambda v, k, s, c, l: (0, 0, 0))]
        + [pl.BlockSpec((1, fsdp, 1) + pulled.shape[3:], pulled_map(j)) for j in range(per)]
        + [pl.BlockSpec((1, per, blk, blk), lambda v, k, s, c, l: (v, k, 0, 0))],
        out_specs=pl.BlockSpec((1, feat, blk), lambda v, k, s, c, l: (v, 0, 0)),
        scratch_shapes=[pltpu.VMEM((feat, blk), jnp.float32)],
    )
    flops = 2 * nb * tiles * feat * blk * blk
    return pl.pallas_call(
        functools.partial(_agg_kernel, nb, steps - 1, per),
        grid_spec=grid_spec,
        out_shape=jax.ShapeDtypeStruct(own.shape, jnp.bfloat16),
        compiler_params=pltpu.CompilerParams(dimension_semantics=("arbitrary", "arbitrary")),
        cost_estimate=pl.CostEstimate(
            flops=flops, transcendentals=0, bytes_accessed=nb * tiles * (2 * feat * blk * 2 + blk * blk * 2) + own.size * 2
        ),
    )(tile_src, tile_count, slot_live, own, *([pulled] * per), tile_values)


def _spread_kernel(own_count, tiles, src_ref, cnt_ref, back_ref, tile_ref, out_ref):
    v = pl.program_id(0)

    @pl.when(v == 0)
    def _():
        out_ref[...] = jnp.zeros_like(out_ref)

    for t in range(tiles):
        src = src_ref[v, t]

        @pl.when((t < cnt_ref[v]) & (src < own_count))
        def _():
            term = lax.dot_general(
                back_ref[0], tile_ref[0, t], (((1,), (1,)), ((), ())), preferred_element_type=jnp.float32
            )
            target = jnp.clip(src, 0, own_count - 1)
            out_ref[target] = out_ref[target] + term


def spread_back(back_second, tile_src, tile_count, tile_values):
    nb, width, blk = back_second.shape
    tiles = tile_src.shape[1]

    def eff(v, t, cnt_ref):
        return jnp.minimum(t, cnt_ref[v] - 1)

    grid_spec = pltpu.PrefetchScalarGridSpec(
        num_scalar_prefetch=2,
        grid=(nb,),
        in_specs=[
            pl.BlockSpec((1, width, blk), lambda v, s, c: (v, 0, 0)),
            pl.BlockSpec((1, tiles, blk, blk), lambda v, s, c: (v, 0, 0, 0)),
        ],
        out_specs=pl.BlockSpec((nb, width, blk), lambda v, s, c: (0, 0, 0)),
    )
    return pl.pallas_call(
        functools.partial(_spread_kernel, nb, tiles),
        grid_spec=grid_spec,
        out_shape=jax.ShapeDtypeStruct(back_second.shape, jnp.float32),
        compiler_params=pltpu.CompilerParams(dimension_semantics=("arbitrary",)),
        cost_estimate=pl.CostEstimate(
            flops=2 * nb * tiles * width * blk * blk,
            transcendentals=0,
            bytes_accessed=back_second.size * 2 + nb * tiles * blk * blk * 2 + back_second.size * 4,
        ),
    )(tile_src, tile_count, back_second, tile_values)


def gather_rows(x, axis):
    n = lax.axis_size(axis)
    spread = lax.all_to_all(jnp.broadcast_to(x[None], (n,) + x.shape), axis, split_axis=0, concat_axis=0, tiled=True)
    return spread.reshape((n * x.shape[0],) + x.shape[1:])


def on_device(
    features,
    history_first,
    history_second,
    pull_list,
    pull_count,
    tile_src,
    tile_count,
    tile_values,
    w_first,
    w_second,
    bias_first,
    out_grad,
):
    dom_size = lax.axis_size("dom")
    fsdp_size = lax.axis_size("fsdp")
    me = lax.axis_index("dom") * fsdp_size + lax.axis_index("fsdp")
    rows, hidden = w_first.shape
    bias_cols = jnp.broadcast_to(bias_first[:, None], (rows, 128))
    packed = lax.all_gather(jnp.concatenate([w_first, w_second, bias_cols], axis=1), "fsdp", axis=0, tiled=True)
    first_full = packed[:, :hidden]
    second_full = packed[:, hidden : 2 * hidden]
    bias_full = packed[:, 2 * hidden].astype(jnp.float32)

    chosen = pull_list[0]
    requesters, slot_cap = chosen.shape
    counts_all = lax.all_gather(pull_count, "dom", axis=0, tiled=True)
    counts_all, chosen = lax.optimization_barrier((counts_all, chosen))
    my_counts = lax.dynamic_index_in_dim(counts_all, me, axis=1, keepdims=False)
    slot_live = (lax.broadcasted_iota(jnp.int32, (slot_cap, dom_size), 0) < my_counts[None, :]).astype(jnp.int32)
    slot_live = slot_live.reshape(-1)

    block_len = features.shape[2]
    first_cols = history_first.shape[1]
    second_cols = history_second.shape[1]
    sent_first = jnp.take(history_first, chosen.reshape(-1), axis=0, mode="clip").reshape(requesters, slot_cap, first_cols, block_len)
    sent_second = jnp.take(history_second, chosen.reshape(-1), axis=0, mode="clip").reshape(requesters, slot_cap, second_cols, block_len)
    arrived_first = lax.all_to_all(sent_first, ("dom", "fsdp"), split_axis=0, concat_axis=0, tiled=True)
    arrived_second = lax.all_to_all(sent_second, ("dom", "fsdp"), split_axis=0, concat_axis=0, tiled=True)
    pulled_first = arrived_first.reshape(dom_size, fsdp_size, slot_cap, first_cols, block_len)
    pulled_second = arrived_second.reshape(dom_size, fsdp_size, slot_cap, second_cols, block_len)

    core = lax.axis_index("dom") % 2
    pair = [(d, d ^ 1) for d in range(dom_size)]
    partner_grad = lax.ppermute(out_grad, "dom", pair)

    back_second = jnp.einsum(
        "ab,vbn->van", second_full, out_grad, preferred_element_type=jnp.float32
    ).astype(jnp.bfloat16)
    back_hidden = spread_back(back_second, tile_src, tile_count, tile_values)

    def halves(x):
        split = x.reshape(x.shape[0], fsdp_size, 2, x.shape[1] // (2 * fsdp_size), x.shape[2])
        mine = lax.dynamic_index_in_dim(split, core, axis=2, keepdims=False)
        theirs = lax.dynamic_index_in_dim(split, 1 - core, axis=2, keepdims=False)
        return mine, theirs

    agg_first = aggregate(features, pulled_first, tile_src, tile_count, slot_live, tile_values)
    pre_act = (
        jnp.einsum("fh,vfn->vhn", first_full, agg_first, preferred_element_type=jnp.float32)
        + bias_full[None, :, None]
    )
    hidden_new = gelu_tanh(pre_act).astype(jnp.bfloat16)
    _, pullback = jax.vjp(gelu_tanh, pre_act)
    back_pre = pullback(back_hidden)[0].astype(jnp.bfloat16)
    bias_term = jnp.sum(back_pre.astype(jnp.float32), axis=(0, 2))
    first_mine, first_theirs = halves(agg_first)
    first_got, back_got = lax.ppermute((first_theirs, back_pre), "dom", pair)
    first_term = jnp.einsum(
        "vprn,vhn->prh", first_mine, back_pre, preferred_element_type=jnp.float32
    ) + jnp.einsum("vprn,vhn->prh", first_got, back_got, preferred_element_type=jnp.float32)

    half_rows = first_term.shape[1]
    lanes = 128
    agg_second = aggregate(hidden_new, pulled_second, tile_src, tile_count, slot_live, tile_values)
    second_mine, second_theirs = halves(agg_second)
    second_got = lax.ppermute(second_theirs, "dom", pair)
    second_term = jnp.einsum(
        "vprn,vbn->prb", second_mine, out_grad, preferred_element_type=jnp.float32
    ) + jnp.einsum("vprn,vbn->prb", second_got, partner_grad, preferred_element_type=jnp.float32)

    bias_cols = jnp.zeros((fsdp_size, 2 * half_rows, lanes), jnp.float32)
    bias_cols = bias_cols.at[:, 0, : hidden // fsdp_size].set(bias_term.reshape(fsdp_size, hidden // fsdp_size))
    packed_terms = jnp.concatenate([jnp.concatenate([first_term, second_term], axis=1), bias_cols], axis=2)
    arrived_terms = lax.all_to_all(packed_terms.astype(jnp.bfloat16), "fsdp", split_axis=0, concat_axis=0, tiled=True)
    shard = jnp.sum(arrived_terms.astype(jnp.float32), axis=0)
    for flip in (2, 4):
        shard = shard + lax.ppermute(shard, "dom", [(d, d ^ flip) for d in range(dom_size)])
    other = lax.ppermute(shard, "dom", pair)
    low = jnp.where(core == 0, shard, other)
    high = jnp.where(core == 0, other, shard)
    first_total = jnp.concatenate([low[:half_rows, :hidden], high[:half_rows, :hidden]], axis=0)
    second_total = jnp.concatenate([low[half_rows:, :hidden], high[half_rows:, :hidden]], axis=0)
    bias_total = (shard + other)[0, hidden : hidden + hidden // fsdp_size]
    return (hidden_new, first_total, second_total, bias_total)


def solution(mesh):
    return jax.shard_map(
        on_device,
        mesh=mesh,
        in_specs=(
            P(("dom", "fsdp"), None, None),
            P("dom", "fsdp", None),
            P("dom", "fsdp", None),
            P("dom", None, None),
            P("dom", None),
            P(("dom", "fsdp"), None),
            P(("dom", "fsdp")),
            P(("dom", "fsdp"), None, None, None),
            P("fsdp", None),
            P("fsdp", None),
            P("fsdp"),
            P(("dom", "fsdp"), None, None),
        ),
        out_specs=(P(("dom", "fsdp"), None, None), P("fsdp", None), P("fsdp", None), P("fsdp")),
        check_vma=False,
    )
```
